32 devices in a mesh: ctx: 8 (over z, x), head: 4 (over y, core).
Axes of the slice: x: 2, y: 2, z: 4, core: 2. Of those that a mesh axis runs over, the one named last changes fastest.
Arguments:
- query_raw: bfloat16 [8192, 4096], P('ctx', 'head'), may hold values from -180 to 180
- key_raw: bfloat16 [8192, 2048], P('ctx', 'head'), may hold values from -180 to 180
- value_proj: bfloat16 [8192, 2048], P('ctx', 'head'), may hold values from -6 to 6
- query_gain: float32 [128], replicated, may hold values from 0.1 to 1.9
- key_gain: float32 [128], replicated, may hold values from 0.1 to 1.9
- out_grad: bfloat16 [8192, 4096], P('ctx', 'head'), may hold values from -9 to 9
- doc_lengths: int32 [16], replicated, may hold values from 1 to 2048, 8192 in all
Outputs:
- query_grad: bfloat16 [8192, 4096], P('ctx', 'head')
- key_grad: bfloat16 [8192, 2048], P('ctx', 'head')
- value_grad: bfloat16 [8192, 2048], P('ctx', 'head')
- query_gain_grad: float32 [128], replicated
- key_gain_grad: float32 [128], replicated
The draws below stay inside these ranges and needn't reach their ends.
All inputs are finite; a program needn't handle non-finite values.
Results may differ from the reference program's by a relative error of at most 0.0083.
Values may be sent and summed in bfloat16 or wider, within the bound.
No kernel may reach another device: no remote copies, remote signals or barrier semaphores. Data moves between devices by JAX's collectives and lax.ppermute only.
A program may use at most 192 MiB of HBM per device.

```python
import math
import jax
import jax.numpy as jnp
import numpy as np
from jax import lax

QHEADS = 32
KVHEADS = 16
HEAD_DIM = 128
WINDOW = 1024
QUERY_SCALAR = 168
TOKENS = 8192
DOCS = 16
MOST = 2048


def rough_rows(key, row_count, col_count):
    key_base, key_rows, key_cols = jax.random.split(key, 3)
    row_scale = jnp.exp(jax.random.uniform(key_rows, (row_count, 1), jnp.float32, 0.0, math.log(10.0)))
    col_scale = jnp.exp(jax.random.uniform(key_cols, (1, col_count), jnp.float32, 0.0, math.log(10.0)))
    base_vals = jnp.clip(jax.random.normal(key_base, (row_count, col_count), jnp.float32), -6.0, 6.0)
    return base_vals * row_scale * col_scale * 0.3


def draw_query_raw(key, part):
    return rough_rows(jax.random.fold_in(key, 11), TOKENS, QHEADS * HEAD_DIM).astype(jnp.bfloat16)


def draw_key_raw(key, part):
    return rough_rows(jax.random.fold_in(key, 23), TOKENS, KVHEADS * HEAD_DIM).astype(jnp.bfloat16)


def draw_out_grad(key, part):
    key_base = jax.random.fold_in(jax.random.fold_in(key, 37), 0)
    ramp = (jnp.arange(TOKENS, dtype=jnp.float32) / TOKENS)[:, None]
    col_count = QHEADS * HEAD_DIM
    base_vals = jnp.clip(jax.random.normal(key_base, (TOKENS, col_count), jnp.float32), -6.0, 6.0)
    return (base_vals * (0.5 + ramp)).astype(jnp.bfloat16)


def block_scale(rng, extent, cuts, low, largest):
    def one(axis_at, blocks):
        heights = jax.random.uniform(jax.random.fold_in(jax.random.fold_in(rng, 6), axis_at), (blocks,), jnp.float32, low / len(cuts), largest / len(cuts))
        return jnp.repeat(jnp.exp(heights), extent[axis_at] // blocks).reshape((-1,) + (1,) * (len(extent) - axis_at - 1))

    factor_of = one(*cuts[0])
    for cut in cuts[1:]:
        factor_of = factor_of * one(*cut)
    return factor_of


def profile(number_of, total, limit, lean):
    portions = [(1 << 20) // math.isqrt(standing ** lean) + 1 for standing in range(2, number_of + 1)]
    rest, given = total - limit - (number_of - 1), [1] * (number_of - 1)
    while rest > 0:
        candidates = [i for i in range(number_of - 1) if given[i] < limit]
        pool, budget = sum([portions[i] for i in candidates]), rest
        for i in candidates:
            addition = min(limit - given[i], max(1, budget * portions[i] // pool), rest)
            given[i] = given[i] + addition
            rest = rest - addition
    return np.array([limit] + given)


def uneven_parts(rng, number_of, total, bound, lean):
    if number_of == 2:
        one = jax.random.randint(rng, (), max(1, total - bound), min(bound, total - 1) + 1)
        return jnp.stack([one, total - one])
    tallies = jnp.asarray(profile(number_of, total, bound, lean), jnp.int32)
    twos = (number_of - 1) // 2
    donor, sink = tallies[1:1 + 2 * twos:2], tallies[2:2 + 2 * twos:2]
    room = jnp.minimum(donor - 1, bound - sink)
    passed = jax.random.randint(jax.random.fold_in(rng, 1), (twos,), 0, 1 << 20) % (room + 1)
    tallies = tallies.at[1:1 + 2 * twos:2].set(donor - passed).at[2:2 + 2 * twos:2].set(sink + passed)
    return tallies[jax.random.permutation(jax.random.fold_in(rng, 2), number_of)]


def normal_values(key, dims, scale, most, cuts=(), kind=jnp.bfloat16):
    level = block_scale(key, dims, cuts, -0.22, 0.18) if cuts else 1.0
    values = jax.random.normal(key, dims, jnp.float32) * scale * level
    return jnp.minimum(jnp.maximum(values, -most), most).astype(kind)


def setup_inputs(seed: int = 0) -> dict:
    arg_keys = jax.random.split(jax.random.key(seed), 8)
    query_raw = draw_query_raw(jax.random.fold_in(arg_keys[7], 71), 0)
    key_raw = draw_key_raw(jax.random.fold_in(arg_keys[7], 71), 0)
    value_proj = normal_values(arg_keys[2], (TOKENS, KVHEADS * HEAD_DIM), 1.0, 6.0, ((0, 8), (1, 4)))
    query_gain = jnp.clip(1.0 + 0.18 * jax.random.normal(arg_keys[3], (HEAD_DIM,), jnp.float32), 0.1, 1.9)
    key_gain = jnp.clip(1.0 + 0.18 * jax.random.normal(arg_keys[4], (HEAD_DIM,), jnp.float32), 0.1, 1.9)
    out_grad = draw_out_grad(jax.random.fold_in(arg_keys[7], 71), 0)
    doc_lengths = uneven_parts(arg_keys[6], DOCS, TOKENS, MOST, 1).astype(jnp.int32)
    return dict(query_raw=query_raw, key_raw=key_raw, value_proj=value_proj, query_gain=query_gain, key_gain=key_gain, out_grad=out_grad, doc_lengths=doc_lengths)


EPS = 1e-06
FAR = -2 ** 30

def norm_rows(raw_rows, head_count):
    values = raw_rows.astype(jnp.float32).reshape(raw_rows.shape[0], head_count, -1)
    inverse = lax.rsqrt(lax.optimization_barrier(jnp.mean(values * values, axis=-1, keepdims=True)) + EPS)
    return (values * inverse, inverse)

def norm_back(raw_rows, gain_vec, head_count, upstream):
    scaled, inverse = norm_rows(raw_rows, head_count)
    incoming = upstream.reshape(scaled.shape)
    weighted = incoming * gain_vec
    inner_sum = lax.optimization_barrier(jnp.mean(weighted * scaled, axis=-1, keepdims=True))
    result = inverse * (weighted - scaled * inner_sum)
    return (result.reshape(raw_rows.shape), lax.optimization_barrier(jnp.sum(incoming * scaled, axis=(0, 1))))

def doc_index(positions, doc_ends):
    return lax.optimization_barrier(jnp.sum((positions[:, None] >= doc_ends[None, :]).astype(jnp.int32), axis=1))

def tile_live(query_pos, query_doc, key_pos, key_doc):
    return (key_pos[None, :] <= query_pos[:, None]) & (query_pos[:, None] - key_pos[None, :] < WINDOW) & (query_doc[:, None] == key_doc[None, :])

def round_keep(values):
    return lax.optimization_barrier(values.astype(jnp.bfloat16)).astype(jnp.float32)

def take_rows(array, first, count):
    return lax.dynamic_slice_in_dim(array, first, count, 0)

def reference(query_raw, key_raw, value_proj, query_gain, key_gain, out_grad, doc_lengths):
    block_rows = math.gcd(512, WINDOW)
    key_span = WINDOW + block_rows
    score_scale = QUERY_SCALAR ** (-0.5)
    group_size = QHEADS // KVHEADS
    query_hat, query_inv = norm_rows(query_raw, QHEADS)
    query_norm = (query_hat * query_gain).astype(jnp.bfloat16).reshape(TOKENS, KVHEADS, group_size, HEAD_DIM)
    key_hat, key_inv = norm_rows(key_raw, KVHEADS)
    key_norm = (key_hat * key_gain).astype(jnp.bfloat16)
    keys_all = jnp.concatenate([jnp.zeros((WINDOW, KVHEADS, HEAD_DIM), jnp.bfloat16), key_norm], axis=0)
    vals_all = jnp.concatenate([jnp.zeros((WINDOW, KVHEADS, HEAD_DIM), jnp.bfloat16), value_proj.reshape(TOKENS, KVHEADS, HEAD_DIM)], axis=0)
    positions = jnp.arange(TOKENS, dtype=jnp.int32)
    doc_ends = jnp.cumsum(doc_lengths).astype(jnp.int32)
    own_doc = doc_index(positions, doc_ends)
    key_pos = jnp.concatenate([jnp.full((WINDOW,), FAR, dtype=jnp.int32), positions])
    key_doc = jnp.concatenate([jnp.zeros((WINDOW,), jnp.int32), own_doc])
    grad_rows = out_grad.reshape(TOKENS, KVHEADS, group_size, HEAD_DIM)
    block_count = TOKENS // block_rows

    def tile_inputs(block_num):
        query_first = (block_num * block_rows).astype(jnp.int32)
        query_tile = take_rows(query_norm, query_first, block_rows).astype(jnp.float32)
        grad_tile = take_rows(grad_rows, query_first, block_rows).astype(jnp.float32)
        key_tile = take_rows(keys_all, query_first, key_span).astype(jnp.float32)
        value_tile = take_rows(vals_all, query_first, key_span).astype(jnp.float32)
        live_mask = tile_live(take_rows(positions, query_first, block_rows), take_rows(own_doc, query_first, block_rows), take_rows(key_pos, query_first, key_span), take_rows(key_doc, query_first, key_span))
        scores = jnp.einsum('qhgd,khd->hgqk', query_tile, key_tile) * score_scale
        return (query_first, query_tile, grad_tile, key_tile, value_tile, live_mask, scores)

    def stats_block(block_num):
        query_first, query_tile, grad_tile, key_tile, value_tile, live_mask, scores = tile_inputs(block_num)
        exp_scores = jnp.where(live_mask, jnp.exp(scores), 0.0)
        totals = lax.optimization_barrier(jnp.sum(exp_scores, axis=-1))
        numerator = jnp.einsum('hgqk,khd->qhgd', round_keep(exp_scores), value_tile)
        row_totals = jnp.transpose(totals, (2, 0, 1))
        attn_out = numerator / row_totals[..., None]
        row_delta = lax.optimization_barrier(jnp.sum(grad_tile * attn_out, axis=-1))
        return (jnp.log(row_totals), row_delta)
    block_ids = jnp.arange(block_count, dtype=jnp.int32)
    log_blocks, delta_blocks = lax.map(stats_block, block_ids)

    def grad_block(carried, inputs):
        key_acc, val_acc = carried
        block_num, log_tile, delta_tile = inputs
        query_first, query_tile, grad_tile, key_tile, value_tile, live_mask, scores = tile_inputs(block_num)
        log_here = jnp.transpose(log_tile, (1, 2, 0))
        delta_here = jnp.transpose(delta_tile, (1, 2, 0))
        weights = jnp.where(live_mask, jnp.exp(scores - log_here[..., None]), 0.0)
        d_weights = jnp.einsum('qhgd,khd->hgqk', grad_tile, value_tile)
        d_scores = round_keep(weights * (d_weights - delta_here[..., None]))
        query_part = score_scale * jnp.einsum('hgqk,khd->qhgd', d_scores, key_tile)
        key_part = score_scale * jnp.einsum('hgqk,qhgd->khd', d_scores, query_tile)
        val_part = jnp.einsum('hgqk,qhgd->khd', round_keep(weights), grad_tile)
        key_acc = lax.dynamic_update_slice_in_dim(key_acc, take_rows(key_acc, query_first, key_span) + key_part, query_first, 0)
        val_acc = lax.dynamic_update_slice_in_dim(val_acc, take_rows(val_acc, query_first, key_span) + val_part, query_first, 0)
        return ((key_acc, val_acc), query_part)
    start_acc = (jnp.zeros((WINDOW + TOKENS, KVHEADS, HEAD_DIM), jnp.float32), jnp.zeros((WINDOW + TOKENS, KVHEADS, HEAD_DIM), jnp.float32))
    (key_acc, val_acc), query_blocks = lax.scan(grad_block, start_acc, (block_ids, log_blocks, delta_blocks))
    query_acc = query_blocks.reshape(TOKENS, QHEADS, HEAD_DIM)
    query_grad, query_gain_grad = norm_back(query_raw, query_gain, QHEADS, query_acc)
    key_grad, key_gain_grad = norm_back(key_raw, key_gain, KVHEADS, key_acc[WINDOW:])
    value_grad = val_acc[WINDOW:].reshape(TOKENS, KVHEADS * HEAD_DIM).astype(jnp.bfloat16)
    return (query_grad.astype(jnp.bfloat16), key_grad.astype(jnp.bfloat16), value_grad, query_gain_grad, key_gain_grad)
```

```python
import functools
import math

import jax
import jax.numpy as jnp
from jax import lax
from jax.experimental import pallas as pl
from jax.experimental.pallas import tpu as pltpu
from jax.sharding import PartitionSpec as P

WINDOW = 1024
QUERY_SCALAR = 168


EPS = 1e-06
BLOCK = 256


def shifted(value, axis, steps):
    count = lax.axis_size(axis)
    leading, last = (max(0, -steps), min(count, count - steps))
    return lax.ppermute(value, axis, [(source, source + steps) for source in range(leading, last)])


def norm_rows(raw_rows, head_count):
    values = raw_rows.astype(jnp.float32).reshape(raw_rows.shape[0], head_count, -1)
    inverse = lax.rsqrt(jnp.mean(values * values, axis=-1, keepdims=True) + EPS)
    return (values * inverse, inverse)


def norm_back(raw_rows, gain_vec, head_count, upstream):
    scaled, inverse = norm_rows(raw_rows, head_count)
    incoming = upstream.reshape(scaled.shape)
    weighted = incoming * gain_vec
    inner_sum = jnp.mean(weighted * scaled, axis=-1, keepdims=True)
    result = inverse * (weighted - scaled * inner_sum)
    return (result.reshape(raw_rows.shape), jnp.sum(incoming * scaled, axis=(0, 1)))


def doc_index(positions, doc_ends):
    return jnp.sum((positions[:, None] >= doc_ends[None, :]).astype(jnp.int32), axis=1)


def attn_kernel(qdoc_ref, kdoc_ref, q_ref, do_ref, k_ref, v_ref, dq_ref, dk_ref, dv_ref, *, group, head_dim):
    blk = BLOCK
    n_tiles = WINDOW // blk + 1
    scale = QUERY_SCALAR ** (-0.5)
    qb = pl.program_id(1)

    @pl.when(qb == 0)
    def _():
        dk_ref[...] = jnp.zeros(dk_ref.shape, jnp.float32)
        dv_ref[...] = jnp.zeros(dv_ref.shape, jnp.float32)

    q_first = pl.multiple_of(qb * blk, blk)
    q_all = q_ref[...]
    do_all = do_ref[...]
    q_g = jnp.concatenate([q_all[:, a * head_dim:(a + 1) * head_dim] for a in range(group)], axis=0)
    do_g = jnp.concatenate([do_all[:, a * head_dim:(a + 1) * head_dim] for a in range(group)], axis=0)
    qdoc = qdoc_ref[...]
    rows = lax.broadcasted_iota(jnp.int32, (blk, blk), 0)
    cols = lax.broadcasted_iota(jnp.int32, (blk, blk), 1)

    def tile_mask(t):
        k_first = pl.multiple_of(q_first + t * blk, blk)
        kdoc = kdoc_ref[:, pl.ds(k_first, blk)]
        live = qdoc == kdoc
        if t == 0:
            live = live & (cols > rows)
        if t == n_tiles - 1:
            live = live & (cols + t * blk <= rows + WINDOW)
        return jnp.concatenate([live] * group, axis=0), k_first

    def scores_of(k_tile):
        return lax.dot_general(q_g, k_tile, (((1,), (1,)), ((), ())), preferred_element_type=jnp.float32) * scale

    totals = jnp.zeros((group * blk, 1), jnp.float32)
    numer = jnp.zeros((group * blk, head_dim), jnp.float32)
    for t in range(n_tiles):
        live, k_first = tile_mask(t)
        k_tile = k_ref[pl.ds(k_first, blk), :]
        v_tile = v_ref[pl.ds(k_first, blk), :]
        exp_s = jnp.where(live, jnp.exp(scores_of(k_tile)), 0.0)
        totals = totals + jnp.sum(exp_s, axis=1, keepdims=True)
        numer = numer + jnp.dot(exp_s.astype(jnp.bfloat16), v_tile, preferred_element_type=jnp.float32)
    log_sums = jnp.log(totals)
    attn_out = numer / totals
    delta = jnp.sum(do_g.astype(jnp.float32) * attn_out, axis=1, keepdims=True)

    dq = jnp.zeros((group * blk, head_dim), jnp.float32)
    for t in range(n_tiles):
        live, k_first = tile_mask(t)
        k_tile = k_ref[pl.ds(k_first, blk), :]
        v_tile = v_ref[pl.ds(k_first, blk), :]
        weights = jnp.where(live, jnp.exp(scores_of(k_tile) - log_sums), 0.0)
        d_weights = lax.dot_general(do_g, v_tile, (((1,), (1,)), ((), ())), preferred_element_type=jnp.float32)
        d_scores = (weights * (d_weights - delta)).astype(jnp.bfloat16)
        dq = dq + jnp.dot(d_scores, k_tile, preferred_element_type=jnp.float32)
        dk_part = lax.dot_general(d_scores, q_g, (((0,), (0,)), ((), ())), preferred_element_type=jnp.float32)
        dv_part = lax.dot_general(
            weights.astype(jnp.bfloat16), do_g, (((0,), (0,)), ((), ())), preferred_element_type=jnp.float32
        )
        dk_ref[pl.ds(k_first, blk), :] += dk_part * scale
        dv_ref[pl.ds(k_first, blk), :] += dv_part
    dq = dq * scale
    dq_ref[...] = jnp.concatenate([dq[a * blk:(a + 1) * blk] for a in range(group)], axis=1)


def attention_grads(query_norm, grad_rows, keys_all, vals_all, own_doc, all_doc, key_heads, head_dim):
    tok_rows, q_cols = query_norm.shape
    key_rows = keys_all.shape[0]
    group = q_cols // (key_heads * head_dim)
    blk = BLOCK
    n_q = tok_rows // blk
    n_tiles = WINDOW // blk + 1
    gw = group * head_dim
    kernel = functools.partial(attn_kernel, group=group, head_dim=head_dim)
    flops = 2 * 7 * key_heads * n_q * n_tiles * (group * blk) * blk * head_dim
    cost = pl.CostEstimate(
        flops=flops,
        transcendentals=2 * key_heads * n_q * n_tiles * group * blk * blk,
        bytes_accessed=2 * 2 * tok_rows * q_cols + 2 * 2 * key_rows * key_heads * head_dim
        + 4 * tok_rows * q_cols + 2 * 4 * key_rows * key_heads * head_dim,
    )
    return pl.pallas_call(
        kernel,
        grid=(key_heads, n_q),
        in_specs=[
            pl.BlockSpec((blk, 1), lambda h, qb: (qb, 0)),
            pl.BlockSpec((1, key_rows), lambda h, qb: (0, 0)),
            pl.BlockSpec((blk, gw), lambda h, qb: (qb, h)),
            pl.BlockSpec((blk, gw), lambda h, qb: (qb, h)),
            pl.BlockSpec((key_rows, head_dim), lambda h, qb: (0, h)),
            pl.BlockSpec((key_rows, head_dim), lambda h, qb: (0, h)),
        ],
        out_specs=[
            pl.BlockSpec((blk, gw), lambda h, qb: (qb, h)),
            pl.BlockSpec((key_rows, head_dim), lambda h, qb: (0, h)),
            pl.BlockSpec((key_rows, head_dim), lambda h, qb: (0, h)),
        ],
        out_shape=[
            jax.ShapeDtypeStruct((tok_rows, q_cols), jnp.float32),
            jax.ShapeDtypeStruct((key_rows, key_heads * head_dim), jnp.float32),
            jax.ShapeDtypeStruct((key_rows, key_heads * head_dim), jnp.float32),
        ],
        compiler_params=pltpu.CompilerParams(dimension_semantics=("arbitrary", "arbitrary")),
        cost_estimate=cost,
    )(own_doc.reshape(tok_rows, 1), all_doc.reshape(1, key_rows), query_norm, grad_rows, keys_all, vals_all)


def per_device(query_raw, key_raw, value_proj, query_gain, key_gain, out_grad, doc_lengths):
    tok_rows = query_raw.shape[0]
    head_dim = query_gain.shape[0]
    query_heads = query_raw.shape[1] // head_dim
    key_heads = key_raw.shape[1] // head_dim
    first_pos = lax.axis_index("ctx") * tok_rows
    doc_ends = jnp.cumsum(doc_lengths)
    own_pos = first_pos + jnp.arange(tok_rows, dtype=jnp.int32)
    own_doc = doc_index(own_pos, doc_ends)
    halo_raw = first_pos - WINDOW + jnp.arange(WINDOW, dtype=jnp.int32)
    halo_doc = jnp.where(halo_raw >= 0, doc_index(halo_raw, doc_ends), -1)
    query_hat, query_inv = norm_rows(query_raw, query_heads)
    query_norm = (query_hat * query_gain).astype(jnp.bfloat16).reshape(tok_rows, query_heads * head_dim)
    key_hat, key_inv = norm_rows(key_raw, key_heads)
    key_norm = (key_hat * key_gain).astype(jnp.bfloat16).reshape(tok_rows, key_heads * head_dim)
    halo_keys, halo_vals = shifted((key_norm[tok_rows - WINDOW:], value_proj[tok_rows - WINDOW:]), "ctx", 1)
    keys_all = jnp.concatenate([halo_keys, key_norm], axis=0)
    vals_all = jnp.concatenate([halo_vals, value_proj], axis=0)
    all_doc = jnp.concatenate([halo_doc, own_doc])
    query_acc, key_acc, val_acc = attention_grads(
        query_norm, out_grad, keys_all, vals_all, own_doc, all_doc, key_heads, head_dim
    )
    back_keys, back_vals = shifted((key_acc[:WINDOW], val_acc[:WINDOW]), "ctx", -1)
    key_own = jnp.concatenate(
        [key_acc[WINDOW:tok_rows], key_acc[tok_rows:] + back_keys], axis=0
    ).reshape(tok_rows, key_heads, head_dim)
    val_own = jnp.concatenate([val_acc[WINDOW:tok_rows], val_acc[tok_rows:] + back_vals], axis=0)
    query_grad, query_part = norm_back(
        query_raw, query_gain, query_heads, query_acc.reshape(tok_rows, query_heads, head_dim)
    )
    key_grad, key_part = norm_back(key_raw, key_gain, key_heads, key_own)
    query_gain_grad, key_gain_grad = lax.psum((query_part, key_part), ("ctx", "head"))
    value_grad = val_own.astype(jnp.bfloat16)
    return (
        query_grad.astype(jnp.bfloat16),
        key_grad.astype(jnp.bfloat16),
        value_grad,
        query_gain_grad,
        key_gain_grad,
    )


def solution(mesh):
    return jax.shard_map(
        per_device,
        mesh=mesh,
        in_specs=(
            P("ctx", "head"),
            P("ctx", "head"),
            P("ctx", "head"),
            P(),
            P(),
            P("ctx", "head"),
            P(),
        ),
        out_specs=(P("ctx", "head"), P("ctx", "head"), P("ctx", "head"), P(), P()),
        check_vma=False,
    )
```

```python
import functools
import math

import jax
import jax.numpy as jnp
from jax import lax
from jax.experimental import pallas as pl
from jax.experimental.pallas import tpu as pltpu
from jax.sharding import PartitionSpec as P

WINDOW = 1024
QUERY_SCALAR = 168


EPS = 1e-06
BLOCK = 256


def shifted(value, axis, steps):
    count = lax.axis_size(axis)
    leading, last = (max(0, -steps), min(count, count - steps))
    return lax.ppermute(value, axis, [(source, source + steps) for source in range(leading, last)])


def butterfly_sum(value, axes):
    for axis in axes:
        count = lax.axis_size(axis)
        if count & (count - 1):
            value = lax.psum(value, axis)
            continue
        step = 1
        while step < count:
            pairs = [(source, source ^ step) for source in range(count)]
            value = value + lax.ppermute(value, axis, pairs)
            step *= 2
    return value


def norm_rows(raw_rows, head_count):
    values = raw_rows.astype(jnp.float32).reshape(raw_rows.shape[0], head_count, -1)
    inverse = lax.rsqrt(jnp.mean(values * values, axis=-1, keepdims=True) + EPS)
    return (values * inverse, inverse)


def norm_back(raw_rows, gain_vec, head_count, upstream):
    scaled, inverse = norm_rows(raw_rows, head_count)
    incoming = upstream.reshape(scaled.shape)
    weighted = incoming * gain_vec
    inner_sum = jnp.mean(weighted * scaled, axis=-1, keepdims=True)
    result = inverse * (weighted - scaled * inner_sum)
    return (result.reshape(raw_rows.shape), jnp.sum(incoming * scaled, axis=(0, 1)))


def doc_index(positions, doc_ends):
    return jnp.sum((positions[:, None] >= doc_ends[None, :]).astype(jnp.int32), axis=1)


def attn_kernel(qdoc_ref, kdoc_ref, q_ref, do_ref, k_ref, v_ref, dq_ref, dk_ref, dv_ref, *, group, head_dim):
    blk = BLOCK
    n_tiles = WINDOW // blk + 1
    scale = QUERY_SCALAR ** (-0.5)
    qb = pl.program_id(1)

    @pl.when(qb == 0)
    def _():
        dk_ref[...] = jnp.zeros(dk_ref.shape, jnp.float32)
        dv_ref[...] = jnp.zeros(dv_ref.shape, jnp.float32)

    q_first = pl.multiple_of(qb * blk, blk)
    q_all = q_ref[...]
    do_all = do_ref[...]
    q_g = jnp.concatenate([q_all[:, a * head_dim:(a + 1) * head_dim] for a in range(group)], axis=0)
    do_g = jnp.concatenate([do_all[:, a * head_dim:(a + 1) * head_dim] for a in range(group)], axis=0)
    qdoc = qdoc_ref[...]
    rows = lax.broadcasted_iota(jnp.int32, (blk, blk), 0)
    cols = lax.broadcasted_iota(jnp.int32, (blk, blk), 1)

    def tile_mask(t):
        k_first = pl.multiple_of(q_first + t * blk, blk)
        kdoc = kdoc_ref[:, pl.ds(k_first, blk)]
        live = qdoc == kdoc
        if t == 0:
            live = live & (cols > rows)
        if t == n_tiles - 1:
            live = live & (cols + t * blk <= rows + WINDOW)
        return jnp.concatenate([live] * group, axis=0), k_first

    def scores_of(k_tile):
        return lax.dot_general(q_g, k_tile, (((1,), (1,)), ((), ())), preferred_element_type=jnp.float32) * scale

    totals = jnp.zeros((group * blk, 1), jnp.float32)
    numer = jnp.zeros((group * blk, head_dim), jnp.float32)
    for t in range(n_tiles):
        live, k_first = tile_mask(t)
        k_tile = k_ref[pl.ds(k_first, blk), :]
        v_tile = v_ref[pl.ds(k_first, blk), :]
        exp_s = jnp.where(live, jnp.exp(scores_of(k_tile)), 0.0)
        totals = totals + jnp.sum(exp_s, axis=1, keepdims=True)
        numer = numer + jnp.dot(exp_s.astype(jnp.bfloat16), v_tile, preferred_element_type=jnp.float32)
    log_sums = jnp.log(totals)
    attn_out = numer / totals
    delta = jnp.sum(do_g.astype(jnp.float32) * attn_out, axis=1, keepdims=True)

    dq = jnp.zeros((group * blk, head_dim), jnp.float32)
    for t in range(n_tiles):
        live, k_first = tile_mask(t)
        k_tile = k_ref[pl.ds(k_first, blk), :]
        v_tile = v_ref[pl.ds(k_first, blk), :]
        weights = jnp.where(live, jnp.exp(scores_of(k_tile) - log_sums), 0.0)
        d_weights = lax.dot_general(do_g, v_tile, (((1,), (1,)), ((), ())), preferred_element_type=jnp.float32)
        d_scores = (weights * (d_weights - delta)).astype(jnp.bfloat16)
        dq = dq + jnp.dot(d_scores, k_tile, preferred_element_type=jnp.float32)
        dk_part = lax.dot_general(d_scores, q_g, (((0,), (0,)), ((), ())), preferred_element_type=jnp.float32)
        dv_part = lax.dot_general(
            weights.astype(jnp.bfloat16), do_g, (((0,), (0,)), ((), ())), preferred_element_type=jnp.float32
        )
        dk_ref[pl.ds(k_first, blk), :] += dk_part * scale
        dv_ref[pl.ds(k_first, blk), :] += dv_part
    dq = dq * scale
    dq_ref[...] = jnp.concatenate([dq[a * blk:(a + 1) * blk] for a in range(group)], axis=1)


def attention_grads(query_norm, grad_rows, keys_all, vals_all, own_doc, all_doc, key_heads, head_dim):
    tok_rows, q_cols = query_norm.shape
    key_rows = keys_all.shape[0]
    group = q_cols // (key_heads * head_dim)
    blk = BLOCK
    n_q = tok_rows // blk
    n_tiles = WINDOW // blk + 1
    gw = group * head_dim
    kernel = functools.partial(attn_kernel, group=group, head_dim=head_dim)
    flops = 2 * 7 * key_heads * n_q * n_tiles * (group * blk) * blk * head_dim
    cost = pl.CostEstimate(
        flops=flops,
        transcendentals=2 * key_heads * n_q * n_tiles * group * blk * blk,
        bytes_accessed=2 * 2 * tok_rows * q_cols + 2 * 2 * key_rows * key_heads * head_dim
        + 4 * tok_rows * q_cols + 2 * 4 * key_rows * key_heads * head_dim,
    )
    return pl.pallas_call(
        kernel,
        grid=(key_heads, n_q),
        in_specs=[
            pl.BlockSpec((blk, 1), lambda h, qb: (qb, 0)),
            pl.BlockSpec((1, key_rows), lambda h, qb: (0, 0)),
            pl.BlockSpec((blk, gw), lambda h, qb: (qb, h)),
            pl.BlockSpec((blk, gw), lambda h, qb: (qb, h)),
            pl.BlockSpec((key_rows, head_dim), lambda h, qb: (0, h)),
            pl.BlockSpec((key_rows, head_dim), lambda h, qb: (0, h)),
        ],
        out_specs=[
            pl.BlockSpec((blk, gw), lambda h, qb: (qb, h)),
            pl.BlockSpec((key_rows, head_dim), lambda h, qb: (0, h)),
            pl.BlockSpec((key_rows, head_dim), lambda h, qb: (0, h)),
        ],
        out_shape=[
            jax.ShapeDtypeStruct((tok_rows, q_cols), jnp.float32),
            jax.ShapeDtypeStruct((key_rows, key_heads * head_dim), jnp.float32),
            jax.ShapeDtypeStruct((key_rows, key_heads * head_dim), jnp.float32),
        ],
        compiler_params=pltpu.CompilerParams(dimension_semantics=("arbitrary", "arbitrary")),
        cost_estimate=cost,
    )(own_doc.reshape(tok_rows, 1), all_doc.reshape(1, key_rows), query_norm, grad_rows, keys_all, vals_all)


def per_device(query_raw, key_raw, value_proj, query_gain, key_gain, out_grad, doc_lengths):
    tok_rows = query_raw.shape[0]
    head_dim = query_gain.shape[0]
    query_heads = query_raw.shape[1] // head_dim
    key_heads = key_raw.shape[1] // head_dim
    first_pos = lax.axis_index("ctx") * tok_rows
    doc_ends = jnp.cumsum(doc_lengths)
    own_pos = first_pos + jnp.arange(tok_rows, dtype=jnp.int32)
    own_doc = doc_index(own_pos, doc_ends)
    halo_raw = first_pos - WINDOW + jnp.arange(WINDOW, dtype=jnp.int32)
    halo_doc = jnp.where(halo_raw >= 0, doc_index(halo_raw, doc_ends), -1)
    query_hat, query_inv = norm_rows(query_raw, query_heads)
    query_norm = (query_hat * query_gain).astype(jnp.bfloat16).reshape(tok_rows, query_heads * head_dim)
    key_hat, key_inv = norm_rows(key_raw, key_heads)
    key_norm = (key_hat * key_gain).astype(jnp.bfloat16).reshape(tok_rows, key_heads * head_dim)
    halo_keys, halo_vals = shifted((key_norm[tok_rows - WINDOW:], value_proj[tok_rows - WINDOW:]), "ctx", 1)
    keys_all = jnp.concatenate([halo_keys, key_norm], axis=0)
    vals_all = jnp.concatenate([halo_vals, value_proj], axis=0)
    all_doc = jnp.concatenate([halo_doc, own_doc])
    query_acc, key_acc, val_acc = attention_grads(
        query_norm, out_grad, keys_all, vals_all, own_doc, all_doc, key_heads, head_dim
    )
    back_keys, back_vals = shifted((key_acc[:WINDOW], val_acc[:WINDOW]), "ctx", -1)
    key_own = jnp.concatenate(
        [key_acc[WINDOW:tok_rows], key_acc[tok_rows:] + back_keys], axis=0
    ).reshape(tok_rows, key_heads, head_dim)
    val_own = jnp.concatenate([val_acc[WINDOW:tok_rows], val_acc[tok_rows:] + back_vals], axis=0)
    query_grad, query_part = norm_back(
        query_raw, query_gain, query_heads, query_acc.reshape(tok_rows, query_heads, head_dim)
    )
    key_grad, key_part = norm_back(key_raw, key_gain, key_heads, key_own)
    query_gain_grad = butterfly_sum(query_part, ("ctx", "head"))
    key_gain_grad = butterfly_sum(key_part, ("ctx", "head"))
    value_grad = val_own.astype(jnp.bfloat16)
    return (
        query_grad.astype(jnp.bfloat16),
        key_grad.astype(jnp.bfloat16),
        value_grad,
        query_gain_grad,
        key_gain_grad,
    )


def solution(mesh):
    return jax.shard_map(
        per_device,
        mesh=mesh,
        in_specs=(
            P("ctx", "head"),
            P("ctx", "head"),
            P("ctx", "head"),
            P(),
            P(),
            P("ctx", "head"),
            P(),
        ),
        out_specs=(P("ctx", "head"), P("ctx", "head"), P("ctx", "head"), P(), P()),
        check_vma=False,
    )
```

```python
import functools
import math

import jax
import jax.numpy as jnp
from jax import lax
from jax.experimental import pallas as pl
from jax.experimental.pallas import tpu as pltpu
from jax.sharding import PartitionSpec as P

WINDOW = 1024
QUERY_SCALAR = 168


EPS = 1e-06
BLOCK = 256


def shifted(value, axis, steps):
    count = lax.axis_size(axis)
    leading, last = (max(0, -steps), min(count, count - steps))
    return lax.ppermute(value, axis, [(source, source + steps) for source in range(leading, last)])


def butterfly_sum(value, axes):
    for axis in axes:
        count = lax.axis_size(axis)
        if count & (count - 1):
            value = lax.psum(value, axis)
            continue
        step = 1
        while step < count:
            pairs = [(source, source ^ step) for source in range(count)]
            value = value + lax.ppermute(value, axis, pairs)
            step *= 2
    return value


def norm_rows(raw_rows, head_count):
    values = raw_rows.astype(jnp.float32).reshape(raw_rows.shape[0], head_count, -1)
    inverse = lax.rsqrt(jnp.mean(values * values, axis=-1, keepdims=True) + EPS)
    return (values * inverse, inverse)


def norm_back(raw_rows, gain_vec, head_count, upstream):
    scaled, inverse = norm_rows(raw_rows, head_count)
    incoming = upstream.reshape(scaled.shape)
    weighted = incoming * gain_vec
    inner_sum = jnp.mean(weighted * scaled, axis=-1, keepdims=True)
    result = inverse * (weighted - scaled * inner_sum)
    return (result.reshape(raw_rows.shape), jnp.sum(incoming * scaled, axis=(0, 1)))


def doc_index(positions, doc_ends):
    return jnp.sum((positions[:, None] >= doc_ends[None, :]).astype(jnp.int32), axis=1)


def tile_mask(qdoc_ref, kdoc_ref, q_first, t, group):
    blk = BLOCK
    n_tiles = WINDOW // blk + 1
    rows = lax.broadcasted_iota(jnp.int32, (blk, blk), 0)
    cols = lax.broadcasted_iota(jnp.int32, (blk, blk), 1)
    k_first = pl.multiple_of(q_first + t * blk, blk)
    live = qdoc_ref[...] == kdoc_ref[:, pl.ds(k_first, blk)]
    if t == 0:
        live = live & (cols > rows)
    if t == n_tiles - 1:
        live = live & (cols + t * blk <= rows + WINDOW)
    return jnp.concatenate([live] * group, axis=0), k_first


def stacked(ref, group, head_dim):
    block = ref[...]
    return jnp.concatenate([block[:, a * head_dim:(a + 1) * head_dim] for a in range(group)], axis=0)


def grad_tile(q_g, do_g, k_tile, v_tile, live, log_sums, delta):
    scale = QUERY_SCALAR ** (-0.5)
    scores = lax.dot_general(q_g, k_tile, (((1,), (1,)), ((), ())), preferred_element_type=jnp.float32) * scale
    weights = jnp.where(live, jnp.exp(scores - log_sums), 0.0)
    d_weights = lax.dot_general(do_g, v_tile, (((1,), (1,)), ((), ())), preferred_element_type=jnp.float32)
    d_scores = (weights * (d_weights - delta)).astype(jnp.bfloat16)
    dq_part = jnp.dot(d_scores, k_tile, preferred_element_type=jnp.float32)
    dk_part = lax.dot_general(d_scores, q_g, (((0,), (0,)), ((), ())), preferred_element_type=jnp.float32)
    dv_part = lax.dot_general(
        weights.astype(jnp.bfloat16), do_g, (((0,), (0,)), ((), ())), preferred_element_type=jnp.float32
    )
    return dq_part, dk_part * scale, dv_part


def halo_kernel(qdoc_ref, kdoc_ref, q_ref, do_ref, k_ref, v_ref,
                dq_ref, dkv_ref, lse_ref, delta_ref, dq_scr, dk_ref, dv_ref, *, group, head_dim):
    blk = BLOCK
    n_tiles = WINDOW // blk + 1
    n_halo = WINDOW // blk
    scale = QUERY_SCALAR ** (-0.5)
    qb = pl.program_id(1)

    @pl.when(qb == 0)
    def _():
        dk_ref[...] = jnp.zeros(dk_ref.shape, jnp.float32)
        dv_ref[...] = jnp.zeros(dv_ref.shape, jnp.float32)

    q_first = pl.multiple_of(qb * blk, blk)
    q_g = stacked(q_ref, group, head_dim)
    do_g = stacked(do_ref, group, head_dim)
    totals = jnp.zeros((group * blk, 1), jnp.float32)
    numer = jnp.zeros((group * blk, head_dim), jnp.float32)
    for t in range(n_tiles):
        live, k_first = tile_mask(qdoc_ref, kdoc_ref, q_first, t, group)
        k_tile = k_ref[pl.ds(k_first, blk), :]
        v_tile = v_ref[pl.ds(k_first, blk), :]
        scores = lax.dot_general(q_g, k_tile, (((1,), (1,)), ((), ())), preferred_element_type=jnp.float32) * scale
        exp_s = jnp.where(live, jnp.exp(scores), 0.0)
        totals = totals + jnp.sum(exp_s, axis=1, keepdims=True)
        numer = numer + jnp.dot(exp_s.astype(jnp.bfloat16), v_tile, preferred_element_type=jnp.float32)
    log_sums = jnp.log(totals)
    attn_out = numer / totals
    delta = jnp.sum(do_g.astype(jnp.float32) * attn_out, axis=1, keepdims=True)
    lse_ref[...] = log_sums
    delta_ref[...] = delta

    dq_scr[...] = jnp.zeros(dq_scr.shape, jnp.float32)
    for t in range(n_halo):
        @pl.when(qb + t < n_halo)
        def _():
            live, k_first = tile_mask(qdoc_ref, kdoc_ref, q_first, t, group)
            k_tile = k_ref[pl.ds(k_first, blk), :]
            v_tile = v_ref[pl.ds(k_first, blk), :]
            dq_part, dk_part, dv_part = grad_tile(q_g, do_g, k_tile, v_tile, live, log_sums, delta)
            dq_scr[...] += dq_part
            dk_ref[pl.ds(k_first, blk), :] += dk_part
            dv_ref[pl.ds(k_first, blk), :] += dv_part
    dq = dq_scr[...]
    dq_ref[...] = jnp.concatenate([dq[a * blk:(a + 1) * blk] for a in range(group)], axis=1) * scale

    @pl.when(qb == pl.num_programs(1) - 1)
    def _():
        dkv_ref[:, :head_dim] = dk_ref[...].astype(jnp.bfloat16)
        dkv_ref[:, head_dim:] = dv_ref[...].astype(jnp.bfloat16)


def own_kernel(qdoc_ref, kdoc_ref, q_ref, do_ref, k_ref, v_ref, lse_ref, delta_ref, dq_in_ref,
               dq_ref, dk_ref, dv_ref, dq_scr, *, group, head_dim):
    blk = BLOCK
    n_tiles = WINDOW // blk + 1
    n_halo = WINDOW // blk
    scale = QUERY_SCALAR ** (-0.5)
    qb = pl.program_id(1)

    @pl.when(qb == 0)
    def _():
        dk_ref[...] = jnp.zeros(dk_ref.shape, jnp.float32)
        dv_ref[...] = jnp.zeros(dv_ref.shape, jnp.float32)

    q_first = pl.multiple_of(qb * blk, blk)
    q_g = stacked(q_ref, group, head_dim)
    do_g = stacked(do_ref, group, head_dim)
    log_sums = lse_ref[...]
    delta = delta_ref[...]
    dq_scr[...] = jnp.zeros(dq_scr.shape, jnp.float32)
    for t in range(n_tiles):
        @pl.when(qb + t >= n_halo)
        def _():
            live, k_first = tile_mask(qdoc_ref, kdoc_ref, q_first, t, group)
            k_tile = k_ref[pl.ds(k_first, blk), :]
            v_tile = v_ref[pl.ds(k_first, blk), :]
            dq_part, dk_part, dv_part = grad_tile(q_g, do_g, k_tile, v_tile, live, log_sums, delta)
            dq_scr[...] += dq_part
            own_first = pl.multiple_of(k_first - WINDOW, blk)
            dk_ref[pl.ds(own_first, blk), :] += dk_part
            dv_ref[pl.ds(own_first, blk), :] += dv_part
    dq = dq_scr[...]
    dq_ref[...] = dq_in_ref[...] + jnp.concatenate([dq[a * blk:(a + 1) * blk] for a in range(group)], axis=1) * scale


def attention_grads(query_norm, grad_rows, keys_all, vals_all, own_doc, all_doc, key_heads, head_dim):
    tok_rows, q_cols = query_norm.shape
    key_rows = keys_all.shape[0]
    group = q_cols // (key_heads * head_dim)
    blk = BLOCK
    n_q = tok_rows // blk
    n_tiles = WINDOW // blk + 1
    gw = group * head_dim
    kv_cols = key_heads * head_dim
    stat_rows = key_heads * n_q * group * blk
    tile_flops = 2 * (group * blk) * blk * head_dim
    halo_tiles = sum(max(0, WINDOW // blk - qb) for qb in range(n_q))
    own_tiles = n_q * n_tiles - halo_tiles
    common_specs = [
        pl.BlockSpec((blk, 1), lambda h, qb: (qb, 0)),
        pl.BlockSpec((1, key_rows), lambda h, qb: (0, 0)),
        pl.BlockSpec((blk, gw), lambda h, qb: (qb, h)),
        pl.BlockSpec((blk, gw), lambda h, qb: (qb, h)),
        pl.BlockSpec((key_rows, head_dim), lambda h, qb: (0, h)),
        pl.BlockSpec((key_rows, head_dim), lambda h, qb: (0, h)),
    ]
    stat_spec = pl.BlockSpec((group * blk, 1), lambda h, qb: (h * n_q + qb, 0))
    dq_spec = pl.BlockSpec((blk, gw), lambda h, qb: (qb, h))
    params = pltpu.CompilerParams(dimension_semantics=("arbitrary", "arbitrary"))
    in_bytes = 2 * 2 * tok_rows * q_cols + 2 * 2 * key_rows * kv_cols
    operands = (own_doc.reshape(tok_rows, 1), all_doc.reshape(1, key_rows), query_norm, grad_rows, keys_all, vals_all)
    dq_half, dkv_halo, log_sums, delta = pl.pallas_call(
        functools.partial(halo_kernel, group=group, head_dim=head_dim),
        grid=(key_heads, n_q),
        in_specs=common_specs,
        out_specs=[
            dq_spec,
            pl.BlockSpec((WINDOW, 2 * head_dim), lambda h, qb: (0, h)),
            stat_spec,
            stat_spec,
        ],
        out_shape=[
            jax.ShapeDtypeStruct((tok_rows, q_cols), jnp.float32),
            jax.ShapeDtypeStruct((WINDOW, 2 * kv_cols), jnp.bfloat16),
            jax.ShapeDtypeStruct((stat_rows, 1), jnp.float32),
            jax.ShapeDtypeStruct((stat_rows, 1), jnp.float32),
        ],
        scratch_shapes=[
            pltpu.VMEM((group * blk, head_dim), jnp.float32),
            pltpu.VMEM((WINDOW, head_dim), jnp.float32),
            pltpu.VMEM((WINDOW, head_dim), jnp.float32),
        ],
        compiler_params=params,
        cost_estimate=pl.CostEstimate(
            flops=key_heads * (2 * n_q * n_tiles + 5 * halo_tiles) * tile_flops,
            transcendentals=key_heads * (n_q * n_tiles + halo_tiles) * group * blk * blk,
            bytes_accessed=in_bytes + 4 * tok_rows * q_cols + 2 * 2 * WINDOW * kv_cols,
        ),
    )(*operands)
    dq, dk_own, dv_own = pl.pallas_call(
        functools.partial(own_kernel, group=group, head_dim=head_dim),
        grid=(key_heads, n_q),
        in_specs=common_specs + [stat_spec, stat_spec, dq_spec],
        out_specs=[
            dq_spec,
            pl.BlockSpec((tok_rows, head_dim), lambda h, qb: (0, h)),
            pl.BlockSpec((tok_rows, head_dim), lambda h, qb: (0, h)),
        ],
        out_shape=[
            jax.ShapeDtypeStruct((tok_rows, q_cols), jnp.float32),
            jax.ShapeDtypeStruct((tok_rows, kv_cols), jnp.float32),
            jax.ShapeDtypeStruct((tok_rows, kv_cols), jnp.float32),
        ],
        scratch_shapes=[pltpu.VMEM((group * blk, head_dim), jnp.float32)],
        input_output_aliases={8: 0},
        compiler_params=params,
        cost_estimate=pl.CostEstimate(
            flops=key_heads * own_tiles * 5 * tile_flops,
            transcendentals=key_heads * own_tiles * group * blk * blk,
            bytes_accessed=in_bytes + 2 * 4 * tok_rows * q_cols + 2 * 4 * tok_rows * kv_cols,
        ),
    )(*operands, log_sums, delta, dq_half)
    return dq, dkv_halo, dk_own, dv_own


def per_device(query_raw, key_raw, value_proj, query_gain, key_gain, out_grad, doc_lengths):
    tok_rows = query_raw.shape[0]
    head_dim = query_gain.shape[0]
    query_heads = query_raw.shape[1] // head_dim
    key_heads = key_raw.shape[1] // head_dim
    first_pos = lax.axis_index("ctx") * tok_rows
    doc_ends = jnp.cumsum(doc_lengths)
    own_pos = first_pos + jnp.arange(tok_rows, dtype=jnp.int32)
    own_doc = doc_index(own_pos, doc_ends)
    halo_raw = first_pos - WINDOW + jnp.arange(WINDOW, dtype=jnp.int32)
    halo_doc = jnp.where(halo_raw >= 0, doc_index(halo_raw, doc_ends), -1)
    query_hat, query_inv = norm_rows(query_raw, query_heads)
    query_norm = (query_hat * query_gain).astype(jnp.bfloat16).reshape(tok_rows, query_heads * head_dim)
    key_hat, key_inv = norm_rows(key_raw, key_heads)
    key_norm = (key_hat * key_gain).astype(jnp.bfloat16).reshape(tok_rows, key_heads * head_dim)
    halo_keys, halo_vals = shifted((key_norm[tok_rows - WINDOW:], value_proj[tok_rows - WINDOW:]), "ctx", 1)
    keys_all = jnp.concatenate([halo_keys, key_norm], axis=0)
    vals_all = jnp.concatenate([halo_vals, value_proj], axis=0)
    all_doc = jnp.concatenate([halo_doc, own_doc])
    query_acc, dkv_halo, dk_own, dv_own = attention_grads(
        query_norm, out_grad, keys_all, vals_all, own_doc, all_doc, key_heads, head_dim
    )
    back = shifted(dkv_halo, "ctx", -1).reshape(WINDOW, key_heads, 2, head_dim)
    back_keys = back[:, :, 0].reshape(WINDOW, key_heads * head_dim)
    back_vals = back[:, :, 1].reshape(WINDOW, key_heads * head_dim)
    key_own = jnp.concatenate(
        [dk_own[: tok_rows - WINDOW], dk_own[tok_rows - WINDOW:] + back_keys.astype(jnp.float32)], axis=0
    ).reshape(tok_rows, key_heads, head_dim)
    val_own = jnp.concatenate(
        [dv_own[: tok_rows - WINDOW], dv_own[tok_rows - WINDOW:] + back_vals.astype(jnp.float32)], axis=0
    )
    query_grad, query_part = norm_back(
        query_raw, query_gain, query_heads, query_acc.reshape(tok_rows, query_heads, head_dim)
    )
    key_grad, key_part = norm_back(key_raw, key_gain, key_heads, key_own)
    gain_grads = butterfly_sum(jnp.stack([query_part, key_part]), ("head", "ctx"))
    query_gain_grad, key_gain_grad = gain_grads[0], gain_grads[1]
    value_grad = val_own.astype(jnp.bfloat16)
    return (
        query_grad.astype(jnp.bfloat16),
        key_grad.astype(jnp.bfloat16),
        value_grad,
        query_gain_grad,
        key_gain_grad,
    )


def solution(mesh):
    return jax.shard_map(
        per_device,
        mesh=mesh,
        in_specs=(
            P("ctx", "head"),
            P("ctx", "head"),
            P("ctx", "head"),
            P(),
            P(),
            P("ctx", "head"),
            P(),
        ),
        out_specs=(P("ctx", "head"), P("ctx", "head"), P("ctx", "head"), P(), P()),
        check_vma=False,
    )
```

```python
import functools
import math

import jax
import jax.numpy as jnp
from jax import lax
from jax.experimental import pallas as pl
from jax.experimental.pallas import tpu as pltpu
from jax.sharding import PartitionSpec as P

WINDOW = 1024
QUERY_SCALAR = 168


EPS = 1e-06
BLOCK = 256


def shifted(value, axis, steps):
    count = lax.axis_size(axis)
    leading, last = (max(0, -steps), min(count, count - steps))
    return lax.ppermute(value, axis, [(source, source + steps) for source in range(leading, last)])


def butterfly_sum(value, axes):
    for axis in axes:
        count = lax.axis_size(axis)
        if count & (count - 1):
            value = lax.psum(value, axis)
            continue
        step = 1
        while step < count:
            pairs = [(source, source ^ step) for source in range(count)]
            value = value + lax.ppermute(value, axis, pairs)
            step *= 2
    return value


def norm_rows(raw_rows, head_count):
    values = raw_rows.astype(jnp.float32).reshape(raw_rows.shape[0], head_count, -1)
    inverse = lax.rsqrt(jnp.mean(values * values, axis=-1, keepdims=True) + EPS)
    return (values * inverse, inverse)


def norm_back(raw_rows, gain_vec, head_count, upstream):
    scaled, inverse = norm_rows(raw_rows, head_count)
    incoming = upstream.reshape(scaled.shape)
    weighted = incoming * gain_vec
    inner_sum = jnp.mean(weighted * scaled, axis=-1, keepdims=True)
    result = inverse * (weighted - scaled * inner_sum)
    return (result.reshape(raw_rows.shape), jnp.sum(incoming * scaled, axis=(0, 1)))


def doc_index(positions, doc_ends):
    return jnp.sum((positions[:, None] >= doc_ends[None, :]).astype(jnp.int32), axis=1)


def tile_mask(qdoc_ref, kdoc_ref, q_first, t, group):
    blk = BLOCK
    n_tiles = WINDOW // blk + 1
    rows = lax.broadcasted_iota(jnp.int32, (blk, blk), 0)
    cols = lax.broadcasted_iota(jnp.int32, (blk, blk), 1)
    k_first = pl.multiple_of(q_first + t * blk, blk)
    live = qdoc_ref[...] == kdoc_ref[:, pl.ds(k_first, blk)]
    if t == 0:
        live = live & (cols > rows)
    if t == n_tiles - 1:
        live = live & (cols + t * blk <= rows + WINDOW)
    return jnp.concatenate([live] * group, axis=0), k_first


def stacked(ref, group, head_dim):
    block = ref[...]
    return jnp.concatenate([block[:, a * head_dim:(a + 1) * head_dim] for a in range(group)], axis=0)


def grad_tile(q_g, do_g, k_tile, v_tile, live, log_sums, delta):
    scale = QUERY_SCALAR ** (-0.5)
    scores = lax.dot_general(q_g, k_tile, (((1,), (1,)), ((), ())), preferred_element_type=jnp.float32) * scale
    weights = jnp.where(live, jnp.exp(scores - log_sums), 0.0)
    d_weights = lax.dot_general(do_g, v_tile, (((1,), (1,)), ((), ())), preferred_element_type=jnp.float32)
    d_scores = (weights * (d_weights - delta)).astype(jnp.bfloat16)
    dq_part = jnp.dot(d_scores, k_tile, preferred_element_type=jnp.float32)
    dk_part = lax.dot_general(d_scores, q_g, (((0,), (0,)), ((), ())), preferred_element_type=jnp.float32)
    dv_part = lax.dot_general(
        weights.astype(jnp.bfloat16), do_g, (((0,), (0,)), ((), ())), preferred_element_type=jnp.float32
    )
    return dq_part, dk_part * scale, dv_part


def halo_kernel(qdoc_ref, kdoc_ref, q_ref, do_ref, k_ref, v_ref,
                dq_ref, dkv_ref, lse_ref, delta_ref, dq_scr, dk_ref, dv_ref, *, group, head_dim):
    blk = BLOCK
    n_tiles = WINDOW // blk + 1
    n_halo = WINDOW // blk
    scale = QUERY_SCALAR ** (-0.5)
    qb = pl.program_id(1)

    @pl.when(qb == 0)
    def _():
        dk_ref[...] = jnp.zeros(dk_ref.shape, jnp.float32)
        dv_ref[...] = jnp.zeros(dv_ref.shape, jnp.float32)

    q_first = pl.multiple_of(qb * blk, blk)
    q_g = stacked(q_ref, group, head_dim)
    do_g = stacked(do_ref, group, head_dim)
    totals = jnp.zeros((group * blk, 1), jnp.float32)
    numer = jnp.zeros((group * blk, head_dim), jnp.float32)
    for t in range(n_tiles):
        live, k_first = tile_mask(qdoc_ref, kdoc_ref, q_first, t, group)
        k_tile = k_ref[pl.ds(k_first, blk), :]
        v_tile = v_ref[pl.ds(k_first, blk), :]
        scores = lax.dot_general(q_g, k_tile, (((1,), (1,)), ((), ())), preferred_element_type=jnp.float32) * scale
        exp_s = jnp.where(live, jnp.exp(scores), 0.0)
        totals = totals + jnp.sum(exp_s, axis=1, keepdims=True)
        numer = numer + jnp.dot(exp_s.astype(jnp.bfloat16), v_tile, preferred_element_type=jnp.float32)
    log_sums = jnp.log(totals)
    attn_out = numer / totals
    delta = jnp.sum(do_g.astype(jnp.float32) * attn_out, axis=1, keepdims=True)
    lse_ref[...] = log_sums
    delta_ref[...] = delta

    dq_scr[...] = jnp.zeros(dq_scr.shape, jnp.float32)
    for t in range(n_halo):
        @pl.when(qb + t < n_halo)
        def _():
            live, k_first = tile_mask(qdoc_ref, kdoc_ref, q_first, t, group)
            k_tile = k_ref[pl.ds(k_first, blk), :]
            v_tile = v_ref[pl.ds(k_first, blk), :]
            dq_part, dk_part, dv_part = grad_tile(q_g, do_g, k_tile, v_tile, live, log_sums, delta)
            dq_scr[...] += dq_part
            dk_ref[pl.ds(k_first, blk), :] += dk_part
            dv_ref[pl.ds(k_first, blk), :] += dv_part
    dq = dq_scr[...]
    dq_ref[...] = jnp.concatenate([dq[a * blk:(a + 1) * blk] for a in range(group)], axis=1) * scale

    @pl.when(qb == pl.num_programs(1) - 1)
    def _():
        dkv_ref[:, :head_dim] = dk_ref[...].astype(jnp.bfloat16)
        dkv_ref[:, head_dim:] = dv_ref[...].astype(jnp.bfloat16)


def norm_grad(raw, gain, upstream):
    inverse = lax.rsqrt(jnp.mean(raw * raw, axis=1, keepdims=True) + EPS)
    scaled = raw * inverse
    weighted = upstream * gain
    inner_sum = jnp.mean(weighted * scaled, axis=1, keepdims=True)
    result = inverse * (weighted - scaled * inner_sum)
    return result, jnp.sum(upstream * scaled, axis=0, keepdims=True)


def own_kernel(qdoc_ref, kdoc_ref, q_ref, do_ref, k_ref, v_ref, lse_ref, delta_ref, dq_in_ref, raw_ref, gain_ref,
               qgrad_ref, qgain_ref, dk_ref, dv_ref, dq_scr, *, group, head_dim):
    blk = BLOCK
    n_tiles = WINDOW // blk + 1
    n_halo = WINDOW // blk
    scale = QUERY_SCALAR ** (-0.5)
    qb = pl.program_id(1)

    @pl.when(qb == 0)
    def _():
        dk_ref[...] = jnp.zeros(dk_ref.shape, jnp.float32)
        dv_ref[...] = jnp.zeros(dv_ref.shape, jnp.float32)

    q_first = pl.multiple_of(qb * blk, blk)
    q_g = stacked(q_ref, group, head_dim)
    do_g = stacked(do_ref, group, head_dim)
    log_sums = lse_ref[...]
    delta = delta_ref[...]
    dq_scr[...] = jnp.zeros(dq_scr.shape, jnp.float32)
    for t in range(n_tiles):
        @pl.when(qb + t >= n_halo)
        def _():
            live, k_first = tile_mask(qdoc_ref, kdoc_ref, q_first, t, group)
            k_tile = k_ref[pl.ds(k_first, blk), :]
            v_tile = v_ref[pl.ds(k_first, blk), :]
            dq_part, dk_part, dv_part = grad_tile(q_g, do_g, k_tile, v_tile, live, log_sums, delta)
            dq_scr[...] += dq_part
            own_first = pl.multiple_of(k_first - WINDOW, blk)
            dk_ref[pl.ds(own_first, blk), :] += dk_part
            dv_ref[pl.ds(own_first, blk), :] += dv_part
    dq = dq_scr[...]
    dq_in = dq_in_ref[...]
    raw = raw_ref[...].astype(jnp.float32)
    gain = gain_ref[...]
    gain_sum = jnp.zeros((1, head_dim), jnp.float32)
    for a in range(group):
        cols = slice(a * head_dim, (a + 1) * head_dim)
        upstream = dq_in[:, cols] + dq[a * blk:(a + 1) * blk] * scale
        result, part = norm_grad(raw[:, cols], gain, upstream)
        qgrad_ref[:, cols] = result.astype(qgrad_ref.dtype)
        gain_sum = gain_sum + part
    qgain_ref[...] = gain_sum.reshape(qgain_ref.shape)


def kv_final_kernel(dk_ref, dv_ref, back_ref, raw_ref, gain_ref, kgrad_ref, vgrad_ref, kgain_ref, *, head_dim):
    tok_rows = dk_ref.shape[0]
    lead = tok_rows - WINDOW
    back = back_ref[...].astype(jnp.float32)
    dk = dk_ref[...]
    dv = dv_ref[...]
    if lead:
        dk = jnp.concatenate([dk[:lead], dk[lead:] + back[:, :head_dim]], axis=0)
        dv = jnp.concatenate([dv[:lead], dv[lead:] + back[:, head_dim:]], axis=0)
    else:
        dk = dk + back[:, :head_dim]
        dv = dv + back[:, head_dim:]
    vgrad_ref[...] = dv.astype(vgrad_ref.dtype)
    result, part = norm_grad(raw_ref[...].astype(jnp.float32), gain_ref[...], dk)
    kgrad_ref[...] = result.astype(kgrad_ref.dtype)
    kgain_ref[...] = part.reshape(kgain_ref.shape)


def kv_final(dk_own, dv_own, back, key_raw, key_gain, key_heads, head_dim):
    tok_rows = dk_own.shape[0]
    kv_cols = key_heads * head_dim
    col_spec = pl.BlockSpec((tok_rows, head_dim), lambda h: (0, h))
    return pl.pallas_call(
        functools.partial(kv_final_kernel, head_dim=head_dim),
        grid=(key_heads,),
        in_specs=[
            col_spec,
            col_spec,
            pl.BlockSpec((WINDOW, 2 * head_dim), lambda h: (0, h)),
            col_spec,
            pl.BlockSpec((1, head_dim), lambda h: (0, 0)),
        ],
        out_specs=[col_spec, col_spec, pl.BlockSpec((1, 1, head_dim), lambda h: (h, 0, 0))],
        out_shape=[
            jax.ShapeDtypeStruct((tok_rows, kv_cols), jnp.bfloat16),
            jax.ShapeDtypeStruct((tok_rows, kv_cols), jnp.bfloat16),
            jax.ShapeDtypeStruct((key_heads, 1, head_dim), jnp.float32),
        ],
        compiler_params=pltpu.CompilerParams(dimension_semantics=("arbitrary",)),
    )(dk_own, dv_own, back, key_raw, key_gain.reshape(1, head_dim))


def attention_grads(query_norm, grad_rows, keys_all, vals_all, own_doc, all_doc, key_heads, head_dim,
                    query_raw, query_gain):
    tok_rows, q_cols = query_norm.shape
    key_rows = keys_all.shape[0]
    group = q_cols // (key_heads * head_dim)
    blk = BLOCK
    n_q = tok_rows // blk
    n_tiles = WINDOW // blk + 1
    gw = group * head_dim
    kv_cols = key_heads * head_dim
    stat_rows = key_heads * n_q * group * blk
    tile_flops = 2 * (group * blk) * blk * head_dim
    halo_tiles = sum(max(0, WINDOW // blk - qb) for qb in range(n_q))
    own_tiles = n_q * n_tiles - halo_tiles
    common_specs = [
        pl.BlockSpec((blk, 1), lambda h, qb: (qb, 0)),
        pl.BlockSpec((1, key_rows), lambda h, qb: (0, 0)),
        pl.BlockSpec((blk, gw), lambda h, qb: (qb, h)),
        pl.BlockSpec((blk, gw), lambda h, qb: (qb, h)),
        pl.BlockSpec((key_rows, head_dim), lambda h, qb: (0, h)),
        pl.BlockSpec((key_rows, head_dim), lambda h, qb: (0, h)),
    ]
    stat_spec = pl.BlockSpec((group * blk, 1), lambda h, qb: (h * n_q + qb, 0))
    dq_spec = pl.BlockSpec((blk, gw), lambda h, qb: (qb, h))
    params = pltpu.CompilerParams(dimension_semantics=("arbitrary", "arbitrary"))
    in_bytes = 2 * 2 * tok_rows * q_cols + 2 * 2 * key_rows * kv_cols
    operands = (own_doc.reshape(tok_rows, 1), all_doc.reshape(1, key_rows), query_norm, grad_rows, keys_all, vals_all)
    dq_half, dkv_halo, log_sums, delta = pl.pallas_call(
        functools.partial(halo_kernel, group=group, head_dim=head_dim),
        grid=(key_heads, n_q),
        in_specs=common_specs,
        out_specs=[
            dq_spec,
            pl.BlockSpec((WINDOW, 2 * head_dim), lambda h, qb: (0, h)),
            stat_spec,
            stat_spec,
        ],
        out_shape=[
            jax.ShapeDtypeStruct((tok_rows, q_cols), jnp.float32),
            jax.ShapeDtypeStruct((WINDOW, 2 * kv_cols), jnp.bfloat16),
            jax.ShapeDtypeStruct((stat_rows, 1), jnp.float32),
            jax.ShapeDtypeStruct((stat_rows, 1), jnp.float32),
        ],
        scratch_shapes=[
            pltpu.VMEM((group * blk, head_dim), jnp.float32),
            pltpu.VMEM((WINDOW, head_dim), jnp.float32),
            pltpu.VMEM((WINDOW, head_dim), jnp.float32),
        ],
        compiler_params=params,
        cost_estimate=pl.CostEstimate(
            flops=key_heads * (2 * n_q * n_tiles + 5 * halo_tiles) * tile_flops,
            transcendentals=key_heads * (n_q * n_tiles + halo_tiles) * group * blk * blk,
            bytes_accessed=in_bytes + 4 * tok_rows * q_cols + 2 * 2 * WINDOW * kv_cols,
        ),
    )(*operands)
    raw_spec = pl.BlockSpec((blk, gw), lambda h, qb: (qb, h))
    gain_spec = pl.BlockSpec((1, head_dim), lambda h, qb: (0, 0))
    query_grad, qgain_parts, dk_own, dv_own = pl.pallas_call(
        functools.partial(own_kernel, group=group, head_dim=head_dim),
        grid=(key_heads, n_q),
        in_specs=common_specs + [stat_spec, stat_spec, dq_spec, raw_spec, gain_spec],
        out_specs=[
            raw_spec,
            pl.BlockSpec((1, 1, head_dim), lambda h, qb: (h * n_q + qb, 0, 0)),
            pl.BlockSpec((tok_rows, head_dim), lambda h, qb: (0, h)),
            pl.BlockSpec((tok_rows, head_dim), lambda h, qb: (0, h)),
        ],
        out_shape=[
            jax.ShapeDtypeStruct((tok_rows, q_cols), jnp.bfloat16),
            jax.ShapeDtypeStruct((key_heads * n_q, 1, head_dim), jnp.float32),
            jax.ShapeDtypeStruct((tok_rows, kv_cols), jnp.float32),
            jax.ShapeDtypeStruct((tok_rows, kv_cols), jnp.float32),
        ],
        scratch_shapes=[pltpu.VMEM((group * blk, head_dim), jnp.float32)],
        compiler_params=params,
        cost_estimate=pl.CostEstimate(
            flops=key_heads * own_tiles * 5 * tile_flops,
            transcendentals=key_heads * own_tiles * group * blk * blk,
            bytes_accessed=in_bytes + 2 * 4 * tok_rows * q_cols + 2 * 4 * tok_rows * kv_cols,
        ),
    )(*operands, log_sums, delta, dq_half, query_raw, query_gain.reshape(1, head_dim))
    return query_grad, jnp.sum(qgain_parts, axis=(0, 1)), dkv_halo, dk_own, dv_own


def per_device(query_raw, key_raw, value_proj, query_gain, key_gain, out_grad, doc_lengths):
    tok_rows = query_raw.shape[0]
    head_dim = query_gain.shape[0]
    query_heads = query_raw.shape[1] // head_dim
    key_heads = key_raw.shape[1] // head_dim
    first_pos = lax.axis_index("ctx") * tok_rows
    doc_ends = jnp.cumsum(doc_lengths)
    own_pos = first_pos + jnp.arange(tok_rows, dtype=jnp.int32)
    own_doc = doc_index(own_pos, doc_ends)
    halo_raw = first_pos - WINDOW + jnp.arange(WINDOW, dtype=jnp.int32)
    halo_doc = jnp.where(halo_raw >= 0, doc_index(halo_raw, doc_ends), -1)
    query_hat, query_inv = norm_rows(query_raw, query_heads)
    query_norm = (query_hat * query_gain).astype(jnp.bfloat16).reshape(tok_rows, query_heads * head_dim)
    key_hat, key_inv = norm_rows(key_raw, key_heads)
    key_norm = (key_hat * key_gain).astype(jnp.bfloat16).reshape(tok_rows, key_heads * head_dim)
    halo_keys, halo_vals = shifted((key_norm[tok_rows - WINDOW:], value_proj[tok_rows - WINDOW:]), "ctx", 1)
    keys_all = jnp.concatenate([halo_keys, key_norm], axis=0)
    vals_all = jnp.concatenate([halo_vals, value_proj], axis=0)
    all_doc = jnp.concatenate([halo_doc, own_doc])
    query_grad, query_part, dkv_halo, dk_own, dv_own = attention_grads(
        query_norm, out_grad, keys_all, vals_all, own_doc, all_doc, key_heads, head_dim, query_raw, query_gain
    )
    back = shifted(dkv_halo, "ctx", -1)
    key_grad, value_grad, key_parts = kv_final(dk_own, dv_own, back, key_raw, key_gain, key_heads, head_dim)
    key_part = jnp.sum(key_parts, axis=(0, 1))
    gain_grads = butterfly_sum(jnp.stack([query_part, key_part]), ("head", "ctx"))
    return (query_grad, key_grad, value_grad, gain_grads[0], gain_grads[1])


def solution(mesh):
    return jax.shard_map(
        per_device,
        mesh=mesh,
        in_specs=(
            P("ctx", "head"),
            P("ctx", "head"),
            P("ctx", "head"),
            P(),
            P(),
            P("ctx", "head"),
            P(),
        ),
        out_specs=(P("ctx", "head"), P("ctx", "head"), P("ctx", "head"), P(), P()),
        check_vma=False,
    )
```

```python
import functools
import math

import jax
import jax.numpy as jnp
from jax import lax
from jax.experimental import pallas as pl
from jax.experimental.pallas import tpu as pltpu
from jax.sharding import PartitionSpec as P

WINDOW = 1024
QUERY_SCALAR = 168


EPS = 1e-06
BLOCK = 256


def shifted(value, axis, steps):
    count = lax.axis_size(axis)
    leading, last = (max(0, -steps), min(count, count - steps))
    return lax.ppermute(value, axis, [(source, source + steps) for source in range(leading, last)])


def xor_tree(values):
    while len(values) > 1:
        values = [values[i] + values[i + 1] for i in range(0, len(values), 2)]
    return values[0]


def butterfly_sum(value, axes):
    for axis in axes:
        count = lax.axis_size(axis)
        if count & (count - 1):
            value = lax.psum(value, axis)
            continue
        bits = count.bit_length() - 1
        low = 0
        while low < bits:
            width = min(3, bits - low)
            shifted_parts = [value]
            for mask in range(1, 1 << width):
                pairs = [(source, source ^ (mask << low)) for source in range(count)]
                shifted_parts.append(lax.ppermute(value, axis, pairs))
            value = xor_tree(shifted_parts)
            low += width
    return value


def norm_rows(raw_rows, head_count):
    values = raw_rows.astype(jnp.float32).reshape(raw_rows.shape[0], head_count, -1)
    inverse = lax.rsqrt(jnp.mean(values * values, axis=-1, keepdims=True) + EPS)
    return (values * inverse, inverse)


def norm_back(raw_rows, gain_vec, head_count, upstream):
    scaled, inverse = norm_rows(raw_rows, head_count)
    incoming = upstream.reshape(scaled.shape)
    weighted = incoming * gain_vec
    inner_sum = jnp.mean(weighted * scaled, axis=-1, keepdims=True)
    result = inverse * (weighted - scaled * inner_sum)
    return (result.reshape(raw_rows.shape), jnp.sum(incoming * scaled, axis=(0, 1)))


def doc_index(positions, doc_ends):
    return jnp.sum((positions[:, None] >= doc_ends[None, :]).astype(jnp.int32), axis=1)


def tile_mask(qdoc_ref, kdoc_ref, q_first, t, group):
    blk = BLOCK
    n_tiles = WINDOW // blk + 1
    rows = lax.broadcasted_iota(jnp.int32, (blk, blk), 0)
    cols = lax.broadcasted_iota(jnp.int32, (blk, blk), 1)
    k_first = q_first + t * blk
    live = qdoc_ref[q_first:q_first + blk, :] == kdoc_ref[:, k_first:k_first + blk]
    if t == 0:
        live = live & (cols > rows)
    if t == n_tiles - 1:
        live = live & (cols + t * blk <= rows + WINDOW)
    return jnp.concatenate([live] * group, axis=0), k_first


def stacked(ref, group, head_dim, first):
    blk = BLOCK
    return jnp.concatenate(
        [ref[first:first + blk, a * head_dim:(a + 1) * head_dim] for a in range(group)], axis=0
    )


def grad_tile(q_g, do_g, k_tile, v_tile, live, log_sums, delta):
    scale = QUERY_SCALAR ** (-0.5)
    scores = lax.dot_general(q_g, k_tile, (((1,), (1,)), ((), ())), preferred_element_type=jnp.float32) * scale
    weights = jnp.where(live, jnp.exp(scores - log_sums), 0.0)
    d_weights = lax.dot_general(do_g, v_tile, (((1,), (1,)), ((), ())), preferred_element_type=jnp.float32)
    d_scores = (weights * (d_weights - delta)).astype(jnp.bfloat16)
    dq_part = jnp.dot(d_scores, k_tile, preferred_element_type=jnp.float32)
    dk_part = lax.dot_general(d_scores, q_g, (((0,), (0,)), ((), ())), preferred_element_type=jnp.float32)
    dv_part = lax.dot_general(
        weights.astype(jnp.bfloat16), do_g, (((0,), (0,)), ((), ())), preferred_element_type=jnp.float32
    )
    return dq_part, dk_part * scale, dv_part


def halo_kernel(qdoc_ref, kdoc_ref, q_ref, do_ref, k_ref, v_ref,
                dq_ref, dkv_ref, lse_ref, delta_ref, dk_ref, dv_ref, *, group, head_dim):
    blk = BLOCK
    n_tiles = WINDOW // blk + 1
    n_halo = WINDOW // blk
    n_q = q_ref.shape[0] // blk
    gb = group * blk
    scale = QUERY_SCALAR ** (-0.5)
    dk_ref[...] = jnp.zeros(dk_ref.shape, jnp.float32)
    dv_ref[...] = jnp.zeros(dv_ref.shape, jnp.float32)
    for qb in range(n_q):
        q_first = qb * blk
        q_g = stacked(q_ref, group, head_dim, q_first)
        do_g = stacked(do_ref, group, head_dim, q_first)
        masks = [tile_mask(qdoc_ref, kdoc_ref, q_first, t, group)[0] for t in range(n_tiles)]
        totals = jnp.zeros((gb, 1), jnp.float32)
        numer = jnp.zeros((gb, head_dim), jnp.float32)
        for t in range(n_tiles):
            k_first = q_first + t * blk
            k_tile = k_ref[k_first:k_first + blk, :]
            v_tile = v_ref[k_first:k_first + blk, :]
            scores = lax.dot_general(
                q_g, k_tile, (((1,), (1,)), ((), ())), preferred_element_type=jnp.float32
            ) * scale
            exp_s = jnp.where(masks[t], jnp.exp(scores), 0.0)
            totals = totals + jnp.sum(exp_s, axis=1, keepdims=True)
            numer = numer + jnp.dot(exp_s.astype(jnp.bfloat16), v_tile, preferred_element_type=jnp.float32)
        log_sums = jnp.log(totals)
        attn_out = numer / totals
        delta = jnp.sum(do_g.astype(jnp.float32) * attn_out, axis=1, keepdims=True)
        lse_ref[qb * gb:(qb + 1) * gb, :] = log_sums
        delta_ref[qb * gb:(qb + 1) * gb, :] = delta
        dq = jnp.zeros((gb, head_dim), jnp.float32)
        for t in range(n_halo - qb):
            k_first = q_first + t * blk
            k_tile = k_ref[k_first:k_first + blk, :]
            v_tile = v_ref[k_first:k_first + blk, :]
            dq_part, dk_part, dv_part = grad_tile(q_g, do_g, k_tile, v_tile, masks[t], log_sums, delta)
            dq = dq + dq_part
            dk_ref[k_first:k_first + blk, :] += dk_part
            dv_ref[k_first:k_first + blk, :] += dv_part
        dq_ref[q_first:q_first + blk, :] = jnp.concatenate(
            [dq[a * blk:(a + 1) * blk] for a in range(group)], axis=1
        ) * scale
    dkv_ref[:, :head_dim] = dk_ref[...].astype(jnp.bfloat16)
    dkv_ref[:, head_dim:] = dv_ref[...].astype(jnp.bfloat16)


def norm_grad(raw, gain, upstream):
    inverse = lax.rsqrt(jnp.mean(raw * raw, axis=1, keepdims=True) + EPS)
    scaled = raw * inverse
    weighted = upstream * gain
    inner_sum = jnp.mean(weighted * scaled, axis=1, keepdims=True)
    result = inverse * (weighted - scaled * inner_sum)
    return result, jnp.sum(upstream * scaled, axis=0, keepdims=True)


def own_kernel(qdoc_ref, kdoc_ref, q_ref, do_ref, k_ref, v_ref, lse_ref, delta_ref, dq_in_ref, raw_ref, gain_ref,
               qgrad_ref, qgain_ref, dk_ref, dv_ref, *, group, head_dim):
    blk = BLOCK
    n_tiles = WINDOW // blk + 1
    n_halo = WINDOW // blk
    n_q = q_ref.shape[0] // blk
    gb = group * blk
    scale = QUERY_SCALAR ** (-0.5)
    dk_ref[...] = jnp.zeros(dk_ref.shape, jnp.float32)
    dv_ref[...] = jnp.zeros(dv_ref.shape, jnp.float32)
    gain = gain_ref[...]
    gain_sum = jnp.zeros((1, head_dim), jnp.float32)
    for qb in range(n_q):
        q_first = qb * blk
        q_g = stacked(q_ref, group, head_dim, q_first)
        do_g = stacked(do_ref, group, head_dim, q_first)
        log_sums = lse_ref[qb * gb:(qb + 1) * gb, :]
        delta = delta_ref[qb * gb:(qb + 1) * gb, :]
        dq = jnp.zeros((gb, head_dim), jnp.float32)
        for t in range(max(0, n_halo - qb), n_tiles):
            live, _ = tile_mask(qdoc_ref, kdoc_ref, q_first, t, group)
            k_first = q_first + t * blk
            k_tile = k_ref[k_first:k_first + blk, :]
            v_tile = v_ref[k_first:k_first + blk, :]
            dq_part, dk_part, dv_part = grad_tile(q_g, do_g, k_tile, v_tile, live, log_sums, delta)
            dq = dq + dq_part
            own_first = k_first - WINDOW
            dk_ref[own_first:own_first + blk, :] += dk_part
            dv_ref[own_first:own_first + blk, :] += dv_part
        dq_in = dq_in_ref[q_first:q_first + blk, :]
        raw = raw_ref[q_first:q_first + blk, :].astype(jnp.float32)
        for a in range(group):
            cols = slice(a * head_dim, (a + 1) * head_dim)
            upstream = dq_in[:, cols] + dq[a * blk:(a + 1) * blk] * scale
            result, part = norm_grad(raw[:, cols], gain, upstream)
            qgrad_ref[q_first:q_first + blk, cols] = result.astype(qgrad_ref.dtype)
            gain_sum = gain_sum + part
    qgain_ref[...] = gain_sum.reshape(qgain_ref.shape)


def kv_final_kernel(dk_ref, dv_ref, back_ref, raw_ref, gain_ref, kgrad_ref, vgrad_ref, kgain_ref, *, head_dim):
    tok_rows = dk_ref.shape[0]
    lead = tok_rows - WINDOW
    back = back_ref[...].astype(jnp.float32)
    dk = dk_ref[...]
    dv = dv_ref[...]
    if lead:
        dk = jnp.concatenate([dk[:lead], dk[lead:] + back[:, :head_dim]], axis=0)
        dv = jnp.concatenate([dv[:lead], dv[lead:] + back[:, head_dim:]], axis=0)
    else:
        dk = dk + back[:, :head_dim]
        dv = dv + back[:, head_dim:]
    vgrad_ref[...] = dv.astype(vgrad_ref.dtype)
    result, part = norm_grad(raw_ref[...].astype(jnp.float32), gain_ref[...], dk)
    kgrad_ref[...] = result.astype(kgrad_ref.dtype)
    kgain_ref[...] = part.reshape(kgain_ref.shape)


def kv_final(dk_own, dv_own, back, key_raw, key_gain, key_heads, head_dim):
    tok_rows = dk_own.shape[0]
    kv_cols = key_heads * head_dim
    col_spec = pl.BlockSpec((tok_rows, head_dim), lambda h: (0, h))
    return pl.pallas_call(
        functools.partial(kv_final_kernel, head_dim=head_dim),
        grid=(key_heads,),
        in_specs=[
            col_spec,
            col_spec,
            pl.BlockSpec((WINDOW, 2 * head_dim), lambda h: (0, h)),
            col_spec,
            pl.BlockSpec((1, head_dim), lambda h: (0, 0)),
        ],
        out_specs=[col_spec, col_spec, pl.BlockSpec((1, 1, head_dim), lambda h: (h, 0, 0))],
        out_shape=[
            jax.ShapeDtypeStruct((tok_rows, kv_cols), jnp.bfloat16),
            jax.ShapeDtypeStruct((tok_rows, kv_cols), jnp.bfloat16),
            jax.ShapeDtypeStruct((key_heads, 1, head_dim), jnp.float32),
        ],
        compiler_params=pltpu.CompilerParams(dimension_semantics=("arbitrary",)),
    )(dk_own, dv_own, back, key_raw, key_gain.reshape(1, head_dim))


def attention_grads(query_norm, grad_rows, keys_all, vals_all, own_doc, all_doc, key_heads, head_dim,
                    query_raw, query_gain):
    tok_rows, q_cols = query_norm.shape
    key_rows = keys_all.shape[0]
    group = q_cols // (key_heads * head_dim)
    blk = BLOCK
    n_q = tok_rows // blk
    n_tiles = WINDOW // blk + 1
    gw = group * head_dim
    kv_cols = key_heads * head_dim
    stat_rows = key_heads * n_q * group * blk
    tile_flops = 2 * (group * blk) * blk * head_dim
    halo_tiles = sum(max(0, WINDOW // blk - qb) for qb in range(n_q))
    own_tiles = n_q * n_tiles - halo_tiles
    common_specs = [
        pl.BlockSpec((tok_rows, 1), lambda h: (0, 0)),
        pl.BlockSpec((1, key_rows), lambda h: (0, 0)),
        pl.BlockSpec((tok_rows, gw), lambda h: (0, h)),
        pl.BlockSpec((tok_rows, gw), lambda h: (0, h)),
        pl.BlockSpec((key_rows, head_dim), lambda h: (0, h)),
        pl.BlockSpec((key_rows, head_dim), lambda h: (0, h)),
    ]
    stat_spec = pl.BlockSpec((n_q * group * blk, 1), lambda h: (h, 0))
    dq_spec = pl.BlockSpec((tok_rows, gw), lambda h: (0, h))
    params = pltpu.CompilerParams(dimension_semantics=("arbitrary",))
    in_bytes = 2 * 2 * tok_rows * q_cols + 2 * 2 * key_rows * kv_cols
    operands = (own_doc.reshape(tok_rows, 1), all_doc.reshape(1, key_rows), query_norm, grad_rows, keys_all, vals_all)
    dq_half, dkv_halo, log_sums, delta = pl.pallas_call(
        functools.partial(halo_kernel, group=group, head_dim=head_dim),
        grid=(key_heads,),
        in_specs=common_specs,
        out_specs=[
            dq_spec,
            pl.BlockSpec((WINDOW, 2 * head_dim), lambda h: (0, h)),
            stat_spec,
            stat_spec,
        ],
        out_shape=[
            jax.ShapeDtypeStruct((tok_rows, q_cols), jnp.float32),
            jax.ShapeDtypeStruct((WINDOW, 2 * kv_cols), jnp.bfloat16),
            jax.ShapeDtypeStruct((stat_rows, 1), jnp.float32),
            jax.ShapeDtypeStruct((stat_rows, 1), jnp.float32),
        ],
        scratch_shapes=[
            pltpu.VMEM((WINDOW, head_dim), jnp.float32),
            pltpu.VMEM((WINDOW, head_dim), jnp.float32),
        ],
        compiler_params=params,
        cost_estimate=pl.CostEstimate(
            flops=key_heads * (2 * n_q * n_tiles + 5 * halo_tiles) * tile_flops,
            transcendentals=key_heads * (n_q * n_tiles + halo_tiles) * group * blk * blk,
            bytes_accessed=in_bytes + 4 * tok_rows * q_cols + 2 * 2 * WINDOW * kv_cols,
        ),
    )(*operands)
    raw_spec = pl.BlockSpec((tok_rows, gw), lambda h: (0, h))
    gain_spec = pl.BlockSpec((1, head_dim), lambda h: (0, 0))
    query_grad, qgain_parts, dk_own, dv_own = pl.pallas_call(
        functools.partial(own_kernel, group=group, head_dim=head_dim),
        grid=(key_heads,),
        in_specs=common_specs + [stat_spec, stat_spec, dq_spec, raw_spec, gain_spec],
        out_specs=[
            raw_spec,
            pl.BlockSpec((1, 1, head_dim), lambda h: (h, 0, 0)),
            pl.BlockSpec((tok_rows, head_dim), lambda h: (0, h)),
            pl.BlockSpec((tok_rows, head_dim), lambda h: (0, h)),
        ],
        out_shape=[
            jax.ShapeDtypeStruct((tok_rows, q_cols), jnp.bfloat16),
            jax.ShapeDtypeStruct((key_heads, 1, head_dim), jnp.float32),
            jax.ShapeDtypeStruct((tok_rows, kv_cols), jnp.float32),
            jax.ShapeDtypeStruct((tok_rows, kv_cols), jnp.float32),
        ],
        compiler_params=params,
        cost_estimate=pl.CostEstimate(
            flops=key_heads * own_tiles * 5 * tile_flops,
            transcendentals=key_heads * own_tiles * group * blk * blk,
            bytes_accessed=in_bytes + 2 * 4 * tok_rows * q_cols + 2 * 4 * tok_rows * kv_cols,
        ),
    )(*operands, log_sums, delta, dq_half, query_raw, query_gain.reshape(1, head_dim))
    return query_grad, jnp.sum(qgain_parts, axis=(0, 1)), dkv_halo, dk_own, dv_own


def per_device(query_raw, key_raw, value_proj, query_gain, key_gain, out_grad, doc_lengths):
    tok_rows = query_raw.shape[0]
    head_dim = query_gain.shape[0]
    query_heads = query_raw.shape[1] // head_dim
    key_heads = key_raw.shape[1] // head_dim
    first_pos = lax.axis_index("ctx") * tok_rows
    doc_ends = jnp.cumsum(doc_lengths)
    own_pos = first_pos + jnp.arange(tok_rows, dtype=jnp.int32)
    own_doc = doc_index(own_pos, doc_ends)
    halo_raw = first_pos - WINDOW + jnp.arange(WINDOW, dtype=jnp.int32)
    halo_doc = jnp.where(halo_raw >= 0, doc_index(halo_raw, doc_ends), -1)
    query_hat, query_inv = norm_rows(query_raw, query_heads)
    query_norm = (query_hat * query_gain).astype(jnp.bfloat16).reshape(tok_rows, query_heads * head_dim)
    key_hat, key_inv = norm_rows(key_raw, key_heads)
    key_norm = (key_hat * key_gain).astype(jnp.bfloat16).reshape(tok_rows, key_heads * head_dim)
    halo_keys, halo_vals = shifted((key_norm[tok_rows - WINDOW:], value_proj[tok_rows - WINDOW:]), "ctx", 1)
    keys_all = jnp.concatenate([halo_keys, key_norm], axis=0)
    vals_all = jnp.concatenate([halo_vals, value_proj], axis=0)
    all_doc = jnp.concatenate([halo_doc, own_doc])
    query_grad, query_part, dkv_halo, dk_own, dv_own = attention_grads(
        query_norm, out_grad, keys_all, vals_all, own_doc, all_doc, key_heads, head_dim, query_raw, query_gain
    )
    back = shifted(dkv_halo, "ctx", -1)
    key_grad, value_grad, key_parts = kv_final(dk_own, dv_own, back, key_raw, key_gain, key_heads, head_dim)
    key_part = jnp.sum(key_parts, axis=(0, 1))
    gain_grads = butterfly_sum(jnp.stack([query_part, key_part]), ("head", "ctx"))
    return (query_grad, key_grad, value_grad, gain_grads[0], gain_grads[1])


def solution(mesh):
    return jax.shard_map(
        per_device,
        mesh=mesh,
        in_specs=(
            P("ctx", "head"),
            P("ctx", "head"),
            P("ctx", "head"),
            P(),
            P(),
            P("ctx", "head"),
            P(),
        ),
        out_specs=(P("ctx", "head"), P("ctx", "head"), P("ctx", "head"), P(), P()),
        check_vma=False,
    )
```

```python
import functools
import math

import jax
import jax.numpy as jnp
from jax import lax
from jax.experimental import pallas as pl
from jax.experimental.pallas import tpu as pltpu
from jax.sharding import PartitionSpec as P

WINDOW = 1024
QUERY_SCALAR = 168


EPS = 1e-06
BLOCK = 256


def shifted(value, axis, steps):
    count = lax.axis_size(axis)
    leading, last = (max(0, -steps), min(count, count - steps))
    return lax.ppermute(value, axis, [(source, source + steps) for source in range(leading, last)])


def xor_tree(values):
    while len(values) > 1:
        values = [values[i] + values[i + 1] for i in range(0, len(values), 2)]
    return values[0]


def butterfly_sum(value, axes):
    for axis in axes:
        count = lax.axis_size(axis)
        if count & (count - 1):
            value = lax.psum(value, axis)
            continue
        bits = count.bit_length() - 1
        low = 0
        while low < bits:
            width = min(3, bits - low)
            shifted_parts = [value]
            for mask in range(1, 1 << width):
                pairs = [(source, source ^ (mask << low)) for source in range(count)]
                shifted_parts.append(lax.ppermute(value, axis, pairs))
            value = xor_tree(shifted_parts)
            low += width
    return value


def norm_rows(raw_rows, head_count):
    values = raw_rows.astype(jnp.float32).reshape(raw_rows.shape[0], head_count, -1)
    inverse = lax.rsqrt(jnp.mean(values * values, axis=-1, keepdims=True) + EPS)
    return (values * inverse, inverse)


def norm_back(raw_rows, gain_vec, head_count, upstream):
    scaled, inverse = norm_rows(raw_rows, head_count)
    incoming = upstream.reshape(scaled.shape)
    weighted = incoming * gain_vec
    inner_sum = jnp.mean(weighted * scaled, axis=-1, keepdims=True)
    result = inverse * (weighted - scaled * inner_sum)
    return (result.reshape(raw_rows.shape), jnp.sum(incoming * scaled, axis=(0, 1)))


def doc_index(positions, doc_ends):
    return jnp.sum((positions[:, None] >= doc_ends[None, :]).astype(jnp.int32), axis=1)


def tile_mask(qdoc_ref, kdoc_ref, q_first, t, group):
    blk = BLOCK
    n_tiles = WINDOW // blk + 1
    rows = lax.broadcasted_iota(jnp.int32, (blk, blk), 0)
    cols = lax.broadcasted_iota(jnp.int32, (blk, blk), 1)
    k_first = q_first + t * blk
    live = qdoc_ref[q_first:q_first + blk, :] == kdoc_ref[:, k_first:k_first + blk]
    if t == 0:
        live = live & (cols > rows)
    if t == n_tiles - 1:
        live = live & (cols + t * blk <= rows + WINDOW)
    return jnp.concatenate([live] * group, axis=0)


def stacked(ref, group, head_dim, first):
    blk = BLOCK
    return jnp.concatenate(
        [ref[first:first + blk, a * head_dim:(a + 1) * head_dim] for a in range(group)], axis=0
    )


def key_tile(halo_ref, kown_ref, vown_ref, k_first, head_dim):
    blk = BLOCK
    if k_first < WINDOW:
        return halo_ref[k_first:k_first + blk, :head_dim], halo_ref[k_first:k_first + blk, head_dim:]
    own_first = k_first - WINDOW
    return kown_ref[own_first:own_first + blk, :], vown_ref[own_first:own_first + blk, :]


def grad_tile(q_g, do_g, k_tile, v_tile, live, log_sums, delta):
    scale = QUERY_SCALAR ** (-0.5)
    scores = lax.dot_general(q_g, k_tile, (((1,), (1,)), ((), ())), preferred_element_type=jnp.float32) * scale
    weights = jnp.where(live, jnp.exp(scores - log_sums), 0.0)
    d_weights = lax.dot_general(do_g, v_tile, (((1,), (1,)), ((), ())), preferred_element_type=jnp.float32)
    d_scores = (weights * (d_weights - delta)).astype(jnp.bfloat16)
    dq_part = jnp.dot(d_scores, k_tile, preferred_element_type=jnp.float32)
    dk_part = lax.dot_general(d_scores, q_g, (((0,), (0,)), ((), ())), preferred_element_type=jnp.float32)
    dv_part = lax.dot_general(
        weights.astype(jnp.bfloat16), do_g, (((0,), (0,)), ((), ())), preferred_element_type=jnp.float32
    )
    return dq_part, dk_part * scale, dv_part


def halo_kernel(qdoc_ref, kdoc_ref, q_ref, do_ref, halo_ref, kown_ref, vown_ref,
                dq_ref, dkv_ref, lse_ref, delta_ref, dk_ref, dv_ref, *, group, head_dim):
    blk = BLOCK
    n_tiles = WINDOW // blk + 1
    n_halo = WINDOW // blk
    n_q = q_ref.shape[0] // blk
    gb = group * blk
    scale = QUERY_SCALAR ** (-0.5)
    dk_ref[...] = jnp.zeros(dk_ref.shape, jnp.float32)
    dv_ref[...] = jnp.zeros(dv_ref.shape, jnp.float32)
    for qb in range(n_q):
        q_first = qb * blk
        q_g = stacked(q_ref, group, head_dim, q_first)
        do_g = stacked(do_ref, group, head_dim, q_first)
        masks = [tile_mask(qdoc_ref, kdoc_ref, q_first, t, group) for t in range(n_tiles)]
        totals = jnp.zeros((gb, 1), jnp.float32)
        numer = jnp.zeros((gb, head_dim), jnp.float32)
        for t in range(n_tiles):
            k_tile, v_tile = key_tile(halo_ref, kown_ref, vown_ref, q_first + t * blk, head_dim)
            scores = lax.dot_general(
                q_g, k_tile, (((1,), (1,)), ((), ())), preferred_element_type=jnp.float32
            ) * scale
            exp_s = jnp.where(masks[t], jnp.exp(scores), 0.0)
            totals = totals + jnp.sum(exp_s, axis=1, keepdims=True)
            numer = numer + jnp.dot(exp_s.astype(jnp.bfloat16), v_tile, preferred_element_type=jnp.float32)
        log_sums = jnp.log(totals)
        attn_out = numer / totals
        delta = jnp.sum(do_g.astype(jnp.float32) * attn_out, axis=1, keepdims=True)
        lse_ref[qb * gb:(qb + 1) * gb, :] = log_sums
        delta_ref[qb * gb:(qb + 1) * gb, :] = delta
        dq = jnp.zeros((gb, head_dim), jnp.float32)
        for t in range(n_halo - qb):
            k_first = q_first + t * blk
            k_tile, v_tile = key_tile(halo_ref, kown_ref, vown_ref, k_first, head_dim)
            dq_part, dk_part, dv_part = grad_tile(q_g, do_g, k_tile, v_tile, masks[t], log_sums, delta)
            dq = dq + dq_part
            dk_ref[k_first:k_first + blk, :] += dk_part
            dv_ref[k_first:k_first + blk, :] += dv_part
        dq_ref[q_first:q_first + blk, :] = jnp.concatenate(
            [dq[a * blk:(a + 1) * blk] for a in range(group)], axis=1
        ) * scale
    dkv_ref[:, :head_dim] = dk_ref[...].astype(jnp.bfloat16)
    dkv_ref[:, head_dim:] = dv_ref[...].astype(jnp.bfloat16)


def norm_grad(raw, gain, upstream):
    inverse = lax.rsqrt(jnp.mean(raw * raw, axis=1, keepdims=True) + EPS)
    scaled = raw * inverse
    weighted = upstream * gain
    inner_sum = jnp.mean(weighted * scaled, axis=1, keepdims=True)
    result = inverse * (weighted - scaled * inner_sum)
    return result, jnp.sum(upstream * scaled, axis=0, keepdims=True)


def own_kernel(qdoc_ref, kdoc_ref, q_ref, do_ref, kown_ref, vown_ref, lse_ref, delta_ref, dq_in_ref, raw_ref,
               gain_ref, qgrad_ref, qgain_ref, dk_ref, dv_ref, *, group, head_dim):
    blk = BLOCK
    n_tiles = WINDOW // blk + 1
    n_halo = WINDOW // blk
    n_q = q_ref.shape[0] // blk
    gb = group * blk
    scale = QUERY_SCALAR ** (-0.5)
    dk_ref[...] = jnp.zeros(dk_ref.shape, jnp.float32)
    dv_ref[...] = jnp.zeros(dv_ref.shape, jnp.float32)
    gain = gain_ref[...]
    gain_sum = jnp.zeros((1, head_dim), jnp.float32)
    for qb in range(n_q):
        q_first = qb * blk
        q_g = stacked(q_ref, group, head_dim, q_first)
        do_g = stacked(do_ref, group, head_dim, q_first)
        log_sums = lse_ref[qb * gb:(qb + 1) * gb, :]
        delta = delta_ref[qb * gb:(qb + 1) * gb, :]
        dq = jnp.zeros((gb, head_dim), jnp.float32)
        for t in range(max(0, n_halo - qb), n_tiles):
            live = tile_mask(qdoc_ref, kdoc_ref, q_first, t, group)
            k_first = q_first + t * blk
            k_tile, v_tile = key_tile(None, kown_ref, vown_ref, k_first, head_dim)
            dq_part, dk_part, dv_part = grad_tile(q_g, do_g, k_tile, v_tile, live, log_sums, delta)
            dq = dq + dq_part
            own_first = k_first - WINDOW
            dk_ref[own_first:own_first + blk, :] += dk_part
            dv_ref[own_first:own_first + blk, :] += dv_part
        dq_in = dq_in_ref[q_first:q_first + blk, :]
        raw = raw_ref[q_first:q_first + blk, :].astype(jnp.float32)
        for a in range(group):
            cols = slice(a * head_dim, (a + 1) * head_dim)
            upstream = dq_in[:, cols] + dq[a * blk:(a + 1) * blk] * scale
            result, part = norm_grad(raw[:, cols], gain, upstream)
            qgrad_ref[q_first:q_first + blk, cols] = result.astype(qgrad_ref.dtype)
            gain_sum = gain_sum + part
    qgain_ref[...] = gain_sum.reshape(qgain_ref.shape)


def kv_final_kernel(dk_ref, dv_ref, back_ref, raw_ref, gain_ref, kgrad_ref, vgrad_ref, kgain_ref, *, head_dim):
    tok_rows = dk_ref.shape[0]
    lead = tok_rows - WINDOW
    back = back_ref[...].astype(jnp.float32)
    dk = dk_ref[...]
    dv = dv_ref[...]
    if lead:
        dk = jnp.concatenate([dk[:lead], dk[lead:] + back[:, :head_dim]], axis=0)
        dv = jnp.concatenate([dv[:lead], dv[lead:] + back[:, head_dim:]], axis=0)
    else:
        dk = dk + back[:, :head_dim]
        dv = dv + back[:, head_dim:]
    vgrad_ref[...] = dv.astype(vgrad_ref.dtype)
    result, part = norm_grad(raw_ref[...].astype(jnp.float32), gain_ref[...], dk)
    kgrad_ref[...] = result.astype(kgrad_ref.dtype)
    kgain_ref[...] = part


def head_pipeline(h, operands, key_norm, value_proj, key_raw, query_raw, query_gain, key_gain, head_dim, group):
    qdoc, kdoc, query_norm, grad_rows = operands
    tok_rows, q_cols = query_norm.shape
    blk = BLOCK
    n_q = tok_rows // blk
    n_tiles = WINDOW // blk + 1
    gw = group * head_dim
    gb_rows = n_q * group * blk
    tile_flops = 2 * (group * blk) * blk * head_dim
    halo_tiles = sum(max(0, WINDOW // blk - qb) for qb in range(n_q))
    own_tiles = n_q * n_tiles - halo_tiles
    send = jnp.concatenate(
        [key_norm[tok_rows - WINDOW:, h * head_dim:(h + 1) * head_dim],
         value_proj[tok_rows - WINDOW:, h * head_dim:(h + 1) * head_dim]],
        axis=1,
    )
    halo = shifted(send, "ctx", 1)
    full = lambda shape: pl.BlockSpec(shape, lambda i: (0, 0))
    qcol = pl.BlockSpec((tok_rows, gw), lambda i, h=h: (0, h))
    kcol = pl.BlockSpec((tok_rows, head_dim), lambda i, h=h: (0, h))
    stat = full((gb_rows, 1))
    params = pltpu.CompilerParams(dimension_semantics=("arbitrary",))
    in_bytes = 2 * 2 * tok_rows * gw + 2 * 2 * (WINDOW + tok_rows) * head_dim
    dq_half, dkv_halo, log_sums, delta = pl.pallas_call(
        functools.partial(halo_kernel, group=group, head_dim=head_dim),
        grid=(1,),
        in_specs=[full(qdoc.shape), full(kdoc.shape), qcol, qcol, full((WINDOW, 2 * head_dim)), kcol, kcol],
        out_specs=[full((tok_rows, gw)), full((WINDOW, 2 * head_dim)), stat, stat],
        out_shape=[
            jax.ShapeDtypeStruct((tok_rows, gw), jnp.float32),
            jax.ShapeDtypeStruct((WINDOW, 2 * head_dim), jnp.bfloat16),
            jax.ShapeDtypeStruct((gb_rows, 1), jnp.float32),
            jax.ShapeDtypeStruct((gb_rows, 1), jnp.float32),
        ],
        scratch_shapes=[pltpu.VMEM((WINDOW, head_dim), jnp.float32), pltpu.VMEM((WINDOW, head_dim), jnp.float32)],
        compiler_params=params,
        cost_estimate=pl.CostEstimate(
            flops=(2 * n_q * n_tiles + 5 * halo_tiles) * tile_flops,
            transcendentals=(n_q * n_tiles + halo_tiles) * group * blk * blk,
            bytes_accessed=in_bytes + 4 * tok_rows * gw + 2 * 2 * WINDOW * head_dim,
        ),
    )(qdoc, kdoc, query_norm, grad_rows, halo, key_norm, value_proj)
    back = shifted(dkv_halo, "ctx", -1)
    query_grad, qgain_part, dk_own, dv_own = pl.pallas_call(
        functools.partial(own_kernel, group=group, head_dim=head_dim),
        grid=(1,),
        in_specs=[full(qdoc.shape), full(kdoc.shape), qcol, qcol, kcol, kcol, stat, stat,
                  full((tok_rows, gw)), qcol, full((1, head_dim))],
        out_specs=[full((tok_rows, gw)), full((1, head_dim)), full((tok_rows, head_dim)), full((tok_rows, head_dim))],
        out_shape=[
            jax.ShapeDtypeStruct((tok_rows, gw), jnp.bfloat16),
            jax.ShapeDtypeStruct((1, head_dim), jnp.float32),
            jax.ShapeDtypeStruct((tok_rows, head_dim), jnp.float32),
            jax.ShapeDtypeStruct((tok_rows, head_dim), jnp.float32),
        ],
        compiler_params=params,
        cost_estimate=pl.CostEstimate(
            flops=own_tiles * 5 * tile_flops,
            transcendentals=own_tiles * group * blk * blk,
            bytes_accessed=in_bytes + 2 * 4 * tok_rows * gw + 2 * 4 * tok_rows * head_dim,
        ),
    )(qdoc, kdoc, query_norm, grad_rows, key_norm, value_proj, log_sums, delta, dq_half, query_raw,
      query_gain.reshape(1, head_dim))
    col = full((tok_rows, head_dim))
    key_grad, value_grad, kgain_part = pl.pallas_call(
        functools.partial(kv_final_kernel, head_dim=head_dim),
        grid=(1,),
        in_specs=[col, col, full((WINDOW, 2 * head_dim)), kcol, full((1, head_dim))],
        out_specs=[col, col, full((1, head_dim))],
        out_shape=[
            jax.ShapeDtypeStruct((tok_rows, head_dim), jnp.bfloat16),
            jax.ShapeDtypeStruct((tok_rows, head_dim), jnp.bfloat16),
            jax.ShapeDtypeStruct((1, head_dim), jnp.float32),
        ],
        compiler_params=params,
    )(dk_own, dv_own, back, key_raw, key_gain.reshape(1, head_dim))
    return query_grad, key_grad, value_grad, qgain_part, kgain_part


def per_device(query_raw, key_raw, value_proj, query_gain, key_gain, out_grad, doc_lengths):
    tok_rows = query_raw.shape[0]
    head_dim = query_gain.shape[0]
    query_heads = query_raw.shape[1] // head_dim
    key_heads = key_raw.shape[1] // head_dim
    group = query_heads // key_heads
    first_pos = lax.axis_index("ctx") * tok_rows
    doc_ends = jnp.cumsum(doc_lengths)
    own_pos = first_pos + jnp.arange(tok_rows, dtype=jnp.int32)
    own_doc = doc_index(own_pos, doc_ends)
    halo_raw = first_pos - WINDOW + jnp.arange(WINDOW, dtype=jnp.int32)
    halo_doc = jnp.where(halo_raw >= 0, doc_index(halo_raw, doc_ends), -1)
    query_hat, query_inv = norm_rows(query_raw, query_heads)
    query_norm = (query_hat * query_gain).astype(jnp.bfloat16).reshape(tok_rows, query_heads * head_dim)
    key_hat, key_inv = norm_rows(key_raw, key_heads)
    key_norm = (key_hat * key_gain).astype(jnp.bfloat16).reshape(tok_rows, key_heads * head_dim)
    all_doc = jnp.concatenate([halo_doc, own_doc])
    operands = (own_doc.reshape(tok_rows, 1), all_doc.reshape(1, WINDOW + tok_rows), query_norm, out_grad)
    pieces = [
        head_pipeline(h, operands, key_norm, value_proj, key_raw, query_raw, query_gain, key_gain, head_dim, group)
        for h in range(key_heads)
    ]
    query_grad = jnp.concatenate([p[0] for p in pieces], axis=1)
    key_grad = jnp.concatenate([p[1] for p in pieces], axis=1)
    value_grad = jnp.concatenate([p[2] for p in pieces], axis=1)
    key_part = pieces[0][4]
    for p in pieces[1:]:
        key_part = key_part + p[4]
    query_part = pieces[0][3]
    for p in pieces[1:]:
        query_part = query_part + p[3]
    gain_grads = butterfly_sum(jnp.concatenate([query_part, key_part], axis=0), ("head", "ctx"))
    return (query_grad, key_grad, value_grad, gain_grads[0], gain_grads[1])


def solution(mesh):
    return jax.shard_map(
        per_device,
        mesh=mesh,
        in_specs=(
            P("ctx", "head"),
            P("ctx", "head"),
            P("ctx", "head"),
            P(),
            P(),
            P("ctx", "head"),
            P(),
        ),
        out_specs=(P("ctx", "head"), P("ctx", "head"), P("ctx", "head"), P(), P()),
        check_vma=False,
    )
```

```python
import functools
import math

import jax
import jax.numpy as jnp
from jax import lax
from jax.experimental import pallas as pl
from jax.experimental.pallas import tpu as pltpu
from jax.sharding import PartitionSpec as P

WINDOW = 1024
QUERY_SCALAR = 168


EPS = 1e-06
BLOCK = 256


def shifted(value, axis, steps):
    count = lax.axis_size(axis)
    leading, last = (max(0, -steps), min(count, count - steps))
    return lax.ppermute(value, axis, [(source, source + steps) for source in range(leading, last)])


def xor_tree(values):
    while len(values) > 1:
        values = [values[i] + values[i + 1] for i in range(0, len(values), 2)]
    return values[0]


def butterfly_sum(value, axes):
    for axis in axes:
        count = lax.axis_size(axis)
        if count & (count - 1):
            value = lax.psum(value, axis)
            continue
        bits = count.bit_length() - 1
        low = 0
        while low < bits:
            width = 1
            shifted_parts = [value]
            for mask in range(1, 1 << width):
                pairs = [(source, source ^ (mask << low)) for source in range(count)]
                shifted_parts.append(lax.ppermute(value, axis, pairs))
            value = xor_tree(shifted_parts)
            low += width
    return value


def norm_rows(raw_rows, head_count):
    values = raw_rows.astype(jnp.float32).reshape(raw_rows.shape[0], head_count, -1)
    inverse = lax.rsqrt(jnp.mean(values * values, axis=-1, keepdims=True) + EPS)
    return (values * inverse, inverse)


def norm_back(raw_rows, gain_vec, head_count, upstream):
    scaled, inverse = norm_rows(raw_rows, head_count)
    incoming = upstream.reshape(scaled.shape)
    weighted = incoming * gain_vec
    inner_sum = jnp.mean(weighted * scaled, axis=-1, keepdims=True)
    result = inverse * (weighted - scaled * inner_sum)
    return (result.reshape(raw_rows.shape), jnp.sum(incoming * scaled, axis=(0, 1)))


def doc_index(positions, doc_ends):
    return jnp.sum((positions[:, None] >= doc_ends[None, :]).astype(jnp.int32), axis=1)


def tile_mask(qdoc_ref, kdoc_ref, q_first, t, group):
    blk = BLOCK
    n_tiles = WINDOW // blk + 1
    rows = lax.broadcasted_iota(jnp.int32, (blk, blk), 0)
    cols = lax.broadcasted_iota(jnp.int32, (blk, blk), 1)
    k_first = q_first + t * blk
    live = qdoc_ref[q_first:q_first + blk, :] == kdoc_ref[:, k_first:k_first + blk]
    if t == 0:
        live = live & (cols > rows)
    if t == n_tiles - 1:
        live = live & (cols + t * blk <= rows + WINDOW)
    return jnp.concatenate([live] * group, axis=0), k_first


def stacked(ref, group, head_dim, first):
    blk = BLOCK
    return jnp.concatenate(
        [ref[first:first + blk, a * head_dim:(a + 1) * head_dim] for a in range(group)], axis=0
    )


def grad_tile(q_g, do_g, k_tile, v_tile, live, log_sums, delta):
    scale = QUERY_SCALAR ** (-0.5)
    scores = lax.dot_general(q_g, k_tile, (((1,), (1,)), ((), ())), preferred_element_type=jnp.float32) * scale
    weights = jnp.where(live, jnp.exp(scores - log_sums), 0.0)
    d_weights = lax.dot_general(do_g, v_tile, (((1,), (1,)), ((), ())), preferred_element_type=jnp.float32)
    d_scores = (weights * (d_weights - delta)).astype(jnp.bfloat16)
    dq_part = jnp.dot(d_scores, k_tile, preferred_element_type=jnp.float32)
    dk_part = lax.dot_general(d_scores, q_g, (((0,), (0,)), ((), ())), preferred_element_type=jnp.float32)
    dv_part = lax.dot_general(
        weights.astype(jnp.bfloat16), do_g, (((0,), (0,)), ((), ())), preferred_element_type=jnp.float32
    )
    return dq_part, dk_part * scale, dv_part


def halo_kernel(qdoc_ref, kdoc_ref, q_ref, do_ref, k_ref, v_ref,
                dq_ref, dkv_ref, lse_ref, delta_ref, dk_ref, dv_ref, *, group, head_dim):
    blk = BLOCK
    n_tiles = WINDOW // blk + 1
    n_halo = WINDOW // blk
    n_q = q_ref.shape[0] // blk
    gb = group * blk
    scale = QUERY_SCALAR ** (-0.5)
    dk_ref[...] = jnp.zeros(dk_ref.shape, jnp.float32)
    dv_ref[...] = jnp.zeros(dv_ref.shape, jnp.float32)
    for qb in range(n_q):
        q_first = qb * blk
        q_g = stacked(q_ref, group, head_dim, q_first)
        do_g = stacked(do_ref, group, head_dim, q_first)
        masks = [tile_mask(qdoc_ref, kdoc_ref, q_first, t, group)[0] for t in range(n_tiles)]
        totals = jnp.zeros((gb, 1), jnp.float32)
        numer = jnp.zeros((gb, head_dim), jnp.float32)
        for t in range(n_tiles):
            k_first = q_first + t * blk
            k_tile = k_ref[k_first:k_first + blk, :]
            v_tile = v_ref[k_first:k_first + blk, :]
            scores = lax.dot_general(
                q_g, k_tile, (((1,), (1,)), ((), ())), preferred_element_type=jnp.float32
            ) * scale
            exp_s = jnp.where(masks[t], jnp.exp(scores), 0.0)
            totals = totals + jnp.sum(exp_s, axis=1, keepdims=True)
            numer = numer + jnp.dot(exp_s.astype(jnp.bfloat16), v_tile, preferred_element_type=jnp.float32)
        log_sums = jnp.log(totals)
        attn_out = numer / totals
        delta = jnp.sum(do_g.astype(jnp.float32) * attn_out, axis=1, keepdims=True)
        lse_ref[qb * gb:(qb + 1) * gb, :] = log_sums
        delta_ref[qb * gb:(qb + 1) * gb, :] = delta
        dq = jnp.zeros((gb, head_dim), jnp.float32)
        for t in range(n_halo - qb):
            k_first = q_first + t * blk
            k_tile = k_ref[k_first:k_first + blk, :]
            v_tile = v_ref[k_first:k_first + blk, :]
            dq_part, dk_part, dv_part = grad_tile(q_g, do_g, k_tile, v_tile, masks[t], log_sums, delta)
            dq = dq + dq_part
            dk_ref[k_first:k_first + blk, :] += dk_part
            dv_ref[k_first:k_first + blk, :] += dv_part
        dq_ref[q_first:q_first + blk, :] = jnp.concatenate(
            [dq[a * blk:(a + 1) * blk] for a in range(group)], axis=1
        ) * scale
    dkv_ref[:, :head_dim] = dk_ref[...].astype(jnp.bfloat16)
    dkv_ref[:, head_dim:] = dv_ref[...].astype(jnp.bfloat16)


def norm_grad(raw, gain, upstream):
    inverse = lax.rsqrt(jnp.mean(raw * raw, axis=1, keepdims=True) + EPS)
    scaled = raw * inverse
    weighted = upstream * gain
    inner_sum = jnp.mean(weighted * scaled, axis=1, keepdims=True)
    result = inverse * (weighted - scaled * inner_sum)
    return result, jnp.sum(upstream * scaled, axis=0, keepdims=True)


def own_kernel(qdoc_ref, kdoc_ref, q_ref, do_ref, k_ref, v_ref, lse_ref, delta_ref, dq_in_ref, raw_ref, gain_ref,
               qgrad_ref, qgain_ref, dk_ref, dv_ref, *, group, head_dim):
    blk = BLOCK
    n_tiles = WINDOW // blk + 1
    n_halo = WINDOW // blk
    n_q = q_ref.shape[0] // blk
    gb = group * blk
    scale = QUERY_SCALAR ** (-0.5)
    dk_ref[...] = jnp.zeros(dk_ref.shape, jnp.float32)
    dv_ref[...] = jnp.zeros(dv_ref.shape, jnp.float32)
    gain = gain_ref[...]
    gain_sum = jnp.zeros((1, head_dim), jnp.float32)
    for qb in range(n_q):
        q_first = qb * blk
        q_g = stacked(q_ref, group, head_dim, q_first)
        do_g = stacked(do_ref, group, head_dim, q_first)
        log_sums = lse_ref[qb * gb:(qb + 1) * gb, :]
        delta = delta_ref[qb * gb:(qb + 1) * gb, :]
        dq = jnp.zeros((gb, head_dim), jnp.float32)
        for t in range(max(0, n_halo - qb), n_tiles):
            live, _ = tile_mask(qdoc_ref, kdoc_ref, q_first, t, group)
            k_first = q_first + t * blk
            k_tile = k_ref[k_first:k_first + blk, :]
            v_tile = v_ref[k_first:k_first + blk, :]
            dq_part, dk_part, dv_part = grad_tile(q_g, do_g, k_tile, v_tile, live, log_sums, delta)
            dq = dq + dq_part
            own_first = k_first - WINDOW
            dk_ref[own_first:own_first + blk, :] += dk_part
            dv_ref[own_first:own_first + blk, :] += dv_part
        dq_in = dq_in_ref[q_first:q_first + blk, :]
        raw = raw_ref[q_first:q_first + blk, :].astype(jnp.float32)
        for a in range(group):
            cols = slice(a * head_dim, (a + 1) * head_dim)
            upstream = dq_in[:, cols] + dq[a * blk:(a + 1) * blk] * scale
            result, part = norm_grad(raw[:, cols], gain, upstream)
            qgrad_ref[q_first:q_first + blk, cols] = result.astype(qgrad_ref.dtype)
            gain_sum = gain_sum + part
    qgain_ref[...] = gain_sum.reshape(qgain_ref.shape)


def kv_final_kernel(dk_ref, dv_ref, back_ref, raw_ref, gain_ref, kgrad_ref, vgrad_ref, kgain_ref, *, head_dim):
    tok_rows = dk_ref.shape[0]
    lead = tok_rows - WINDOW
    back = back_ref[...].astype(jnp.float32)
    dk = dk_ref[...]
    dv = dv_ref[...]
    if lead:
        dk = jnp.concatenate([dk[:lead], dk[lead:] + back[:, :head_dim]], axis=0)
        dv = jnp.concatenate([dv[:lead], dv[lead:] + back[:, head_dim:]], axis=0)
    else:
        dk = dk + back[:, :head_dim]
        dv = dv + back[:, head_dim:]
    vgrad_ref[...] = dv.astype(vgrad_ref.dtype)
    result, part = norm_grad(raw_ref[...].astype(jnp.float32), gain_ref[...], dk)
    kgrad_ref[...] = result.astype(kgrad_ref.dtype)
    kgain_ref[...] = part.reshape(kgain_ref.shape)


def kv_final(dk_own, dv_own, back, key_raw, key_gain, key_heads, head_dim):
    tok_rows = dk_own.shape[0]
    kv_cols = key_heads * head_dim
    col_spec = pl.BlockSpec((tok_rows, head_dim), lambda h: (0, h))
    return pl.pallas_call(
        functools.partial(kv_final_kernel, head_dim=head_dim),
        grid=(key_heads,),
        in_specs=[
            col_spec,
            col_spec,
            pl.BlockSpec((WINDOW, 2 * head_dim), lambda h: (0, h)),
            col_spec,
            pl.BlockSpec((1, head_dim), lambda h: (0, 0)),
        ],
        out_specs=[col_spec, col_spec, pl.BlockSpec((1, 1, head_dim), lambda h: (h, 0, 0))],
        out_shape=[
            jax.ShapeDtypeStruct((tok_rows, kv_cols), jnp.bfloat16),
            jax.ShapeDtypeStruct((tok_rows, kv_cols), jnp.bfloat16),
            jax.ShapeDtypeStruct((key_heads, 1, head_dim), jnp.float32),
        ],
        compiler_params=pltpu.CompilerParams(dimension_semantics=("arbitrary",)),
    )(dk_own, dv_own, back, key_raw, key_gain.reshape(1, head_dim))


def attention_grads(query_norm, grad_rows, keys_all, vals_all, own_doc, all_doc, key_heads, head_dim,
                    query_raw, query_gain):
    tok_rows, q_cols = query_norm.shape
    key_rows = keys_all.shape[0]
    group = q_cols // (key_heads * head_dim)
    blk = BLOCK
    n_q = tok_rows // blk
    n_tiles = WINDOW // blk + 1
    gw = group * head_dim
    kv_cols = key_heads * head_dim
    stat_rows = key_heads * n_q * group * blk
    tile_flops = 2 * (group * blk) * blk * head_dim
    halo_tiles = sum(max(0, WINDOW // blk - qb) for qb in range(n_q))
    own_tiles = n_q * n_tiles - halo_tiles
    common_specs = [
        pl.BlockSpec((tok_rows, 1), lambda h: (0, 0)),
        pl.BlockSpec((1, key_rows), lambda h: (0, 0)),
        pl.BlockSpec((tok_rows, gw), lambda h: (0, h)),
        pl.BlockSpec((tok_rows, gw), lambda h: (0, h)),
        pl.BlockSpec((key_rows, head_dim), lambda h: (0, h)),
        pl.BlockSpec((key_rows, head_dim), lambda h: (0, h)),
    ]
    stat_spec = pl.BlockSpec((n_q * group * blk, 1), lambda h: (h, 0))
    dq_spec = pl.BlockSpec((tok_rows, gw), lambda h: (0, h))
    params = pltpu.CompilerParams(dimension_semantics=("arbitrary",))
    in_bytes = 2 * 2 * tok_rows * q_cols + 2 * 2 * key_rows * kv_cols
    operands = (own_doc.reshape(tok_rows, 1), all_doc.reshape(1, key_rows), query_norm, grad_rows, keys_all, vals_all)
    dq_half, dkv_halo, log_sums, delta = pl.pallas_call(
        functools.partial(halo_kernel, group=group, head_dim=head_dim),
        grid=(key_heads,),
        in_specs=common_specs,
        out_specs=[
            dq_spec,
            pl.BlockSpec((WINDOW, 2 * head_dim), lambda h: (0, h)),
            stat_spec,
            stat_spec,
        ],
        out_shape=[
            jax.ShapeDtypeStruct((tok_rows, q_cols), jnp.float32),
            jax.ShapeDtypeStruct((WINDOW, 2 * kv_cols), jnp.bfloat16),
            jax.ShapeDtypeStruct((stat_rows, 1), jnp.float32),
            jax.ShapeDtypeStruct((stat_rows, 1), jnp.float32),
        ],
        scratch_shapes=[
            pltpu.VMEM((WINDOW, head_dim), jnp.float32),
            pltpu.VMEM((WINDOW, head_dim), jnp.float32),
        ],
        compiler_params=params,
        cost_estimate=pl.CostEstimate(
            flops=key_heads * (2 * n_q * n_tiles + 5 * halo_tiles) * tile_flops,
            transcendentals=key_heads * (n_q * n_tiles + halo_tiles) * group * blk * blk,
            bytes_accessed=in_bytes + 4 * tok_rows * q_cols + 2 * 2 * WINDOW * kv_cols,
        ),
    )(*operands)
    raw_spec = pl.BlockSpec((tok_rows, gw), lambda h: (0, h))
    gain_spec = pl.BlockSpec((1, head_dim), lambda h: (0, 0))
    query_grad, qgain_parts, dk_own, dv_own = pl.pallas_call(
        functools.partial(own_kernel, group=group, head_dim=head_dim),
        grid=(key_heads,),
        in_specs=common_specs + [stat_spec, stat_spec, dq_spec, raw_spec, gain_spec],
        out_specs=[
            raw_spec,
            pl.BlockSpec((1, 1, head_dim), lambda h: (h, 0, 0)),
            pl.BlockSpec((tok_rows, head_dim), lambda h: (0, h)),
            pl.BlockSpec((tok_rows, head_dim), lambda h: (0, h)),
        ],
        out_shape=[
            jax.ShapeDtypeStruct((tok_rows, q_cols), jnp.bfloat16),
            jax.ShapeDtypeStruct((key_heads, 1, head_dim), jnp.float32),
            jax.ShapeDtypeStruct((tok_rows, kv_cols), jnp.float32),
            jax.ShapeDtypeStruct((tok_rows, kv_cols), jnp.float32),
        ],
        compiler_params=params,
        cost_estimate=pl.CostEstimate(
            flops=key_heads * own_tiles * 5 * tile_flops,
            transcendentals=key_heads * own_tiles * group * blk * blk,
            bytes_accessed=in_bytes + 2 * 4 * tok_rows * q_cols + 2 * 4 * tok_rows * kv_cols,
        ),
    )(*operands, log_sums, delta, dq_half, query_raw, query_gain.reshape(1, head_dim))
    return query_grad, jnp.sum(qgain_parts, axis=(0, 1)), dkv_halo, dk_own, dv_own


def per_device(query_raw, key_raw, value_proj, query_gain, key_gain, out_grad, doc_lengths):
    tok_rows = query_raw.shape[0]
    head_dim = query_gain.shape[0]
    query_heads = query_raw.shape[1] // head_dim
    key_heads = key_raw.shape[1] // head_dim
    first_pos = lax.axis_index("ctx") * tok_rows
    doc_ends = jnp.cumsum(doc_lengths)
    own_pos = first_pos + jnp.arange(tok_rows, dtype=jnp.int32)
    own_doc = doc_index(own_pos, doc_ends)
    halo_raw = first_pos - WINDOW + jnp.arange(WINDOW, dtype=jnp.int32)
    halo_doc = jnp.where(halo_raw >= 0, doc_index(halo_raw, doc_ends), -1)
    query_hat, query_inv = norm_rows(query_raw, query_heads)
    query_norm = (query_hat * query_gain).astype(jnp.bfloat16).reshape(tok_rows, query_heads * head_dim)
    key_hat, key_inv = norm_rows(key_raw, key_heads)
    key_norm = (key_hat * key_gain).astype(jnp.bfloat16).reshape(tok_rows, key_heads * head_dim)
    halo_keys, halo_vals = shifted((key_norm[tok_rows - WINDOW:], value_proj[tok_rows - WINDOW:]), "ctx", 1)
    keys_all = jnp.concatenate([halo_keys, key_norm], axis=0)
    vals_all = jnp.concatenate([halo_vals, value_proj], axis=0)
    all_doc = jnp.concatenate([halo_doc, own_doc])
    query_grad, query_part, dkv_halo, dk_own, dv_own = attention_grads(
        query_norm, out_grad, keys_all, vals_all, own_doc, all_doc, key_heads, head_dim, query_raw, query_gain
    )
    back = shifted(dkv_halo, "ctx", -1)
    key_grad, value_grad, key_parts = kv_final(dk_own, dv_own, back, key_raw, key_gain, key_heads, head_dim)
    key_part = jnp.sum(key_parts, axis=(0, 1))
    gain_grads = butterfly_sum(jnp.stack([query_part, key_part]), ("head", "ctx"))
    return (query_grad, key_grad, value_grad, gain_grads[0], gain_grads[1])


def solution(mesh):
    return jax.shard_map(
        per_device,
        mesh=mesh,
        in_specs=(
            P("ctx", "head"),
            P("ctx", "head"),
            P("ctx", "head"),
            P(),
            P(),
            P("ctx", "head"),
            P(),
        ),
        out_specs=(P("ctx", "head"), P("ctx", "head"), P("ctx", "head"), P(), P()),
        check_vma=False,
    )
```

```python
import functools
import math

import jax
import jax.numpy as jnp
from jax import lax
from jax.experimental import pallas as pl
from jax.experimental.pallas import tpu as pltpu
from jax.sharding import PartitionSpec as P

WINDOW = 1024
QUERY_SCALAR = 168


EPS = 1e-06
BLOCK = 256


def shifted(value, axis, steps):
    count = lax.axis_size(axis)
    leading, last = (max(0, -steps), min(count, count - steps))
    return lax.ppermute(value, axis, [(source, source + steps) for source in range(leading, last)])


def xor_tree(values):
    while len(values) > 1:
        values = [values[i] + values[i + 1] for i in range(0, len(values), 2)]
    return values[0]


def butterfly_sum(value, axes):
    for axis in axes:
        count = lax.axis_size(axis)
        if count & (count - 1):
            value = lax.psum(value, axis)
            continue
        bits = count.bit_length() - 1
        low = 0
        while low < bits:
            width = 1
            shifted_parts = [value]
            for mask in range(1, 1 << width):
                pairs = [(source, source ^ (mask << low)) for source in range(count)]
                shifted_parts.append(lax.ppermute(value, axis, pairs))
            value = xor_tree(shifted_parts)
            low += width
    return value


def norm_rows(raw_rows, head_count):
    values = raw_rows.astype(jnp.float32).reshape(raw_rows.shape[0], head_count, -1)
    inverse = lax.rsqrt(jnp.mean(values * values, axis=-1, keepdims=True) + EPS)
    return (values * inverse, inverse)


def norm_back(raw_rows, gain_vec, head_count, upstream):
    scaled, inverse = norm_rows(raw_rows, head_count)
    incoming = upstream.reshape(scaled.shape)
    weighted = incoming * gain_vec
    inner_sum = jnp.mean(weighted * scaled, axis=-1, keepdims=True)
    result = inverse * (weighted - scaled * inner_sum)
    return (result.reshape(raw_rows.shape), jnp.sum(incoming * scaled, axis=(0, 1)))


def doc_index(positions, doc_ends):
    return jnp.sum((positions[:, None] >= doc_ends[None, :]).astype(jnp.int32), axis=1)


def tile_mask(qdoc_ref, kdoc_ref, q_first, t, group):
    blk = BLOCK
    n_tiles = WINDOW // blk + 1
    rows = lax.broadcasted_iota(jnp.int32, (blk, blk), 0)
    cols = lax.broadcasted_iota(jnp.int32, (blk, blk), 1)
    k_first = q_first + t * blk
    live = qdoc_ref[q_first:q_first + blk, :] == kdoc_ref[:, k_first:k_first + blk]
    if t == 0:
        live = live & (cols > rows)
    if t == n_tiles - 1:
        live = live & (cols + t * blk <= rows + WINDOW)
    return jnp.concatenate([live] * group, axis=0), k_first


def stacked(ref, group, head_dim, first):
    blk = BLOCK
    return jnp.concatenate(
        [ref[first:first + blk, a * head_dim:(a + 1) * head_dim] for a in range(group)], axis=0
    )


def grad_tile(q_g, do_g, k_tile, v_tile, live, log_sums, delta):
    scale = QUERY_SCALAR ** (-0.5)
    scores = lax.dot_general(q_g, k_tile, (((1,), (1,)), ((), ())), preferred_element_type=jnp.float32) * scale
    weights = jnp.where(live, jnp.exp(scores - log_sums), 0.0)
    d_weights = lax.dot_general(do_g, v_tile, (((1,), (1,)), ((), ())), preferred_element_type=jnp.float32)
    d_scores = (weights * (d_weights - delta)).astype(jnp.bfloat16)
    dq_part = jnp.dot(d_scores, k_tile, preferred_element_type=jnp.float32)
    dk_part = lax.dot_general(d_scores, q_g, (((0,), (0,)), ((), ())), preferred_element_type=jnp.float32)
    dv_part = lax.dot_general(
        weights.astype(jnp.bfloat16), do_g, (((0,), (0,)), ((), ())), preferred_element_type=jnp.float32
    )
    return dq_part, dk_part * scale, dv_part


def halo_kernel(qdoc_ref, kdoc_ref, q_ref, do_ref, k_ref, v_ref, kgain_ref,
                dq_ref, dkv_ref, lse_ref, delta_ref, kpart_ref, dk_ref, dv_ref, kn_ref, *, group, head_dim):
    blk = BLOCK
    n_tiles = WINDOW // blk + 1
    n_halo = WINDOW // blk
    n_q = q_ref.shape[0] // blk
    gb = group * blk
    scale = QUERY_SCALAR ** (-0.5)
    dk_ref[...] = jnp.zeros(dk_ref.shape, jnp.float32)
    dv_ref[...] = jnp.zeros(dv_ref.shape, jnp.float32)
    halo_raw = k_ref[0:WINDOW, :].astype(jnp.float32)
    halo_inv = lax.rsqrt(jnp.mean(halo_raw * halo_raw, axis=1, keepdims=True) + EPS)
    kn_ref[...] = (halo_raw * halo_inv * kgain_ref[...]).astype(jnp.bfloat16)

    def key_tile(k_first):
        src = kn_ref if k_first < WINDOW else k_ref
        return src[k_first:k_first + blk, :], v_ref[k_first:k_first + blk, :]
    for qb in range(n_q):
        q_first = qb * blk
        q_g = stacked(q_ref, group, head_dim, q_first)
        do_g = stacked(do_ref, group, head_dim, q_first)
        masks = [tile_mask(qdoc_ref, kdoc_ref, q_first, t, group)[0] for t in range(n_tiles)]
        totals = jnp.zeros((gb, 1), jnp.float32)
        numer = jnp.zeros((gb, head_dim), jnp.float32)
        for t in range(n_tiles):
            k_first = q_first + t * blk
            k_tile, v_tile = key_tile(k_first)
            scores = lax.dot_general(
                q_g, k_tile, (((1,), (1,)), ((), ())), preferred_element_type=jnp.float32
            ) * scale
            exp_s = jnp.where(masks[t], jnp.exp(scores), 0.0)
            totals = totals + jnp.sum(exp_s, axis=1, keepdims=True)
            numer = numer + jnp.dot(exp_s.astype(jnp.bfloat16), v_tile, preferred_element_type=jnp.float32)
        log_sums = jnp.log(totals)
        attn_out = numer / totals
        delta = jnp.sum(do_g.astype(jnp.float32) * attn_out, axis=1, keepdims=True)
        lse_ref[qb * gb:(qb + 1) * gb, :] = log_sums
        delta_ref[qb * gb:(qb + 1) * gb, :] = delta
        dq = jnp.zeros((gb, head_dim), jnp.float32)
        for t in range(n_halo - qb):
            k_first = q_first + t * blk
            k_tile, v_tile = key_tile(k_first)
            dq_part, dk_part, dv_part = grad_tile(q_g, do_g, k_tile, v_tile, masks[t], log_sums, delta)
            dq = dq + dq_part
            dk_ref[k_first:k_first + blk, :] += dk_part
            dv_ref[k_first:k_first + blk, :] += dv_part
        dq_ref[q_first:q_first + blk, :] = jnp.concatenate(
            [dq[a * blk:(a + 1) * blk] for a in range(group)], axis=1
        ) * scale
    dkv_ref[:, :head_dim] = dk_ref[...].astype(jnp.bfloat16)
    dkv_ref[:, head_dim:] = dv_ref[...].astype(jnp.bfloat16)
    halo_raw = k_ref[0:WINDOW, :].astype(jnp.float32)
    halo_hat = halo_raw * lax.rsqrt(jnp.mean(halo_raw * halo_raw, axis=1, keepdims=True) + EPS)
    kpart_ref[...] = jnp.sum(dk_ref[...] * halo_hat, axis=0, keepdims=True).reshape(kpart_ref.shape)


def norm_grad(raw, gain, upstream):
    inverse = lax.rsqrt(jnp.mean(raw * raw, axis=1, keepdims=True) + EPS)
    scaled = raw * inverse
    weighted = upstream * gain
    inner_sum = jnp.mean(weighted * scaled, axis=1, keepdims=True)
    result = inverse * (weighted - scaled * inner_sum)
    return result, jnp.sum(upstream * scaled, axis=0, keepdims=True)


def own_kernel(qdoc_ref, kdoc_ref, q_ref, do_ref, k_ref, v_ref, lse_ref, delta_ref, dq_in_ref, raw_ref, gain_ref,
               kraw_ref, qgrad_ref, qgain_ref, kpart_ref, dk_ref, dv_ref, *, group, head_dim):
    blk = BLOCK
    n_tiles = WINDOW // blk + 1
    n_halo = WINDOW // blk
    n_q = q_ref.shape[0] // blk
    gb = group * blk
    scale = QUERY_SCALAR ** (-0.5)
    dk_ref[...] = jnp.zeros(dk_ref.shape, jnp.float32)
    dv_ref[...] = jnp.zeros(dv_ref.shape, jnp.float32)
    gain = gain_ref[...]
    gain_sum = jnp.zeros((1, head_dim), jnp.float32)
    for qb in range(n_q):
        q_first = qb * blk
        q_g = stacked(q_ref, group, head_dim, q_first)
        do_g = stacked(do_ref, group, head_dim, q_first)
        log_sums = lse_ref[qb * gb:(qb + 1) * gb, :]
        delta = delta_ref[qb * gb:(qb + 1) * gb, :]
        dq = jnp.zeros((gb, head_dim), jnp.float32)
        for t in range(max(0, n_halo - qb), n_tiles):
            live, _ = tile_mask(qdoc_ref, kdoc_ref, q_first, t, group)
            k_first = q_first + t * blk
            k_tile = k_ref[k_first:k_first + blk, :]
            v_tile = v_ref[k_first:k_first + blk, :]
            dq_part, dk_part, dv_part = grad_tile(q_g, do_g, k_tile, v_tile, live, log_sums, delta)
            dq = dq + dq_part
            own_first = k_first - WINDOW
            dk_ref[own_first:own_first + blk, :] += dk_part
            dv_ref[own_first:own_first + blk, :] += dv_part
        dq_in = dq_in_ref[q_first:q_first + blk, :]
        raw = raw_ref[q_first:q_first + blk, :].astype(jnp.float32)
        for a in range(group):
            cols = slice(a * head_dim, (a + 1) * head_dim)
            upstream = dq_in[:, cols] + dq[a * blk:(a + 1) * blk] * scale
            result, part = norm_grad(raw[:, cols], gain, upstream)
            qgrad_ref[q_first:q_first + blk, cols] = result.astype(qgrad_ref.dtype)
            gain_sum = gain_sum + part
    qgain_ref[...] = gain_sum.reshape(qgain_ref.shape)
    key_raw = kraw_ref[...].astype(jnp.float32)
    key_hat = key_raw * lax.rsqrt(jnp.mean(key_raw * key_raw, axis=1, keepdims=True) + EPS)
    kpart_ref[...] = jnp.sum(dk_ref[...] * key_hat, axis=0, keepdims=True).reshape(kpart_ref.shape)


def kv_final_kernel(dk_ref, dv_ref, back_ref, raw_ref, gain_ref, kgrad_ref, vgrad_ref, kgain_ref, *, head_dim):
    tok_rows = dk_ref.shape[0]
    lead = tok_rows - WINDOW
    back = back_ref[...].astype(jnp.float32)
    dk = dk_ref[...]
    dv = dv_ref[...]
    if lead:
        dk = jnp.concatenate([dk[:lead], dk[lead:] + back[:, :head_dim]], axis=0)
        dv = jnp.concatenate([dv[:lead], dv[lead:] + back[:, head_dim:]], axis=0)
    else:
        dk = dk + back[:, :head_dim]
        dv = dv + back[:, head_dim:]
    vgrad_ref[...] = dv.astype(vgrad_ref.dtype)
    result, part = norm_grad(raw_ref[...].astype(jnp.float32), gain_ref[...], dk)
    kgrad_ref[...] = result.astype(kgrad_ref.dtype)
    kgain_ref[...] = part.reshape(kgain_ref.shape)


def kv_final(dk_own, dv_own, back, key_raw, key_gain, key_heads, head_dim):
    tok_rows = dk_own.shape[0]
    kv_cols = key_heads * head_dim
    col_spec = pl.BlockSpec((tok_rows, head_dim), lambda h: (0, h))
    return pl.pallas_call(
        functools.partial(kv_final_kernel, head_dim=head_dim),
        grid=(key_heads,),
        in_specs=[
            col_spec,
            col_spec,
            pl.BlockSpec((WINDOW, 2 * head_dim), lambda h: (0, h)),
            col_spec,
            pl.BlockSpec((1, head_dim), lambda h: (0, 0)),
        ],
        out_specs=[col_spec, col_spec, pl.BlockSpec((1, 1, head_dim), lambda h: (h, 0, 0))],
        out_shape=[
            jax.ShapeDtypeStruct((tok_rows, kv_cols), jnp.bfloat16),
            jax.ShapeDtypeStruct((tok_rows, kv_cols), jnp.bfloat16),
            jax.ShapeDtypeStruct((key_heads, 1, head_dim), jnp.float32),
        ],
        compiler_params=pltpu.CompilerParams(dimension_semantics=("arbitrary",)),
    )(dk_own, dv_own, back, key_raw, key_gain.reshape(1, head_dim))


def attention_grads(query_norm, grad_rows, keys_all, vals_all, own_doc, all_doc, key_heads, head_dim,
                    query_raw, query_gain, key_raw, key_gain):
    tok_rows, q_cols = query_norm.shape
    key_rows = keys_all.shape[0]
    group = q_cols // (key_heads * head_dim)
    blk = BLOCK
    n_q = tok_rows // blk
    n_tiles = WINDOW // blk + 1
    gw = group * head_dim
    kv_cols = key_heads * head_dim
    stat_rows = key_heads * n_q * group * blk
    tile_flops = 2 * (group * blk) * blk * head_dim
    halo_tiles = sum(max(0, WINDOW // blk - qb) for qb in range(n_q))
    own_tiles = n_q * n_tiles - halo_tiles
    common_specs = [
        pl.BlockSpec((tok_rows, 1), lambda h: (0, 0)),
        pl.BlockSpec((1, key_rows), lambda h: (0, 0)),
        pl.BlockSpec((tok_rows, gw), lambda h: (0, h)),
        pl.BlockSpec((tok_rows, gw), lambda h: (0, h)),
        pl.BlockSpec((key_rows, head_dim), lambda h: (0, h)),
        pl.BlockSpec((key_rows, head_dim), lambda h: (0, h)),
    ]
    stat_spec = pl.BlockSpec((n_q * group * blk, 1), lambda h: (h, 0))
    dq_spec = pl.BlockSpec((tok_rows, gw), lambda h: (0, h))
    params = pltpu.CompilerParams(dimension_semantics=("arbitrary",))
    in_bytes = 2 * 2 * tok_rows * q_cols + 2 * 2 * key_rows * kv_cols
    operands = (own_doc.reshape(tok_rows, 1), all_doc.reshape(1, key_rows), query_norm, grad_rows, keys_all, vals_all)
    part_spec = pl.BlockSpec((1, 1, head_dim), lambda h: (h, 0, 0))
    part_shape = jax.ShapeDtypeStruct((key_heads, 1, head_dim), jnp.float32)
    gain_spec = pl.BlockSpec((1, head_dim), lambda h: (0, 0))
    dq_half, dkv_halo, log_sums, delta, khalo_parts = pl.pallas_call(
        functools.partial(halo_kernel, group=group, head_dim=head_dim),
        grid=(key_heads,),
        in_specs=common_specs + [gain_spec],
        out_specs=[
            dq_spec,
            pl.BlockSpec((WINDOW, 2 * head_dim), lambda h: (0, h)),
            stat_spec,
            stat_spec,
            part_spec,
        ],
        out_shape=[
            jax.ShapeDtypeStruct((tok_rows, q_cols), jnp.float32),
            jax.ShapeDtypeStruct((WINDOW, 2 * kv_cols), jnp.bfloat16),
            jax.ShapeDtypeStruct((stat_rows, 1), jnp.float32),
            jax.ShapeDtypeStruct((stat_rows, 1), jnp.float32),
            part_shape,
        ],
        scratch_shapes=[
            pltpu.VMEM((WINDOW, head_dim), jnp.float32),
            pltpu.VMEM((WINDOW, head_dim), jnp.float32),
            pltpu.VMEM((WINDOW, head_dim), jnp.bfloat16),
        ],
        compiler_params=params,
        cost_estimate=pl.CostEstimate(
            flops=key_heads * (2 * n_q * n_tiles + 5 * halo_tiles) * tile_flops,
            transcendentals=key_heads * (n_q * n_tiles + halo_tiles) * group * blk * blk,
            bytes_accessed=in_bytes + 4 * tok_rows * q_cols + 2 * 2 * WINDOW * kv_cols,
        ),
    )(*operands, key_gain.reshape(1, head_dim))
    raw_spec = pl.BlockSpec((tok_rows, gw), lambda h: (0, h))
    kraw_spec = pl.BlockSpec((tok_rows, head_dim), lambda h: (0, h))
    query_grad, qgain_parts, kown_parts, dk_own, dv_own = pl.pallas_call(
        functools.partial(own_kernel, group=group, head_dim=head_dim),
        grid=(key_heads,),
        in_specs=common_specs + [stat_spec, stat_spec, dq_spec, raw_spec, gain_spec, kraw_spec],
        out_specs=[
            raw_spec,
            part_spec,
            part_spec,
            pl.BlockSpec((tok_rows, head_dim), lambda h: (0, h)),
            pl.BlockSpec((tok_rows, head_dim), lambda h: (0, h)),
        ],
        out_shape=[
            jax.ShapeDtypeStruct((tok_rows, q_cols), jnp.bfloat16),
            part_shape,
            part_shape,
            jax.ShapeDtypeStruct((tok_rows, kv_cols), jnp.float32),
            jax.ShapeDtypeStruct((tok_rows, kv_cols), jnp.float32),
        ],
        compiler_params=params,
        cost_estimate=pl.CostEstimate(
            flops=key_heads * own_tiles * 5 * tile_flops,
            transcendentals=key_heads * own_tiles * group * blk * blk,
            bytes_accessed=in_bytes + 2 * 4 * tok_rows * q_cols + 2 * 4 * tok_rows * kv_cols,
        ),
    )(*operands, log_sums, delta, dq_half, query_raw, query_gain.reshape(1, head_dim), key_raw)
    key_part = jnp.sum(khalo_parts, axis=(0, 1)) + jnp.sum(kown_parts, axis=(0, 1))
    return query_grad, jnp.sum(qgain_parts, axis=(0, 1)), key_part, dkv_halo, dk_own, dv_own


def per_device(query_raw, key_raw, value_proj, query_gain, key_gain, out_grad, doc_lengths):
    tok_rows = query_raw.shape[0]
    head_dim = query_gain.shape[0]
    query_heads = query_raw.shape[1] // head_dim
    key_heads = key_raw.shape[1] // head_dim
    first_pos = lax.axis_index("ctx") * tok_rows
    doc_ends = jnp.cumsum(doc_lengths)
    own_pos = first_pos + jnp.arange(tok_rows, dtype=jnp.int32)
    own_doc = doc_index(own_pos, doc_ends)
    halo_raw = first_pos - WINDOW + jnp.arange(WINDOW, dtype=jnp.int32)
    halo_doc = jnp.where(halo_raw >= 0, doc_index(halo_raw, doc_ends), -1)
    query_hat, query_inv = norm_rows(query_raw, query_heads)
    query_norm = (query_hat * query_gain).astype(jnp.bfloat16).reshape(tok_rows, query_heads * head_dim)
    key_hat, key_inv = norm_rows(key_raw, key_heads)
    key_norm = (key_hat * key_gain).astype(jnp.bfloat16).reshape(tok_rows, key_heads * head_dim)
    halo_keys, halo_vals = shifted((key_raw[tok_rows - WINDOW:], value_proj[tok_rows - WINDOW:]), "ctx", 1)
    keys_all = jnp.concatenate([halo_keys, key_norm], axis=0)
    vals_all = jnp.concatenate([halo_vals, value_proj], axis=0)
    all_doc = jnp.concatenate([halo_doc, own_doc])
    query_grad, query_part, key_part, dkv_halo, dk_own, dv_own = attention_grads(
        query_norm, out_grad, keys_all, vals_all, own_doc, all_doc, key_heads, head_dim, query_raw, query_gain,
        key_raw, key_gain,
    )
    gain_grads = butterfly_sum(jnp.stack([query_part, key_part]), ("head", "ctx"))
    back = shifted(dkv_halo, "ctx", -1)
    key_grad, value_grad, _ = kv_final(dk_own, dv_own, back, key_raw, key_gain, key_heads, head_dim)
    return (query_grad, key_grad, value_grad, gain_grads[0], gain_grads[1])


def solution(mesh):
    return jax.shard_map(
        per_device,
        mesh=mesh,
        in_specs=(
            P("ctx", "head"),
            P("ctx", "head"),
            P("ctx", "head"),
            P(),
            P(),
            P("ctx", "head"),
            P(),
        ),
        out_specs=(P("ctx", "head"), P("ctx", "head"), P("ctx", "head"), P(), P()),
        check_vma=False,
    )
```

```python
import functools
import math

import jax
import jax.numpy as jnp
from jax import lax
from jax.experimental import pallas as pl
from jax.experimental.pallas import tpu as pltpu
from jax.sharding import PartitionSpec as P

WINDOW = 1024
QUERY_SCALAR = 168


EPS = 1e-06
BLOCK = 256


def shifted(value, axis, steps):
    count = lax.axis_size(axis)
    leading, last = (max(0, -steps), min(count, count - steps))
    return lax.ppermute(value, axis, [(source, source + steps) for source in range(leading, last)])


def xor_tree(values):
    while len(values) > 1:
        values = [values[i] + values[i + 1] for i in range(0, len(values), 2)]
    return values[0]


def butterfly_sum(value, axes):
    for axis in axes:
        count = lax.axis_size(axis)
        if count & (count - 1):
            value = lax.psum(value, axis)
            continue
        bits = count.bit_length() - 1
        low = 0
        while low < bits:
            width = 1
            shifted_parts = [value]
            for mask in range(1, 1 << width):
                pairs = [(source, source ^ (mask << low)) for source in range(count)]
                shifted_parts.append(lax.ppermute(value, axis, pairs))
            value = xor_tree(shifted_parts)
            low += width
    return value


def norm_rows(raw_rows, head_count):
    values = raw_rows.astype(jnp.float32).reshape(raw_rows.shape[0], head_count, -1)
    inverse = lax.rsqrt(jnp.mean(values * values, axis=-1, keepdims=True) + EPS)
    return (values * inverse, inverse)


def norm_back(raw_rows, gain_vec, head_count, upstream):
    scaled, inverse = norm_rows(raw_rows, head_count)
    incoming = upstream.reshape(scaled.shape)
    weighted = incoming * gain_vec
    inner_sum = jnp.mean(weighted * scaled, axis=-1, keepdims=True)
    result = inverse * (weighted - scaled * inner_sum)
    return (result.reshape(raw_rows.shape), jnp.sum(incoming * scaled, axis=(0, 1)))


def doc_index(positions, doc_ends):
    return jnp.sum((positions[:, None] >= doc_ends[None, :]).astype(jnp.int32), axis=1)


def tile_mask(qdoc_ref, kdoc_ref, q_first, t, group):
    blk = BLOCK
    n_tiles = WINDOW // blk + 1
    rows = lax.broadcasted_iota(jnp.int32, (blk, blk), 0)
    cols = lax.broadcasted_iota(jnp.int32, (blk, blk), 1)
    k_first = q_first + t * blk
    live = qdoc_ref[q_first:q_first + blk, :] == kdoc_ref[:, k_first:k_first + blk]
    if t == 0:
        live = live & (cols > rows)
    if t == n_tiles - 1:
        live = live & (cols + t * blk <= rows + WINDOW)
    return jnp.concatenate([live] * group, axis=0), k_first


def stacked(ref, group, head_dim, first):
    blk = BLOCK
    return jnp.concatenate(
        [ref[first:first + blk, a * head_dim:(a + 1) * head_dim] for a in range(group)], axis=0
    )


def grad_tile(q_g, do_g, k_tile, v_tile, live, log_sums, delta):
    scale = QUERY_SCALAR ** (-0.5)
    scores = lax.dot_general(q_g, k_tile, (((1,), (1,)), ((), ())), preferred_element_type=jnp.float32) * scale
    weights = jnp.where(live, jnp.exp(scores - log_sums), 0.0)
    d_weights = lax.dot_general(do_g, v_tile, (((1,), (1,)), ((), ())), preferred_element_type=jnp.float32)
    d_scores = (weights * (d_weights - delta)).astype(jnp.bfloat16)
    dq_part = jnp.dot(d_scores, k_tile, preferred_element_type=jnp.float32)
    dk_part = lax.dot_general(d_scores, q_g, (((0,), (0,)), ((), ())), preferred_element_type=jnp.float32)
    dv_part = lax.dot_general(
        weights.astype(jnp.bfloat16), do_g, (((0,), (0,)), ((), ())), preferred_element_type=jnp.float32
    )
    return dq_part, dk_part * scale, dv_part


def halo_kernel(qdoc_ref, kdoc_ref, q_ref, do_ref, hk_ref, hv_ref, k_ref, v_ref, kgain_ref, *refs,
                group, head_dim, n_alias):
    dq_ref, dkv_ref, lse_ref, delta_ref, kpart_ref, dk_ref, dv_ref, kn_ref = refs[n_alias:]
    blk = BLOCK
    n_tiles = WINDOW // blk + 1
    n_halo = WINDOW // blk
    n_q = q_ref.shape[0] // blk
    gb = group * blk
    scale = QUERY_SCALAR ** (-0.5)
    dk_ref[...] = jnp.zeros(dk_ref.shape, jnp.float32)
    dv_ref[...] = jnp.zeros(dv_ref.shape, jnp.float32)
    halo_raw = hk_ref[...].astype(jnp.float32)
    halo_inv = lax.rsqrt(jnp.mean(halo_raw * halo_raw, axis=1, keepdims=True) + EPS)
    kn_ref[...] = (halo_raw * halo_inv * kgain_ref[...]).astype(jnp.bfloat16)

    def key_tile(k_first):
        if k_first < WINDOW:
            return kn_ref[k_first:k_first + blk, :], hv_ref[k_first:k_first + blk, :]
        own_first = k_first - WINDOW
        return k_ref[own_first:own_first + blk, :], v_ref[own_first:own_first + blk, :]

    for qb in range(n_q):
        q_first = qb * blk
        q_g = stacked(q_ref, group, head_dim, q_first)
        do_g = stacked(do_ref, group, head_dim, q_first)
        masks = [tile_mask(qdoc_ref, kdoc_ref, q_first, t, group)[0] for t in range(n_tiles)]
        totals = jnp.zeros((gb, 1), jnp.float32)
        numer = jnp.zeros((gb, head_dim), jnp.float32)
        for t in range(n_tiles):
            k_first = q_first + t * blk
            k_tile, v_tile = key_tile(k_first)
            scores = lax.dot_general(
                q_g, k_tile, (((1,), (1,)), ((), ())), preferred_element_type=jnp.float32
            ) * scale
            exp_s = jnp.where(masks[t], jnp.exp(scores), 0.0)
            totals = totals + jnp.sum(exp_s, axis=1, keepdims=True)
            numer = numer + jnp.dot(exp_s.astype(jnp.bfloat16), v_tile, preferred_element_type=jnp.float32)
        log_sums = jnp.log(totals)
        attn_out = numer / totals
        delta = jnp.sum(do_g.astype(jnp.float32) * attn_out, axis=1, keepdims=True)
        lse_ref[qb * gb:(qb + 1) * gb, :] = log_sums
        delta_ref[qb * gb:(qb + 1) * gb, :] = delta
        dq = jnp.zeros((gb, head_dim), jnp.float32)
        for t in range(n_halo - qb):
            k_first = q_first + t * blk
            k_tile, v_tile = key_tile(k_first)
            dq_part, dk_part, dv_part = grad_tile(q_g, do_g, k_tile, v_tile, masks[t], log_sums, delta)
            dq = dq + dq_part
            dk_ref[k_first:k_first + blk, :] += dk_part
            dv_ref[k_first:k_first + blk, :] += dv_part
        dq_ref[q_first:q_first + blk, :] = jnp.concatenate(
            [dq[a * blk:(a + 1) * blk] for a in range(group)], axis=1
        ) * scale
    dkv_ref[:, :head_dim] = dk_ref[...].astype(jnp.bfloat16)
    dkv_ref[:, head_dim:] = dv_ref[...].astype(jnp.bfloat16)
    halo_hat = halo_raw * halo_inv
    kpart_ref[...] = jnp.sum(dk_ref[...] * halo_hat, axis=0, keepdims=True).reshape(kpart_ref.shape)


def norm_grad(raw, gain, upstream):
    inverse = lax.rsqrt(jnp.mean(raw * raw, axis=1, keepdims=True) + EPS)
    scaled = raw * inverse
    weighted = upstream * gain
    inner_sum = jnp.mean(weighted * scaled, axis=1, keepdims=True)
    result = inverse * (weighted - scaled * inner_sum)
    return result, jnp.sum(upstream * scaled, axis=0, keepdims=True)


def own_kernel(qdoc_ref, kdoc_ref, q_ref, do_ref, k_ref, v_ref, lse_ref, delta_ref, dq_in_ref, raw_ref, gain_ref,
               kraw_ref, qgrad_ref, qgain_ref, kpart_ref, dk_ref, dv_ref, *, group, head_dim):
    blk = BLOCK
    n_tiles = WINDOW // blk + 1
    n_halo = WINDOW // blk
    n_q = q_ref.shape[0] // blk
    gb = group * blk
    scale = QUERY_SCALAR ** (-0.5)
    dk_ref[...] = jnp.zeros(dk_ref.shape, jnp.float32)
    dv_ref[...] = jnp.zeros(dv_ref.shape, jnp.float32)
    gain = gain_ref[...]
    gain_sum = jnp.zeros((1, head_dim), jnp.float32)
    for qb in range(n_q):
        q_first = qb * blk
        q_g = stacked(q_ref, group, head_dim, q_first)
        do_g = stacked(do_ref, group, head_dim, q_first)
        log_sums = lse_ref[qb * gb:(qb + 1) * gb, :]
        delta = delta_ref[qb * gb:(qb + 1) * gb, :]
        dq = jnp.zeros((gb, head_dim), jnp.float32)
        for t in range(max(0, n_halo - qb), n_tiles):
            live, _ = tile_mask(qdoc_ref, kdoc_ref, q_first, t, group)
            k_first = q_first + t * blk
            own_first = k_first - WINDOW
            k_tile = k_ref[own_first:own_first + blk, :]
            v_tile = v_ref[own_first:own_first + blk, :]
            dq_part, dk_part, dv_part = grad_tile(q_g, do_g, k_tile, v_tile, live, log_sums, delta)
            dq = dq + dq_part
            dk_ref[own_first:own_first + blk, :] += dk_part
            dv_ref[own_first:own_first + blk, :] += dv_part
        dq_in = dq_in_ref[q_first:q_first + blk, :]
        raw = raw_ref[q_first:q_first + blk, :].astype(jnp.float32)
        for a in range(group):
            cols = slice(a * head_dim, (a + 1) * head_dim)
            upstream = dq_in[:, cols] + dq[a * blk:(a + 1) * blk] * scale
            result, part = norm_grad(raw[:, cols], gain, upstream)
            qgrad_ref[q_first:q_first + blk, cols] = result.astype(qgrad_ref.dtype)
            gain_sum = gain_sum + part
    qgain_ref[...] = gain_sum.reshape(qgain_ref.shape)
    key_raw = kraw_ref[...].astype(jnp.float32)
    key_hat = key_raw * lax.rsqrt(jnp.mean(key_raw * key_raw, axis=1, keepdims=True) + EPS)
    kpart_ref[...] = jnp.sum(dk_ref[...] * key_hat, axis=0, keepdims=True).reshape(kpart_ref.shape)


def kv_final_kernel(dk_ref, dv_ref, back_ref, raw_ref, gain_ref, kgrad_ref, vgrad_ref, kgain_ref, *, head_dim):
    tok_rows = dk_ref.shape[0]
    lead = tok_rows - WINDOW
    back = back_ref[...].astype(jnp.float32)
    dk = dk_ref[...]
    dv = dv_ref[...]
    if lead:
        dk = jnp.concatenate([dk[:lead], dk[lead:] + back[:, :head_dim]], axis=0)
        dv = jnp.concatenate([dv[:lead], dv[lead:] + back[:, head_dim:]], axis=0)
    else:
        dk = dk + back[:, :head_dim]
        dv = dv + back[:, head_dim:]
    vgrad_ref[...] = dv.astype(vgrad_ref.dtype)
    result, part = norm_grad(raw_ref[...].astype(jnp.float32), gain_ref[...], dk)
    kgrad_ref[...] = result.astype(kgrad_ref.dtype)
    kgain_ref[...] = part.reshape(kgain_ref.shape)


def kv_final(dk_own, dv_own, back, key_raw, key_gain, key_heads, head_dim):
    tok_rows = dk_own.shape[0]
    kv_cols = key_heads * head_dim
    col_spec = pl.BlockSpec((tok_rows, head_dim), lambda h: (0, h))
    return pl.pallas_call(
        functools.partial(kv_final_kernel, head_dim=head_dim),
        grid=(key_heads,),
        in_specs=[
            col_spec,
            col_spec,
            pl.BlockSpec((WINDOW, 2 * head_dim), lambda h: (0, h)),
            col_spec,
            pl.BlockSpec((1, head_dim), lambda h: (0, 0)),
        ],
        out_specs=[col_spec, col_spec, pl.BlockSpec((1, 1, head_dim), lambda h: (h, 0, 0))],
        out_shape=[
            jax.ShapeDtypeStruct((tok_rows, kv_cols), jnp.bfloat16),
            jax.ShapeDtypeStruct((tok_rows, kv_cols), jnp.bfloat16),
            jax.ShapeDtypeStruct((key_heads, 1, head_dim), jnp.float32),
        ],
        compiler_params=pltpu.CompilerParams(dimension_semantics=("arbitrary",)),
    )(dk_own, dv_own, back, key_raw, key_gain.reshape(1, head_dim))


def attention_grads(query_norm, grad_rows, halo_pieces, key_norm, value_proj, own_doc, all_doc, key_heads,
                    head_dim, query_raw, query_gain, key_raw, key_gain):
    tok_rows, q_cols = query_norm.shape
    key_rows = WINDOW + tok_rows
    group = q_cols // (key_heads * head_dim)
    blk = BLOCK
    n_q = tok_rows // blk
    n_tiles = WINDOW // blk + 1
    gw = group * head_dim
    kv_cols = key_heads * head_dim
    stat_rows = key_heads * n_q * group * blk
    tile_flops = 2 * (group * blk) * blk * head_dim
    halo_tiles = sum(max(0, WINDOW // blk - qb) for qb in range(n_q))
    own_tiles = n_q * n_tiles - halo_tiles
    n_piece = key_heads // len(halo_pieces)
    params = pltpu.CompilerParams(dimension_semantics=("arbitrary",))
    gain_spec = pl.BlockSpec((1, head_dim), lambda h: (0, 0))
    doc_specs = [pl.BlockSpec((tok_rows, 1), lambda h: (0, 0)), pl.BlockSpec((1, key_rows), lambda h: (0, 0))]
    qdoc, kdoc = own_doc.reshape(tok_rows, 1), all_doc.reshape(1, key_rows)
    buffers = ()
    kparts = []
    for piece, (hk, hv) in enumerate(halo_pieces):
        h0 = piece * n_piece
        qcol = pl.BlockSpec((tok_rows, gw), lambda h, h0=h0: (0, h + h0))
        kcol = pl.BlockSpec((tok_rows, head_dim), lambda h, h0=h0: (0, h + h0))
        hcol = pl.BlockSpec((WINDOW, head_dim), lambda h: (0, h))
        stat = pl.BlockSpec((n_q * group * blk, 1), lambda h, h0=h0: (h + h0, 0))
        outs = pl.pallas_call(
            functools.partial(halo_kernel, group=group, head_dim=head_dim, n_alias=len(buffers)),
            grid=(n_piece,),
            in_specs=doc_specs + [qcol, qcol, hcol, hcol, kcol, kcol, gain_spec]
            + [pl.BlockSpec(memory_space=pl.ANY)] * len(buffers),
            out_specs=[
                qcol,
                pl.BlockSpec((WINDOW, 2 * head_dim), lambda h, h0=h0: (0, h + h0)),
                stat,
                stat,
                pl.BlockSpec((1, 1, head_dim), lambda h: (h, 0, 0)),
            ],
            out_shape=[
                jax.ShapeDtypeStruct((tok_rows, q_cols), jnp.float32),
                jax.ShapeDtypeStruct((WINDOW, 2 * kv_cols), jnp.bfloat16),
                jax.ShapeDtypeStruct((stat_rows, 1), jnp.float32),
                jax.ShapeDtypeStruct((stat_rows, 1), jnp.float32),
                jax.ShapeDtypeStruct((n_piece, 1, head_dim), jnp.float32),
            ],
            scratch_shapes=[
                pltpu.VMEM((WINDOW, head_dim), jnp.float32),
                pltpu.VMEM((WINDOW, head_dim), jnp.float32),
                pltpu.VMEM((WINDOW, head_dim), jnp.bfloat16),
            ],
            input_output_aliases={9 + i: i for i in range(len(buffers))},
            compiler_params=params,
            cost_estimate=pl.CostEstimate(
                flops=n_piece * (2 * n_q * n_tiles + 5 * halo_tiles) * tile_flops,
                transcendentals=n_piece * (n_q * n_tiles + halo_tiles) * group * blk * blk,
                bytes_accessed=n_piece * (2 * 2 * tok_rows * gw + 2 * 2 * key_rows * head_dim
                                          + 4 * tok_rows * gw + 2 * 2 * WINDOW * head_dim),
            ),
        )(qdoc, kdoc, query_norm, grad_rows, hk, hv, key_norm, value_proj, key_gain.reshape(1, head_dim), *buffers)
        buffers = tuple(outs[:4])
        kparts.append(outs[4])
    dq_half, dkv_halo, log_sums, delta = buffers
    qcol = pl.BlockSpec((tok_rows, gw), lambda h: (0, h))
    kcol = pl.BlockSpec((tok_rows, head_dim), lambda h: (0, h))
    stat = pl.BlockSpec((n_q * group * blk, 1), lambda h: (h, 0))
    part_spec = pl.BlockSpec((1, 1, head_dim), lambda h: (h, 0, 0))
    part_shape = jax.ShapeDtypeStruct((key_heads, 1, head_dim), jnp.float32)
    query_grad, qgain_parts, kown_parts, dk_own, dv_own = pl.pallas_call(
        functools.partial(own_kernel, group=group, head_dim=head_dim),
        grid=(key_heads,),
        in_specs=doc_specs + [qcol, qcol, kcol, kcol, stat, stat, qcol, qcol, gain_spec, kcol],
        out_specs=[qcol, part_spec, part_spec, kcol, kcol],
        out_shape=[
            jax.ShapeDtypeStruct((tok_rows, q_cols), jnp.bfloat16),
            part_shape,
            part_shape,
            jax.ShapeDtypeStruct((tok_rows, kv_cols), jnp.float32),
            jax.ShapeDtypeStruct((tok_rows, kv_cols), jnp.float32),
        ],
        compiler_params=params,
        cost_estimate=pl.CostEstimate(
            flops=key_heads * own_tiles * 5 * tile_flops,
            transcendentals=key_heads * own_tiles * group * blk * blk,
            bytes_accessed=2 * 2 * tok_rows * q_cols + 2 * 2 * tok_rows * kv_cols + 2 * 4 * tok_rows * q_cols
            + 2 * 4 * tok_rows * kv_cols,
        ),
    )(qdoc, kdoc, query_norm, grad_rows, key_norm, value_proj, log_sums, delta, dq_half, query_raw,
      query_gain.reshape(1, head_dim), key_raw)
    key_part = jnp.sum(kown_parts, axis=(0, 1))
    for part in kparts:
        key_part = key_part + jnp.sum(part, axis=(0, 1))
    return query_grad, jnp.sum(qgain_parts, axis=(0, 1)), key_part, dkv_halo, dk_own, dv_own


def per_device(query_raw, key_raw, value_proj, query_gain, key_gain, out_grad, doc_lengths):
    tok_rows = query_raw.shape[0]
    head_dim = query_gain.shape[0]
    query_heads = query_raw.shape[1] // head_dim
    key_heads = key_raw.shape[1] // head_dim
    first_pos = lax.axis_index("ctx") * tok_rows
    doc_ends = jnp.cumsum(doc_lengths)
    own_pos = first_pos + jnp.arange(tok_rows, dtype=jnp.int32)
    own_doc = doc_index(own_pos, doc_ends)
    halo_raw = first_pos - WINDOW + jnp.arange(WINDOW, dtype=jnp.int32)
    halo_doc = jnp.where(halo_raw >= 0, doc_index(halo_raw, doc_ends), -1)
    query_hat, query_inv = norm_rows(query_raw, query_heads)
    query_norm = (query_hat * query_gain).astype(jnp.bfloat16).reshape(tok_rows, query_heads * head_dim)
    key_hat, key_inv = norm_rows(key_raw, key_heads)
    key_norm = (key_hat * key_gain).astype(jnp.bfloat16).reshape(tok_rows, key_heads * head_dim)
    n_pieces = 2 if key_heads % 2 == 0 else 1
    width = key_heads * head_dim // n_pieces
    halo_pieces = []
    for piece in range(n_pieces):
        cols = slice(piece * width, (piece + 1) * width)
        send = (key_raw[tok_rows - WINDOW:, cols], value_proj[tok_rows - WINDOW:, cols])
        if halo_pieces:
            send = lax.optimization_barrier((send, halo_pieces[-1][0]))[0]
        halo_pieces.append(shifted(send, "ctx", 1))
    all_doc = jnp.concatenate([halo_doc, own_doc])
    query_grad, query_part, key_part, dkv_halo, dk_own, dv_own = attention_grads(
        query_norm, out_grad, halo_pieces, key_norm, value_proj, own_doc, all_doc, key_heads, head_dim,
        query_raw, query_gain, key_raw, key_gain,
    )
    gain_grads = butterfly_sum(jnp.stack([query_part, key_part]), ("head", "ctx"))
    back = shifted(dkv_halo, "ctx", -1)
    key_grad, value_grad, _ = kv_final(dk_own, dv_own, back, key_raw, key_gain, key_heads, head_dim)
    return (query_grad, key_grad, value_grad, gain_grads[0], gain_grads[1])


def solution(mesh):
    return jax.shard_map(
        per_device,
        mesh=mesh,
        in_specs=(
            P("ctx", "head"),
            P("ctx", "head"),
            P("ctx", "head"),
            P(),
            P(),
            P("ctx", "head"),
            P(),
        ),
        out_specs=(P("ctx", "head"), P("ctx", "head"), P("ctx", "head"), P(), P()),
        check_vma=False,
    )
```

```python
import functools
import math

import jax
import jax.numpy as jnp
from jax import lax
from jax.experimental import pallas as pl
from jax.experimental.pallas import tpu as pltpu
from jax.sharding import PartitionSpec as P

WINDOW = 1024
QUERY_SCALAR = 168


EPS = 1e-06
BLOCK = 256


def shifted(value, axis, steps):
    count = lax.axis_size(axis)
    leading, last = (max(0, -steps), min(count, count - steps))
    return lax.ppermute(value, axis, [(source, source + steps) for source in range(leading, last)])


def xor_tree(values):
    while len(values) > 1:
        values = [values[i] + values[i + 1] for i in range(0, len(values), 2)]
    return values[0]


def butterfly_sum(value, axes):
    for axis in axes:
        count = lax.axis_size(axis)
        if count & (count - 1):
            value = lax.psum(value, axis)
            continue
        bits = count.bit_length() - 1
        low = 0
        while low < bits:
            width = 1
            shifted_parts = [value]
            for mask in range(1, 1 << width):
                pairs = [(source, source ^ (mask << low)) for source in range(count)]
                shifted_parts.append(lax.ppermute(value, axis, pairs))
            value = xor_tree(shifted_parts)
            low += width
    return value


def norm_rows(raw_rows, head_count):
    values = raw_rows.astype(jnp.float32).reshape(raw_rows.shape[0], head_count, -1)
    inverse = lax.rsqrt(jnp.mean(values * values, axis=-1, keepdims=True) + EPS)
    return (values * inverse, inverse)


def norm_back(raw_rows, gain_vec, head_count, upstream):
    scaled, inverse = norm_rows(raw_rows, head_count)
    incoming = upstream.reshape(scaled.shape)
    weighted = incoming * gain_vec
    inner_sum = jnp.mean(weighted * scaled, axis=-1, keepdims=True)
    result = inverse * (weighted - scaled * inner_sum)
    return (result.reshape(raw_rows.shape), jnp.sum(incoming * scaled, axis=(0, 1)))


def doc_index(positions, doc_ends):
    return jnp.sum((positions[:, None] >= doc_ends[None, :]).astype(jnp.int32), axis=1)


def tile_mask(qdoc_ref, kdoc_ref, q_first, t, group):
    blk = BLOCK
    n_tiles = WINDOW // blk + 1
    rows = lax.broadcasted_iota(jnp.int32, (blk, blk), 0)
    cols = lax.broadcasted_iota(jnp.int32, (blk, blk), 1)
    k_first = q_first + t * blk
    live = qdoc_ref[q_first:q_first + blk, :] == kdoc_ref[:, k_first:k_first + blk]
    if t == 0:
        live = live & (cols > rows)
    if t == n_tiles - 1:
        live = live & (cols + t * blk <= rows + WINDOW)
    return jnp.concatenate([live] * group, axis=0), k_first


def normed_rows(raw, gain):
    inverse = lax.rsqrt(jnp.mean(raw * raw, axis=1, keepdims=True) + EPS)
    return (raw * inverse * gain).astype(jnp.bfloat16)


def normed_stack(ref, gain, group, head_dim, first):
    blk = BLOCK
    return jnp.concatenate(
        [normed_rows(ref[first:first + blk, a * head_dim:(a + 1) * head_dim].astype(jnp.float32), gain)
         for a in range(group)],
        axis=0,
    )


def stacked(ref, group, head_dim, first):
    blk = BLOCK
    return jnp.concatenate(
        [ref[first:first + blk, a * head_dim:(a + 1) * head_dim] for a in range(group)], axis=0
    )


def grad_tile(q_g, do_g, k_tile, v_tile, live, log_sums, delta):
    scale = QUERY_SCALAR ** (-0.5)
    scores = lax.dot_general(q_g, k_tile, (((1,), (1,)), ((), ())), preferred_element_type=jnp.float32) * scale
    weights = jnp.where(live, jnp.exp(scores - log_sums), 0.0)
    d_weights = lax.dot_general(do_g, v_tile, (((1,), (1,)), ((), ())), preferred_element_type=jnp.float32)
    d_scores = (weights * (d_weights - delta)).astype(jnp.bfloat16)
    dq_part = jnp.dot(d_scores, k_tile, preferred_element_type=jnp.float32)
    dk_part = lax.dot_general(d_scores, q_g, (((0,), (0,)), ((), ())), preferred_element_type=jnp.float32)
    dv_part = lax.dot_general(
        weights.astype(jnp.bfloat16), do_g, (((0,), (0,)), ((), ())), preferred_element_type=jnp.float32
    )
    return dq_part, dk_part * scale, dv_part


def halo_kernel(qdoc_ref, kdoc_ref, q_ref, do_ref, hk_ref, hv_ref, kraw_ref, v_ref, kgain_ref, qgain_ref, *refs,
                group, head_dim, n_alias):
    dq_ref, dkv_ref, lse_ref, delta_ref, kpart_ref, dk_ref, dv_ref, kn_ref, k_ref = refs[n_alias:]
    blk = BLOCK
    n_tiles = WINDOW // blk + 1
    n_halo = WINDOW // blk
    n_q = q_ref.shape[0] // blk
    gb = group * blk
    scale = QUERY_SCALAR ** (-0.5)
    dk_ref[...] = jnp.zeros(dk_ref.shape, jnp.float32)
    dv_ref[...] = jnp.zeros(dv_ref.shape, jnp.float32)
    halo_raw = hk_ref[...].astype(jnp.float32)
    halo_inv = lax.rsqrt(jnp.mean(halo_raw * halo_raw, axis=1, keepdims=True) + EPS)
    kn_ref[...] = (halo_raw * halo_inv * kgain_ref[...]).astype(jnp.bfloat16)
    k_ref[...] = normed_rows(kraw_ref[...].astype(jnp.float32), kgain_ref[...])
    qgain = qgain_ref[...]

    def key_tile(k_first):
        if k_first < WINDOW:
            return kn_ref[k_first:k_first + blk, :], hv_ref[k_first:k_first + blk, :]
        own_first = k_first - WINDOW
        return k_ref[own_first:own_first + blk, :], v_ref[own_first:own_first + blk, :]

    for qb in range(n_q):
        q_first = qb * blk
        q_g = normed_stack(q_ref, qgain, group, head_dim, q_first)
        do_g = stacked(do_ref, group, head_dim, q_first)
        masks = [tile_mask(qdoc_ref, kdoc_ref, q_first, t, group)[0] for t in range(n_tiles)]
        totals = jnp.zeros((gb, 1), jnp.float32)
        numer = jnp.zeros((gb, head_dim), jnp.float32)
        for t in range(n_tiles):
            k_first = q_first + t * blk
            k_tile, v_tile = key_tile(k_first)
            scores = lax.dot_general(
                q_g, k_tile, (((1,), (1,)), ((), ())), preferred_element_type=jnp.float32
            ) * scale
            exp_s = jnp.where(masks[t], jnp.exp(scores), 0.0)
            totals = totals + jnp.sum(exp_s, axis=1, keepdims=True)
            numer = numer + jnp.dot(exp_s.astype(jnp.bfloat16), v_tile, preferred_element_type=jnp.float32)
        log_sums = jnp.log(totals)
        attn_out = numer / totals
        delta = jnp.sum(do_g.astype(jnp.float32) * attn_out, axis=1, keepdims=True)
        lse_ref[qb * gb:(qb + 1) * gb, :] = log_sums
        delta_ref[qb * gb:(qb + 1) * gb, :] = delta
        dq = jnp.zeros((gb, head_dim), jnp.float32)
        for t in range(n_halo - qb):
            k_first = q_first + t * blk
            k_tile, v_tile = key_tile(k_first)
            dq_part, dk_part, dv_part = grad_tile(q_g, do_g, k_tile, v_tile, masks[t], log_sums, delta)
            dq = dq + dq_part
            dk_ref[k_first:k_first + blk, :] += dk_part
            dv_ref[k_first:k_first + blk, :] += dv_part
        dq_ref[q_first:q_first + blk, :] = jnp.concatenate(
            [dq[a * blk:(a + 1) * blk] for a in range(group)], axis=1
        ) * scale
    dkv_ref[:, :head_dim] = dk_ref[...].astype(jnp.bfloat16)
    dkv_ref[:, head_dim:] = dv_ref[...].astype(jnp.bfloat16)
    halo_hat = halo_raw * halo_inv
    kpart_ref[...] = jnp.sum(dk_ref[...] * halo_hat, axis=0, keepdims=True).reshape(kpart_ref.shape)


def norm_grad(raw, gain, upstream):
    inverse = lax.rsqrt(jnp.mean(raw * raw, axis=1, keepdims=True) + EPS)
    scaled = raw * inverse
    weighted = upstream * gain
    inner_sum = jnp.mean(weighted * scaled, axis=1, keepdims=True)
    result = inverse * (weighted - scaled * inner_sum)
    return result, jnp.sum(upstream * scaled, axis=0, keepdims=True)


def own_kernel(qdoc_ref, kdoc_ref, do_ref, v_ref, lse_ref, delta_ref, dq_in_ref, raw_ref, gain_ref,
               kraw_ref, kgain_ref, qgrad_ref, qgain_ref, kpart_ref, dk_ref, dv_ref, k_ref, *, group, head_dim):
    q_ref = raw_ref
    blk = BLOCK
    n_tiles = WINDOW // blk + 1
    n_halo = WINDOW // blk
    n_q = q_ref.shape[0] // blk
    gb = group * blk
    scale = QUERY_SCALAR ** (-0.5)
    dk_ref[...] = jnp.zeros(dk_ref.shape, jnp.float32)
    dv_ref[...] = jnp.zeros(dv_ref.shape, jnp.float32)
    gain = gain_ref[...]
    k_ref[...] = normed_rows(kraw_ref[...].astype(jnp.float32), kgain_ref[...])
    gain_sum = jnp.zeros((1, head_dim), jnp.float32)
    for qb in range(n_q):
        q_first = qb * blk
        q_g = normed_stack(q_ref, gain, group, head_dim, q_first)
        do_g = stacked(do_ref, group, head_dim, q_first)
        log_sums = lse_ref[qb * gb:(qb + 1) * gb, :]
        delta = delta_ref[qb * gb:(qb + 1) * gb, :]
        dq = jnp.zeros((gb, head_dim), jnp.float32)
        for t in range(max(0, n_halo - qb), n_tiles):
            live, _ = tile_mask(qdoc_ref, kdoc_ref, q_first, t, group)
            k_first = q_first + t * blk
            own_first = k_first - WINDOW
            k_tile = k_ref[own_first:own_first + blk, :]
            v_tile = v_ref[own_first:own_first + blk, :]
            dq_part, dk_part, dv_part = grad_tile(q_g, do_g, k_tile, v_tile, live, log_sums, delta)
            dq = dq + dq_part
            dk_ref[own_first:own_first + blk, :] += dk_part
            dv_ref[own_first:own_first + blk, :] += dv_part
        dq_in = dq_in_ref[q_first:q_first + blk, :]
        raw = raw_ref[q_first:q_first + blk, :].astype(jnp.float32)
        for a in range(group):
            cols = slice(a * head_dim, (a + 1) * head_dim)
            upstream = dq_in[:, cols] + dq[a * blk:(a + 1) * blk] * scale
            result, part = norm_grad(raw[:, cols], gain, upstream)
            qgrad_ref[q_first:q_first + blk, cols] = result.astype(qgrad_ref.dtype)
            gain_sum = gain_sum + part
    qgain_ref[...] = gain_sum.reshape(qgain_ref.shape)
    key_raw = kraw_ref[...].astype(jnp.float32)
    key_hat = key_raw * lax.rsqrt(jnp.mean(key_raw * key_raw, axis=1, keepdims=True) + EPS)
    kpart_ref[...] = jnp.sum(dk_ref[...] * key_hat, axis=0, keepdims=True).reshape(kpart_ref.shape)


def kv_final_kernel(dk_ref, dv_ref, back_ref, raw_ref, gain_ref, kgrad_ref, vgrad_ref, kgain_ref, *, head_dim):
    tok_rows = dk_ref.shape[0]
    lead = tok_rows - WINDOW
    back = back_ref[...].astype(jnp.float32)
    dk = dk_ref[...]
    dv = dv_ref[...]
    if lead:
        dk = jnp.concatenate([dk[:lead], dk[lead:] + back[:, :head_dim]], axis=0)
        dv = jnp.concatenate([dv[:lead], dv[lead:] + back[:, head_dim:]], axis=0)
    else:
        dk = dk + back[:, :head_dim]
        dv = dv + back[:, head_dim:]
    vgrad_ref[...] = dv.astype(vgrad_ref.dtype)
    result, part = norm_grad(raw_ref[...].astype(jnp.float32), gain_ref[...], dk)
    kgrad_ref[...] = result.astype(kgrad_ref.dtype)
    kgain_ref[...] = part.reshape(kgain_ref.shape)


def kv_final(dk_own, dv_own, back, key_raw, key_gain, key_heads, head_dim):
    tok_rows = dk_own.shape[0]
    kv_cols = key_heads * head_dim
    col_spec = pl.BlockSpec((tok_rows, head_dim), lambda h: (0, h))
    return pl.pallas_call(
        functools.partial(kv_final_kernel, head_dim=head_dim),
        grid=(key_heads,),
        in_specs=[
            col_spec,
            col_spec,
            pl.BlockSpec((WINDOW, 2 * head_dim), lambda h: (0, h)),
            col_spec,
            pl.BlockSpec((1, head_dim), lambda h: (0, 0)),
        ],
        out_specs=[col_spec, col_spec, pl.BlockSpec((1, 1, head_dim), lambda h: (h, 0, 0))],
        out_shape=[
            jax.ShapeDtypeStruct((tok_rows, kv_cols), jnp.bfloat16),
            jax.ShapeDtypeStruct((tok_rows, kv_cols), jnp.bfloat16),
            jax.ShapeDtypeStruct((key_heads, 1, head_dim), jnp.float32),
        ],
        compiler_params=pltpu.CompilerParams(dimension_semantics=("arbitrary",)),
    )(dk_own, dv_own, back, key_raw, key_gain.reshape(1, head_dim))


def attention_grads(grad_rows, halo_pieces, value_proj, own_doc, all_doc, key_heads,
                    head_dim, query_raw, query_gain, key_raw, key_gain):
    tok_rows, q_cols = query_raw.shape
    key_rows = WINDOW + tok_rows
    group = q_cols // (key_heads * head_dim)
    blk = BLOCK
    n_q = tok_rows // blk
    n_tiles = WINDOW // blk + 1
    gw = group * head_dim
    kv_cols = key_heads * head_dim
    stat_rows = key_heads * n_q * group * blk
    tile_flops = 2 * (group * blk) * blk * head_dim
    halo_tiles = sum(max(0, WINDOW // blk - qb) for qb in range(n_q))
    own_tiles = n_q * n_tiles - halo_tiles
    n_piece = key_heads // len(halo_pieces)
    params = pltpu.CompilerParams(dimension_semantics=("arbitrary",))
    gain_spec = pl.BlockSpec((1, head_dim), lambda h: (0, 0))
    doc_specs = [pl.BlockSpec((tok_rows, 1), lambda h: (0, 0)), pl.BlockSpec((1, key_rows), lambda h: (0, 0))]
    qdoc, kdoc = own_doc.reshape(tok_rows, 1), all_doc.reshape(1, key_rows)
    buffers = ()
    kparts = []
    for piece, (hk, hv) in enumerate(halo_pieces):
        h0 = piece * n_piece
        qcol = pl.BlockSpec((tok_rows, gw), lambda h, h0=h0: (0, h + h0))
        kcol = pl.BlockSpec((tok_rows, head_dim), lambda h, h0=h0: (0, h + h0))
        hcol = pl.BlockSpec((WINDOW, head_dim), lambda h: (0, h))
        stat = pl.BlockSpec((n_q * group * blk, 1), lambda h, h0=h0: (h + h0, 0))
        outs = pl.pallas_call(
            functools.partial(halo_kernel, group=group, head_dim=head_dim, n_alias=len(buffers)),
            grid=(n_piece,),
            in_specs=doc_specs + [qcol, qcol, hcol, hcol, kcol, kcol, gain_spec, gain_spec]
            + [pl.BlockSpec(memory_space=pl.ANY)] * len(buffers),
            out_specs=[
                qcol,
                pl.BlockSpec((WINDOW, 2 * head_dim), lambda h, h0=h0: (0, h + h0)),
                stat,
                stat,
                pl.BlockSpec((1, 1, head_dim), lambda h: (h, 0, 0)),
            ],
            out_shape=[
                jax.ShapeDtypeStruct((tok_rows, q_cols), jnp.float32),
                jax.ShapeDtypeStruct((WINDOW, 2 * kv_cols), jnp.bfloat16),
                jax.ShapeDtypeStruct((stat_rows, 1), jnp.float32),
                jax.ShapeDtypeStruct((stat_rows, 1), jnp.float32),
                jax.ShapeDtypeStruct((n_piece, 1, head_dim), jnp.float32),
            ],
            scratch_shapes=[
                pltpu.VMEM((WINDOW, head_dim), jnp.float32),
                pltpu.VMEM((WINDOW, head_dim), jnp.float32),
                pltpu.VMEM((WINDOW, head_dim), jnp.bfloat16),
                pltpu.VMEM((tok_rows, head_dim), jnp.bfloat16),
            ],
            input_output_aliases={10 + i: i for i in range(len(buffers))},
            compiler_params=params,
            cost_estimate=pl.CostEstimate(
                flops=n_piece * (2 * n_q * n_tiles + 5 * halo_tiles) * tile_flops,
                transcendentals=n_piece * (n_q * n_tiles + halo_tiles) * group * blk * blk,
                bytes_accessed=n_piece * (2 * 2 * tok_rows * gw + 2 * 2 * key_rows * head_dim
                                          + 4 * tok_rows * gw + 2 * 2 * WINDOW * head_dim),
            ),
        )(qdoc, kdoc, query_raw, grad_rows, hk, hv, key_raw, value_proj, key_gain.reshape(1, head_dim),
          query_gain.reshape(1, head_dim), *buffers)
        buffers = tuple(outs[:4])
        kparts.append(outs[4])
    dq_half, dkv_halo, log_sums, delta = buffers
    qcol = pl.BlockSpec((tok_rows, gw), lambda h: (0, h))
    kcol = pl.BlockSpec((tok_rows, head_dim), lambda h: (0, h))
    stat = pl.BlockSpec((n_q * group * blk, 1), lambda h: (h, 0))
    part_spec = pl.BlockSpec((1, 1, head_dim), lambda h: (h, 0, 0))
    part_shape = jax.ShapeDtypeStruct((key_heads, 1, head_dim), jnp.float32)
    query_grad, qgain_parts, kown_parts, dk_own, dv_own = pl.pallas_call(
        functools.partial(own_kernel, group=group, head_dim=head_dim),
        grid=(key_heads,),
        in_specs=doc_specs + [qcol, kcol, stat, stat, qcol, qcol, gain_spec, kcol, gain_spec],
        out_specs=[qcol, part_spec, part_spec, kcol, kcol],
        scratch_shapes=[pltpu.VMEM((tok_rows, head_dim), jnp.bfloat16)],
        out_shape=[
            jax.ShapeDtypeStruct((tok_rows, q_cols), jnp.bfloat16),
            part_shape,
            part_shape,
            jax.ShapeDtypeStruct((tok_rows, kv_cols), jnp.float32),
            jax.ShapeDtypeStruct((tok_rows, kv_cols), jnp.float32),
        ],
        compiler_params=params,
        cost_estimate=pl.CostEstimate(
            flops=key_heads * own_tiles * 5 * tile_flops,
            transcendentals=key_heads * own_tiles * group * blk * blk,
            bytes_accessed=2 * 2 * tok_rows * q_cols + 2 * 2 * tok_rows * kv_cols + 2 * 4 * tok_rows * q_cols
            + 2 * 4 * tok_rows * kv_cols,
        ),
    )(qdoc, kdoc, grad_rows, value_proj, log_sums, delta, dq_half, query_raw,
      query_gain.reshape(1, head_dim), key_raw, key_gain.reshape(1, head_dim))
    key_part = jnp.sum(kown_parts, axis=(0, 1))
    for part in kparts:
        key_part = key_part + jnp.sum(part, axis=(0, 1))
    return query_grad, jnp.sum(qgain_parts, axis=(0, 1)), key_part, dkv_halo, dk_own, dv_own


def per_device(query_raw, key_raw, value_proj, query_gain, key_gain, out_grad, doc_lengths):
    tok_rows = query_raw.shape[0]
    head_dim = query_gain.shape[0]
    query_heads = query_raw.shape[1] // head_dim
    key_heads = key_raw.shape[1] // head_dim
    first_pos = lax.axis_index("ctx") * tok_rows
    doc_ends = jnp.cumsum(doc_lengths)
    own_pos = first_pos + jnp.arange(tok_rows, dtype=jnp.int32)
    own_doc = doc_index(own_pos, doc_ends)
    halo_raw = first_pos - WINDOW + jnp.arange(WINDOW, dtype=jnp.int32)
    halo_doc = jnp.where(halo_raw >= 0, doc_index(halo_raw, doc_ends), -1)
    n_pieces = 2 if key_heads % 2 == 0 else 1
    width = key_heads * head_dim // n_pieces
    halo_pieces = []
    for piece in range(n_pieces):
        cols = slice(piece * width, (piece + 1) * width)
        send = (key_raw[tok_rows - WINDOW:, cols], value_proj[tok_rows - WINDOW:, cols])
        if halo_pieces:
            send = lax.optimization_barrier((send, halo_pieces[-1][0]))[0]
        halo_pieces.append(shifted(send, "ctx", 1))
    all_doc = jnp.concatenate([halo_doc, own_doc])
    query_grad, query_part, key_part, dkv_halo, dk_own, dv_own = attention_grads(
        out_grad, halo_pieces, value_proj, own_doc, all_doc, key_heads, head_dim,
        query_raw, query_gain, key_raw, key_gain,
    )
    gain_grads = butterfly_sum(jnp.stack([query_part, key_part]), ("head", "ctx"))
    back = shifted(dkv_halo, "ctx", -1)
    key_grad, value_grad, _ = kv_final(dk_own, dv_own, back, key_raw, key_gain, key_heads, head_dim)
    return (query_grad, key_grad, value_grad, gain_grads[0], gain_grads[1])


def solution(mesh):
    return jax.shard_map(
        per_device,
        mesh=mesh,
        in_specs=(
            P("ctx", "head"),
            P("ctx", "head"),
            P("ctx", "head"),
            P(),
            P(),
            P("ctx", "head"),
            P(),
        ),
        out_specs=(P("ctx", "head"), P("ctx", "head"), P("ctx", "head"), P(), P()),
        check_vma=False,
    )
```

```python
import functools
import math

import jax
import jax.numpy as jnp
from jax import lax
from jax.experimental import pallas as pl
from jax.experimental.pallas import tpu as pltpu
from jax.sharding import PartitionSpec as P

WINDOW = 1024
QUERY_SCALAR = 168


EPS = 1e-06
BLOCK = 256


def shifted(value, axis, steps):
    count = lax.axis_size(axis)
    leading, last = (max(0, -steps), min(count, count - steps))
    return lax.ppermute(value, axis, [(source, source + steps) for source in range(leading, last)])


def xor_tree(values):
    while len(values) > 1:
        values = [values[i] + values[i + 1] for i in range(0, len(values), 2)]
    return values[0]


def butterfly_sum(value, axes):
    for axis in axes:
        count = lax.axis_size(axis)
        if count & (count - 1):
            value = lax.psum(value, axis)
            continue
        bits = count.bit_length() - 1
        low = 0
        while low < bits:
            width = 1
            shifted_parts = [value]
            for mask in range(1, 1 << width):
                pairs = [(source, source ^ (mask << low)) for source in range(count)]
                shifted_parts.append(lax.ppermute(value, axis, pairs))
            value = xor_tree(shifted_parts)
            low += width
    return value


def norm_rows(raw_rows, head_count):
    values = raw_rows.astype(jnp.float32).reshape(raw_rows.shape[0], head_count, -1)
    inverse = lax.rsqrt(jnp.mean(values * values, axis=-1, keepdims=True) + EPS)
    return (values * inverse, inverse)


def norm_back(raw_rows, gain_vec, head_count, upstream):
    scaled, inverse = norm_rows(raw_rows, head_count)
    incoming = upstream.reshape(scaled.shape)
    weighted = incoming * gain_vec
    inner_sum = jnp.mean(weighted * scaled, axis=-1, keepdims=True)
    result = inverse * (weighted - scaled * inner_sum)
    return (result.reshape(raw_rows.shape), jnp.sum(incoming * scaled, axis=(0, 1)))


def doc_index(positions, doc_ends):
    return jnp.sum((positions[:, None] >= doc_ends[None, :]).astype(jnp.int32), axis=1)


def tile_mask(qdoc_ref, kdoc_ref, q_first, t, group):
    blk = BLOCK
    n_tiles = WINDOW // blk + 1
    rows = lax.broadcasted_iota(jnp.int32, (blk, blk), 0)
    cols = lax.broadcasted_iota(jnp.int32, (blk, blk), 1)
    k_first = q_first + t * blk
    live = qdoc_ref[q_first:q_first + blk, :] == kdoc_ref[:, k_first:k_first + blk]
    if t == 0:
        live = live & (cols > rows)
    if t == n_tiles - 1:
        live = live & (cols + t * blk <= rows + WINDOW)
    return jnp.concatenate([live] * group, axis=0), k_first


def normed_rows(raw, gain):
    inverse = lax.rsqrt(jnp.mean(raw * raw, axis=1, keepdims=True) + EPS)
    return (raw * inverse * gain).astype(jnp.bfloat16)


def normed_stack(ref, gain, group, head_dim, first):
    blk = BLOCK
    return jnp.concatenate(
        [normed_rows(ref[first:first + blk, a * head_dim:(a + 1) * head_dim].astype(jnp.float32), gain)
         for a in range(group)],
        axis=0,
    )


def stacked(ref, group, head_dim, first):
    blk = BLOCK
    return jnp.concatenate(
        [ref[first:first + blk, a * head_dim:(a + 1) * head_dim] for a in range(group)], axis=0
    )


def grad_tile(q_g, do_g, k_tile, v_tile, live, log_sums, delta):
    scale = QUERY_SCALAR ** (-0.5)
    scores = lax.dot_general(q_g, k_tile, (((1,), (1,)), ((), ())), preferred_element_type=jnp.float32) * scale
    weights = jnp.where(live, jnp.exp(scores - log_sums), 0.0)
    d_weights = lax.dot_general(do_g, v_tile, (((1,), (1,)), ((), ())), preferred_element_type=jnp.float32)
    d_scores = (weights * (d_weights - delta)).astype(jnp.bfloat16)
    dq_part = jnp.dot(d_scores, k_tile, preferred_element_type=jnp.float32)
    dk_part = lax.dot_general(d_scores, q_g, (((0,), (0,)), ((), ())), preferred_element_type=jnp.float32)
    dv_part = lax.dot_general(
        weights.astype(jnp.bfloat16), do_g, (((0,), (0,)), ((), ())), preferred_element_type=jnp.float32
    )
    return dq_part, dk_part * scale, dv_part


def halo_kernel(qdoc_ref, kdoc_ref, q_ref, do_ref, hk_ref, hv_ref, kraw_ref, v_ref, kgain_ref, qgain_ref, *refs,
                group, head_dim, n_alias):
    dq_ref, dkv_ref, lse_ref, delta_ref, kpart_ref, dk_ref, dv_ref, kn_ref, k_ref = refs[n_alias:]
    blk = BLOCK
    n_tiles = WINDOW // blk + 1
    n_halo = WINDOW // blk
    n_q = q_ref.shape[0] // blk
    gb = group * blk
    scale = QUERY_SCALAR ** (-0.5)
    dk_ref[...] = jnp.zeros(dk_ref.shape, jnp.float32)
    dv_ref[...] = jnp.zeros(dv_ref.shape, jnp.float32)
    halo_raw = hk_ref[...].astype(jnp.float32)
    halo_inv = lax.rsqrt(jnp.mean(halo_raw * halo_raw, axis=1, keepdims=True) + EPS)
    kn_ref[...] = (halo_raw * halo_inv * kgain_ref[...]).astype(jnp.bfloat16)
    k_ref[...] = normed_rows(kraw_ref[...].astype(jnp.float32), kgain_ref[...])
    qgain = qgain_ref[...]

    def key_tile(k_first):
        if k_first < WINDOW:
            return kn_ref[k_first:k_first + blk, :], hv_ref[k_first:k_first + blk, :]
        own_first = k_first - WINDOW
        return k_ref[own_first:own_first + blk, :], v_ref[own_first:own_first + blk, :]

    for qb in range(n_q):
        q_first = qb * blk
        q_g = normed_stack(q_ref, qgain, group, head_dim, q_first)
        do_g = stacked(do_ref, group, head_dim, q_first)
        masks = [tile_mask(qdoc_ref, kdoc_ref, q_first, t, group)[0] for t in range(n_tiles)]
        totals = jnp.zeros((gb, 1), jnp.float32)
        numer = jnp.zeros((gb, head_dim), jnp.float32)
        for t in range(n_tiles):
            k_first = q_first + t * blk
            k_tile, v_tile = key_tile(k_first)
            scores = lax.dot_general(
                q_g, k_tile, (((1,), (1,)), ((), ())), preferred_element_type=jnp.float32
            ) * scale
            exp_s = jnp.where(masks[t], jnp.exp(scores), 0.0)
            totals = totals + jnp.sum(exp_s, axis=1, keepdims=True)
            numer = numer + jnp.dot(exp_s.astype(jnp.bfloat16), v_tile, preferred_element_type=jnp.float32)
        log_sums = jnp.log(totals)
        attn_out = numer / totals
        delta = jnp.sum(do_g.astype(jnp.float32) * attn_out, axis=1, keepdims=True)
        lse_ref[qb * gb:(qb + 1) * gb, :] = log_sums
        delta_ref[qb * gb:(qb + 1) * gb, :] = delta
        dq = jnp.zeros((gb, head_dim), jnp.float32)
        for t in range(n_halo - qb):
            k_first = q_first + t * blk
            k_tile, v_tile = key_tile(k_first)
            dq_part, dk_part, dv_part = grad_tile(q_g, do_g, k_tile, v_tile, masks[t], log_sums, delta)
            dq = dq + dq_part
            dk_ref[k_first:k_first + blk, :] += dk_part
            dv_ref[k_first:k_first + blk, :] += dv_part
        dq_ref[q_first:q_first + blk, :] = jnp.concatenate(
            [dq[a * blk:(a + 1) * blk] for a in range(group)], axis=1
        ) * scale
    dkv_ref[:, :head_dim] = dk_ref[...].astype(jnp.bfloat16)
    dkv_ref[:, head_dim:] = dv_ref[...].astype(jnp.bfloat16)
    halo_hat = halo_raw * halo_inv
    kpart_ref[...] = jnp.sum(dk_ref[...] * halo_hat, axis=0, keepdims=True).reshape(kpart_ref.shape)


def norm_grad(raw, gain, upstream):
    inverse = lax.rsqrt(jnp.mean(raw * raw, axis=1, keepdims=True) + EPS)
    scaled = raw * inverse
    weighted = upstream * gain
    inner_sum = jnp.mean(weighted * scaled, axis=1, keepdims=True)
    result = inverse * (weighted - scaled * inner_sum)
    return result, jnp.sum(upstream * scaled, axis=0, keepdims=True)


def own_kernel(qdoc_ref, kdoc_ref, do_ref, v_ref, lse_ref, delta_ref, dq_in_ref, raw_ref, gain_ref,
               kraw_ref, kgain_ref, qgrad_ref, qgain_ref, kpart_ref, dk_ref, dv_ref, k_ref, *, group, head_dim):
    q_ref = raw_ref
    blk = BLOCK
    n_tiles = WINDOW // blk + 1
    n_halo = WINDOW // blk
    n_q = q_ref.shape[0] // blk
    gb = group * blk
    scale = QUERY_SCALAR ** (-0.5)
    dk_ref[...] = jnp.zeros(dk_ref.shape, jnp.float32)
    dv_ref[...] = jnp.zeros(dv_ref.shape, jnp.float32)
    gain = gain_ref[...]
    k_ref[...] = normed_rows(kraw_ref[...].astype(jnp.float32), kgain_ref[...])
    gain_sum = jnp.zeros((1, head_dim), jnp.float32)
    for qb in range(n_q):
        q_first = qb * blk
        q_g = normed_stack(q_ref, gain, group, head_dim, q_first)
        do_g = stacked(do_ref, group, head_dim, q_first)
        log_sums = lse_ref[qb * gb:(qb + 1) * gb, :]
        delta = delta_ref[qb * gb:(qb + 1) * gb, :]
        dq = jnp.zeros((gb, head_dim), jnp.float32)
        for t in range(max(0, n_halo - qb), n_tiles):
            live, _ = tile_mask(qdoc_ref, kdoc_ref, q_first, t, group)
            k_first = q_first + t * blk
            own_first = k_first - WINDOW
            k_tile = k_ref[own_first:own_first + blk, :]
            v_tile = v_ref[own_first:own_first + blk, :]
            dq_part, dk_part, dv_part = grad_tile(q_g, do_g, k_tile, v_tile, live, log_sums, delta)
            dq = dq + dq_part
            dk_ref[own_first:own_first + blk, :] += dk_part
            dv_ref[own_first:own_first + blk, :] += dv_part
        dq_in = dq_in_ref[q_first:q_first + blk, :]
        raw = raw_ref[q_first:q_first + blk, :].astype(jnp.float32)
        for a in range(group):
            cols = slice(a * head_dim, (a + 1) * head_dim)
            upstream = dq_in[:, cols] + dq[a * blk:(a + 1) * blk] * scale
            result, part = norm_grad(raw[:, cols], gain, upstream)
            qgrad_ref[q_first:q_first + blk, cols] = result.astype(qgrad_ref.dtype)
            gain_sum = gain_sum + part
    qgain_ref[...] = gain_sum.reshape(qgain_ref.shape)
    key_raw = kraw_ref[...].astype(jnp.float32)
    key_hat = key_raw * lax.rsqrt(jnp.mean(key_raw * key_raw, axis=1, keepdims=True) + EPS)
    kpart_ref[...] = jnp.sum(dk_ref[...] * key_hat, axis=0, keepdims=True).reshape(kpart_ref.shape)


def kv_final_kernel(dk_ref, dv_ref, back_ref, raw_ref, gain_ref, kgrad_ref, vgrad_ref, kgain_ref, *, head_dim):
    tok_rows = dk_ref.shape[0]
    lead = tok_rows - WINDOW
    back = back_ref[...].astype(jnp.float32)
    dk = dk_ref[...]
    dv = dv_ref[...]
    if lead:
        dk = jnp.concatenate([dk[:lead], dk[lead:] + back[:, :head_dim]], axis=0)
        dv = jnp.concatenate([dv[:lead], dv[lead:] + back[:, head_dim:]], axis=0)
    else:
        dk = dk + back[:, :head_dim]
        dv = dv + back[:, head_dim:]
    vgrad_ref[...] = dv.astype(vgrad_ref.dtype)
    result, part = norm_grad(raw_ref[...].astype(jnp.float32), gain_ref[...], dk)
    kgrad_ref[...] = result.astype(kgrad_ref.dtype)
    kgain_ref[...] = part.reshape(kgain_ref.shape)


def kv_final(dk_own, dv_own, back, key_raw, key_gain, key_heads, head_dim):
    tok_rows = dk_own.shape[0]
    kv_cols = key_heads * head_dim
    col_spec = pl.BlockSpec((tok_rows, head_dim), lambda h: (0, h))
    return pl.pallas_call(
        functools.partial(kv_final_kernel, head_dim=head_dim),
        grid=(key_heads,),
        in_specs=[
            col_spec,
            col_spec,
            pl.BlockSpec((WINDOW, 2 * head_dim), lambda h: (0, h)),
            col_spec,
            pl.BlockSpec((1, head_dim), lambda h: (0, 0)),
        ],
        out_specs=[col_spec, col_spec, pl.BlockSpec((1, 1, head_dim), lambda h: (h, 0, 0))],
        out_shape=[
            jax.ShapeDtypeStruct((tok_rows, kv_cols), jnp.bfloat16),
            jax.ShapeDtypeStruct((tok_rows, kv_cols), jnp.bfloat16),
            jax.ShapeDtypeStruct((key_heads, 1, head_dim), jnp.float32),
        ],
        compiler_params=pltpu.CompilerParams(dimension_semantics=("arbitrary",)),
    )(dk_own, dv_own, back, key_raw, key_gain.reshape(1, head_dim))


def attention_grads(grad_rows, halo_pieces, value_proj, own_doc, all_doc, key_heads,
                    head_dim, query_raw, query_gain, key_raw, key_gain):
    tok_rows, q_cols = query_raw.shape
    key_rows = WINDOW + tok_rows
    group = q_cols // (key_heads * head_dim)
    blk = BLOCK
    n_q = tok_rows // blk
    n_tiles = WINDOW // blk + 1
    gw = group * head_dim
    kv_cols = key_heads * head_dim
    stat_rows = key_heads * n_q * group * blk
    tile_flops = 2 * (group * blk) * blk * head_dim
    halo_tiles = sum(max(0, WINDOW // blk - qb) for qb in range(n_q))
    own_tiles = n_q * n_tiles - halo_tiles
    n_piece = key_heads // len(halo_pieces)
    params = pltpu.CompilerParams(dimension_semantics=("arbitrary",))
    gain_spec = pl.BlockSpec((1, head_dim), lambda h: (0, 0))
    doc_specs = [pl.BlockSpec((tok_rows, 1), lambda h: (0, 0)), pl.BlockSpec((1, key_rows), lambda h: (0, 0))]
    qdoc, kdoc = own_doc.reshape(tok_rows, 1), all_doc.reshape(1, key_rows)
    buffers = ()
    kparts = []
    for piece, halo in enumerate(halo_pieces):
        h0 = piece * n_piece
        qcol = pl.BlockSpec((tok_rows, gw), lambda h, h0=h0: (0, h + h0))
        kcol = pl.BlockSpec((tok_rows, head_dim), lambda h, h0=h0: (0, h + h0))
        hcol = pl.BlockSpec((WINDOW, head_dim), lambda h: (0, h))
        vcol = pl.BlockSpec((WINDOW, head_dim), lambda h, n_piece=n_piece: (0, h + n_piece))
        stat = pl.BlockSpec((n_q * group * blk, 1), lambda h, h0=h0: (h + h0, 0))
        outs = pl.pallas_call(
            functools.partial(halo_kernel, group=group, head_dim=head_dim, n_alias=len(buffers)),
            grid=(n_piece,),
            in_specs=doc_specs + [qcol, qcol, hcol, vcol, kcol, kcol, gain_spec, gain_spec]
            + [pl.BlockSpec(memory_space=pl.ANY)] * len(buffers),
            out_specs=[
                qcol,
                pl.BlockSpec((WINDOW, 2 * head_dim), lambda h, h0=h0: (0, h + h0)),
                stat,
                stat,
                pl.BlockSpec((1, 1, head_dim), lambda h: (h, 0, 0)),
            ],
            out_shape=[
                jax.ShapeDtypeStruct((tok_rows, q_cols), jnp.float32),
                jax.ShapeDtypeStruct((WINDOW, 2 * kv_cols), jnp.bfloat16),
                jax.ShapeDtypeStruct((stat_rows, 1), jnp.float32),
                jax.ShapeDtypeStruct((stat_rows, 1), jnp.float32),
                jax.ShapeDtypeStruct((n_piece, 1, head_dim), jnp.float32),
            ],
            scratch_shapes=[
                pltpu.VMEM((WINDOW, head_dim), jnp.float32),
                pltpu.VMEM((WINDOW, head_dim), jnp.float32),
                pltpu.VMEM((WINDOW, head_dim), jnp.bfloat16),
                pltpu.VMEM((tok_rows, head_dim), jnp.bfloat16),
            ],
            input_output_aliases={10 + i: i for i in range(len(buffers))},
            compiler_params=params,
            cost_estimate=pl.CostEstimate(
                flops=n_piece * (2 * n_q * n_tiles + 5 * halo_tiles) * tile_flops,
                transcendentals=n_piece * (n_q * n_tiles + halo_tiles) * group * blk * blk,
                bytes_accessed=n_piece * (2 * 2 * tok_rows * gw + 2 * 2 * key_rows * head_dim
                                          + 4 * tok_rows * gw + 2 * 2 * WINDOW * head_dim),
            ),
        )(qdoc, kdoc, query_raw, grad_rows, halo, halo, key_raw, value_proj, key_gain.reshape(1, head_dim),
          query_gain.reshape(1, head_dim), *buffers)
        buffers = tuple(outs[:4])
        kparts.append(outs[4])
    dq_half, dkv_halo, log_sums, delta = buffers
    qcol = pl.BlockSpec((tok_rows, gw), lambda h: (0, h))
    kcol = pl.BlockSpec((tok_rows, head_dim), lambda h: (0, h))
    stat = pl.BlockSpec((n_q * group * blk, 1), lambda h: (h, 0))
    part_spec = pl.BlockSpec((1, 1, head_dim), lambda h: (h, 0, 0))
    part_shape = jax.ShapeDtypeStruct((key_heads, 1, head_dim), jnp.float32)
    query_grad, qgain_parts, kown_parts, dk_own, dv_own = pl.pallas_call(
        functools.partial(own_kernel, group=group, head_dim=head_dim),
        grid=(key_heads,),
        in_specs=doc_specs + [qcol, kcol, stat, stat, qcol, qcol, gain_spec, kcol, gain_spec],
        out_specs=[qcol, part_spec, part_spec, kcol, kcol],
        scratch_shapes=[pltpu.VMEM((tok_rows, head_dim), jnp.bfloat16)],
        out_shape=[
            jax.ShapeDtypeStruct((tok_rows, q_cols), jnp.bfloat16),
            part_shape,
            part_shape,
            jax.ShapeDtypeStruct((tok_rows, kv_cols), jnp.float32),
            jax.ShapeDtypeStruct((tok_rows, kv_cols), jnp.float32),
        ],
        compiler_params=params,
        cost_estimate=pl.CostEstimate(
            flops=key_heads * own_tiles * 5 * tile_flops,
            transcendentals=key_heads * own_tiles * group * blk * blk,
            bytes_accessed=2 * 2 * tok_rows * q_cols + 2 * 2 * tok_rows * kv_cols + 2 * 4 * tok_rows * q_cols
            + 2 * 4 * tok_rows * kv_cols,
        ),
    )(qdoc, kdoc, grad_rows, value_proj, log_sums, delta, dq_half, query_raw,
      query_gain.reshape(1, head_dim), key_raw, key_gain.reshape(1, head_dim))
    key_part = jnp.sum(kown_parts, axis=(0, 1))
    for part in kparts:
        key_part = key_part + jnp.sum(part, axis=(0, 1))
    return query_grad, jnp.sum(qgain_parts, axis=(0, 1)), key_part, dkv_halo, dk_own, dv_own


def per_device(query_raw, key_raw, value_proj, query_gain, key_gain, out_grad, doc_lengths):
    tok_rows = query_raw.shape[0]
    head_dim = query_gain.shape[0]
    query_heads = query_raw.shape[1] // head_dim
    key_heads = key_raw.shape[1] // head_dim
    first_pos = lax.axis_index("ctx") * tok_rows
    doc_ends = jnp.cumsum(doc_lengths)
    own_pos = first_pos + jnp.arange(tok_rows, dtype=jnp.int32)
    own_doc = doc_index(own_pos, doc_ends)
    halo_raw = first_pos - WINDOW + jnp.arange(WINDOW, dtype=jnp.int32)
    halo_doc = jnp.where(halo_raw >= 0, doc_index(halo_raw, doc_ends), -1)
    n_pieces = 2 if key_heads % 2 == 0 else 1
    width = key_heads * head_dim // n_pieces
    halo_pieces = []
    for piece in range(n_pieces):
        cols = slice(piece * width, (piece + 1) * width)
        send = jnp.concatenate([key_raw[tok_rows - WINDOW:, cols], value_proj[tok_rows - WINDOW:, cols]], axis=1)
        if halo_pieces:
            send = lax.optimization_barrier((send, halo_pieces[-1]))[0]
        halo_pieces.append(shifted(send, "ctx", 1))
    all_doc = jnp.concatenate([halo_doc, own_doc])
    query_grad, query_part, key_part, dkv_halo, dk_own, dv_own = attention_grads(
        out_grad, halo_pieces, value_proj, own_doc, all_doc, key_heads, head_dim,
        query_raw, query_gain, key_raw, key_gain,
    )
    gain_grads = butterfly_sum(jnp.stack([query_part, key_part]), ("head", "ctx"))
    back = shifted(dkv_halo, "ctx", -1)
    key_grad, value_grad, _ = kv_final(dk_own, dv_own, back, key_raw, key_gain, key_heads, head_dim)
    return (query_grad, key_grad, value_grad, gain_grads[0], gain_grads[1])


def solution(mesh):
    return jax.shard_map(
        per_device,
        mesh=mesh,
        in_specs=(
            P("ctx", "head"),
            P("ctx", "head"),
            P("ctx", "head"),
            P(),
            P(),
            P("ctx", "head"),
            P(),
        ),
        out_specs=(P("ctx", "head"), P("ctx", "head"), P("ctx", "head"), P(), P()),
        check_vma=False,
    )
```

```python
import functools
import math

import jax
import jax.numpy as jnp
from jax import lax
from jax.experimental import pallas as pl
from jax.experimental.pallas import tpu as pltpu
from jax.sharding import PartitionSpec as P

WINDOW = 1024
QUERY_SCALAR = 168


EPS = 1e-06
BLOCK = 256


def shifted(value, axis, steps):
    count = lax.axis_size(axis)
    leading, last = (max(0, -steps), min(count, count - steps))
    return lax.ppermute(value, axis, [(source, source + steps) for source in range(leading, last)])


def xor_tree(values):
    while len(values) > 1:
        values = [values[i] + values[i + 1] for i in range(0, len(values), 2)]
    return values[0]


def butterfly_sum(value, axes):
    for axis in axes:
        count = lax.axis_size(axis)
        if count & (count - 1):
            value = lax.psum(value, axis)
            continue
        bits = count.bit_length() - 1
        low = 0
        while low < bits:
            width = 1
            shifted_parts = [value]
            for mask in range(1, 1 << width):
                pairs = [(source, source ^ (mask << low)) for source in range(count)]
                shifted_parts.append(lax.ppermute(value, axis, pairs))
            value = xor_tree(shifted_parts)
            low += width
    return value


def norm_rows(raw_rows, head_count):
    values = raw_rows.astype(jnp.float32).reshape(raw_rows.shape[0], head_count, -1)
    inverse = lax.rsqrt(jnp.mean(values * values, axis=-1, keepdims=True) + EPS)
    return (values * inverse, inverse)


def norm_back(raw_rows, gain_vec, head_count, upstream):
    scaled, inverse = norm_rows(raw_rows, head_count)
    incoming = upstream.reshape(scaled.shape)
    weighted = incoming * gain_vec
    inner_sum = jnp.mean(weighted * scaled, axis=-1, keepdims=True)
    result = inverse * (weighted - scaled * inner_sum)
    return (result.reshape(raw_rows.shape), jnp.sum(incoming * scaled, axis=(0, 1)))


def doc_index(positions, doc_ends):
    return jnp.sum((positions[:, None] >= doc_ends[None, :]).astype(jnp.int32), axis=1)


def tile_mask(qdoc_ref, kdoc_ref, q_first, t, group):
    blk = BLOCK
    n_tiles = WINDOW // blk + 1
    rows = lax.broadcasted_iota(jnp.int32, (blk, blk), 0)
    cols = lax.broadcasted_iota(jnp.int32, (blk, blk), 1)
    k_first = q_first + t * blk
    live = qdoc_ref[q_first:q_first + blk, :] == kdoc_ref[:, k_first:k_first + blk]
    if t == 0:
        live = live & (cols > rows)
    if t == n_tiles - 1:
        live = live & (cols + t * blk <= rows + WINDOW)
    return jnp.concatenate([live] * group, axis=0), k_first


def normed_rows(raw, gain):
    inverse = lax.rsqrt(jnp.mean(raw * raw, axis=1, keepdims=True) + EPS)
    return (raw * inverse * gain).astype(jnp.bfloat16)


def normed_stack(ref, gain, group, head_dim, first):
    blk = BLOCK
    return jnp.concatenate(
        [normed_rows(ref[first:first + blk, a * head_dim:(a + 1) * head_dim].astype(jnp.float32), gain)
         for a in range(group)],
        axis=0,
    )


def stacked(ref, group, head_dim, first):
    blk = BLOCK
    return jnp.concatenate(
        [ref[first:first + blk, a * head_dim:(a + 1) * head_dim] for a in range(group)], axis=0
    )


def grad_tile(q_g, do_g, k_tile, v_tile, live, log_sums, delta):
    scale = QUERY_SCALAR ** (-0.5)
    scores = lax.dot_general(q_g, k_tile, (((1,), (1,)), ((), ())), preferred_element_type=jnp.float32) * scale
    weights = jnp.where(live, jnp.exp(scores - log_sums), 0.0)
    d_weights = lax.dot_general(do_g, v_tile, (((1,), (1,)), ((), ())), preferred_element_type=jnp.float32)
    d_scores = (weights * (d_weights - delta)).astype(jnp.bfloat16)
    dq_part = jnp.dot(d_scores, k_tile, preferred_element_type=jnp.float32)
    dk_part = lax.dot_general(d_scores, q_g, (((0,), (0,)), ((), ())), preferred_element_type=jnp.float32)
    dv_part = lax.dot_general(
        weights.astype(jnp.bfloat16), do_g, (((0,), (0,)), ((), ())), preferred_element_type=jnp.float32
    )
    return dq_part, dk_part * scale, dv_part


def halo_kernel(qdoc_ref, kdoc_ref, q_ref, do_ref, hk_ref, hv_ref, kraw_ref, v_ref, kgain_ref, qgain_ref, *refs,
                group, head_dim, n_alias):
    dq_ref, dkv_ref, lse_ref, delta_ref, kpart_ref, dk_ref, dv_ref, kn_ref, k_ref = refs[n_alias:]
    blk = BLOCK
    n_tiles = WINDOW // blk + 1
    n_halo = WINDOW // blk
    n_q = q_ref.shape[0] // blk
    gb = group * blk
    scale = QUERY_SCALAR ** (-0.5)
    dk_ref[...] = jnp.zeros(dk_ref.shape, jnp.float32)
    dv_ref[...] = jnp.zeros(dv_ref.shape, jnp.float32)
    halo_raw = hk_ref[...].astype(jnp.float32)
    halo_inv = lax.rsqrt(jnp.mean(halo_raw * halo_raw, axis=1, keepdims=True) + EPS)
    kn_ref[...] = (halo_raw * halo_inv * kgain_ref[...]).astype(jnp.bfloat16)
    k_ref[...] = normed_rows(kraw_ref[...].astype(jnp.float32), kgain_ref[...])
    qgain = qgain_ref[...]

    def key_tile(k_first):
        if k_first < WINDOW:
            return kn_ref[k_first:k_first + blk, :], hv_ref[k_first:k_first + blk, :]
        own_first = k_first - WINDOW
        return k_ref[own_first:own_first + blk, :], v_ref[own_first:own_first + blk, :]

    for qb in range(n_q):
        q_first = qb * blk
        q_g = normed_stack(q_ref, qgain, group, head_dim, q_first)
        do_g = stacked(do_ref, group, head_dim, q_first)
        masks = [tile_mask(qdoc_ref, kdoc_ref, q_first, t, group)[0] for t in range(n_tiles)]
        totals = jnp.zeros((gb, 1), jnp.float32)
        numer = jnp.zeros((gb, head_dim), jnp.float32)
        for t in range(n_tiles):
            k_first = q_first + t * blk
            k_tile, v_tile = key_tile(k_first)
            scores = lax.dot_general(
                q_g, k_tile, (((1,), (1,)), ((), ())), preferred_element_type=jnp.float32
            ) * scale
            exp_s = jnp.where(masks[t], jnp.exp(scores), 0.0)
            totals = totals + jnp.sum(exp_s, axis=1, keepdims=True)
            numer = numer + jnp.dot(exp_s.astype(jnp.bfloat16), v_tile, preferred_element_type=jnp.float32)
        log_sums = jnp.log(totals)
        attn_out = numer / totals
        delta = jnp.sum(do_g.astype(jnp.float32) * attn_out, axis=1, keepdims=True)
        lse_ref[qb * gb:(qb + 1) * gb, :] = log_sums
        delta_ref[qb * gb:(qb + 1) * gb, :] = delta
        dq = jnp.zeros((gb, head_dim), jnp.float32)
        for t in range(n_halo - qb):
            k_first = q_first + t * blk
            k_tile, v_tile = key_tile(k_first)
            dq_part, dk_part, dv_part = grad_tile(q_g, do_g, k_tile, v_tile, masks[t], log_sums, delta)
            dq = dq + dq_part
            dk_ref[k_first:k_first + blk, :] += dk_part
            dv_ref[k_first:k_first + blk, :] += dv_part
        dq_ref[q_first:q_first + blk, :] = jnp.concatenate(
            [dq[a * blk:(a + 1) * blk] for a in range(group)], axis=1
        ) * scale
    dkv_ref[:, :head_dim] = dk_ref[...].astype(jnp.bfloat16)
    dkv_ref[:, head_dim:] = dv_ref[...].astype(jnp.bfloat16)
    halo_hat = halo_raw * halo_inv
    kpart_ref[...] = jnp.sum(dk_ref[...] * halo_hat, axis=0, keepdims=True).reshape(kpart_ref.shape)


def norm_grad(raw, gain, upstream):
    inverse = lax.rsqrt(jnp.mean(raw * raw, axis=1, keepdims=True) + EPS)
    scaled = raw * inverse
    weighted = upstream * gain
    inner_sum = jnp.mean(weighted * scaled, axis=1, keepdims=True)
    result = inverse * (weighted - scaled * inner_sum)
    return result, jnp.sum(upstream * scaled, axis=0, keepdims=True)


def own_kernel(qdoc_ref, kdoc_ref, do_ref, v_ref, lse_ref, delta_ref, dq_in_ref, raw_ref, gain_ref,
               kraw_ref, kgain_ref, *refs, group, head_dim, n_alias):
    qgrad_ref, qgain_ref, kpart_ref, dk_ref, dv_ref, k_ref = refs[n_alias:]
    q_ref = raw_ref
    blk = BLOCK
    n_tiles = WINDOW // blk + 1
    n_halo = WINDOW // blk
    n_q = q_ref.shape[0] // blk
    gb = group * blk
    scale = QUERY_SCALAR ** (-0.5)
    dk_ref[...] = jnp.zeros(dk_ref.shape, jnp.float32)
    dv_ref[...] = jnp.zeros(dv_ref.shape, jnp.float32)
    gain = gain_ref[...]
    k_ref[...] = normed_rows(kraw_ref[...].astype(jnp.float32), kgain_ref[...])
    gain_sum = jnp.zeros((1, head_dim), jnp.float32)
    for qb in range(n_q):
        q_first = qb * blk
        q_g = normed_stack(q_ref, gain, group, head_dim, q_first)
        do_g = stacked(do_ref, group, head_dim, q_first)
        log_sums = lse_ref[qb * gb:(qb + 1) * gb, :]
        delta = delta_ref[qb * gb:(qb + 1) * gb, :]
        dq = jnp.zeros((gb, head_dim), jnp.float32)
        for t in range(max(0, n_halo - qb), n_tiles):
            live, _ = tile_mask(qdoc_ref, kdoc_ref, q_first, t, group)
            k_first = q_first + t * blk
            own_first = k_first - WINDOW
            k_tile = k_ref[own_first:own_first + blk, :]
            v_tile = v_ref[own_first:own_first + blk, :]
            dq_part, dk_part, dv_part = grad_tile(q_g, do_g, k_tile, v_tile, live, log_sums, delta)
            dq = dq + dq_part
            dk_ref[own_first:own_first + blk, :] += dk_part
            dv_ref[own_first:own_first + blk, :] += dv_part
        dq_in = dq_in_ref[q_first:q_first + blk, :]
        raw = raw_ref[q_first:q_first + blk, :].astype(jnp.float32)
        for a in range(group):
            cols = slice(a * head_dim, (a + 1) * head_dim)
            upstream = dq_in[:, cols] + dq[a * blk:(a + 1) * blk] * scale
            result, part = norm_grad(raw[:, cols], gain, upstream)
            qgrad_ref[q_first:q_first + blk, cols] = result.astype(qgrad_ref.dtype)
            gain_sum = gain_sum + part
    qgain_ref[...] = gain_sum.reshape(qgain_ref.shape)
    key_raw = kraw_ref[...].astype(jnp.float32)
    key_hat = key_raw * lax.rsqrt(jnp.mean(key_raw * key_raw, axis=1, keepdims=True) + EPS)
    kpart_ref[...] = jnp.sum(dk_ref[...] * key_hat, axis=0, keepdims=True).reshape(kpart_ref.shape)


def kv_final_kernel(dk_ref, dv_ref, back_ref, raw_ref, gain_ref, kgrad_ref, vgrad_ref, kgain_ref, *, head_dim):
    tok_rows = dk_ref.shape[0]
    lead = tok_rows - WINDOW
    back = back_ref[...].astype(jnp.float32)
    dk = dk_ref[...]
    dv = dv_ref[...]
    if lead:
        dk = jnp.concatenate([dk[:lead], dk[lead:] + back[:, :head_dim]], axis=0)
        dv = jnp.concatenate([dv[:lead], dv[lead:] + back[:, head_dim:]], axis=0)
    else:
        dk = dk + back[:, :head_dim]
        dv = dv + back[:, head_dim:]
    vgrad_ref[...] = dv.astype(vgrad_ref.dtype)
    result, part = norm_grad(raw_ref[...].astype(jnp.float32), gain_ref[...], dk)
    kgrad_ref[...] = result.astype(kgrad_ref.dtype)
    kgain_ref[...] = part.reshape(kgain_ref.shape)


def kv_final(dk_own, dv_own, back, key_raw, key_gain, key_heads, head_dim):
    tok_rows = dk_own.shape[0]
    kv_cols = key_heads * head_dim
    col_spec = pl.BlockSpec((tok_rows, head_dim), lambda h: (0, h))
    return pl.pallas_call(
        functools.partial(kv_final_kernel, head_dim=head_dim),
        grid=(key_heads,),
        in_specs=[
            col_spec,
            col_spec,
            pl.BlockSpec((WINDOW, 2 * head_dim), lambda h: (0, h)),
            col_spec,
            pl.BlockSpec((1, head_dim), lambda h: (0, 0)),
        ],
        out_specs=[col_spec, col_spec, pl.BlockSpec((1, 1, head_dim), lambda h: (h, 0, 0))],
        out_shape=[
            jax.ShapeDtypeStruct((tok_rows, kv_cols), jnp.bfloat16),
            jax.ShapeDtypeStruct((tok_rows, kv_cols), jnp.bfloat16),
            jax.ShapeDtypeStruct((key_heads, 1, head_dim), jnp.float32),
        ],
        compiler_params=pltpu.CompilerParams(dimension_semantics=("arbitrary",)),
    )(dk_own, dv_own, back, key_raw, key_gain.reshape(1, head_dim))


def attention_grads(grad_rows, halo_pieces, value_proj, own_doc, all_doc, key_heads,
                    head_dim, query_raw, query_gain, key_raw, key_gain):
    tok_rows, q_cols = query_raw.shape
    key_rows = WINDOW + tok_rows
    group = q_cols // (key_heads * head_dim)
    blk = BLOCK
    n_q = tok_rows // blk
    n_tiles = WINDOW // blk + 1
    gw = group * head_dim
    kv_cols = key_heads * head_dim
    stat_rows = key_heads * n_q * group * blk
    tile_flops = 2 * (group * blk) * blk * head_dim
    halo_tiles = sum(max(0, WINDOW // blk - qb) for qb in range(n_q))
    own_tiles = n_q * n_tiles - halo_tiles
    n_piece = key_heads // len(halo_pieces)
    params = pltpu.CompilerParams(dimension_semantics=("arbitrary",))
    gain_spec = pl.BlockSpec((1, head_dim), lambda h: (0, 0))
    doc_specs = [pl.BlockSpec((tok_rows, 1), lambda h: (0, 0)), pl.BlockSpec((1, key_rows), lambda h: (0, 0))]
    qdoc, kdoc = own_doc.reshape(tok_rows, 1), all_doc.reshape(1, key_rows)
    buffers = ()
    key_part = None
    query_part = None
    backs = []
    for piece, halo in enumerate(halo_pieces):
        h0 = piece * n_piece
        if query_part is not None:
            halo = lax.optimization_barrier((halo, query_part))[0]
        qcol = pl.BlockSpec((tok_rows, gw), lambda h, h0=h0: (0, h + h0))
        kcol = pl.BlockSpec((tok_rows, head_dim), lambda h, h0=h0: (0, h + h0))
        hcol = pl.BlockSpec((WINDOW, head_dim), lambda h: (0, h))
        vcol = pl.BlockSpec((WINDOW, head_dim), lambda h, n_piece=n_piece: (0, h + n_piece))
        local_q = pl.BlockSpec((tok_rows, gw), lambda h: (0, h))
        stat = pl.BlockSpec((n_q * group * blk, 1), lambda h: (h, 0))
        part_spec = pl.BlockSpec((1, 1, head_dim), lambda h: (h, 0, 0))
        part_shape = jax.ShapeDtypeStruct((n_piece, 1, head_dim), jnp.float32)
        dq_half, dkv_halo, log_sums, delta, khalo = pl.pallas_call(
            functools.partial(halo_kernel, group=group, head_dim=head_dim, n_alias=0),
            grid=(n_piece,),
            in_specs=doc_specs + [qcol, qcol, hcol, vcol, kcol, kcol, gain_spec, gain_spec],
            out_specs=[local_q, pl.BlockSpec((WINDOW, 2 * head_dim), lambda h: (0, h)), stat, stat, part_spec],
            out_shape=[
                jax.ShapeDtypeStruct((tok_rows, gw * n_piece), jnp.float32),
                jax.ShapeDtypeStruct((WINDOW, 2 * head_dim * n_piece), jnp.bfloat16),
                jax.ShapeDtypeStruct((stat_rows * n_piece // key_heads, 1), jnp.float32),
                jax.ShapeDtypeStruct((stat_rows * n_piece // key_heads, 1), jnp.float32),
                part_shape,
            ],
            scratch_shapes=[
                pltpu.VMEM((WINDOW, head_dim), jnp.float32),
                pltpu.VMEM((WINDOW, head_dim), jnp.float32),
                pltpu.VMEM((WINDOW, head_dim), jnp.bfloat16),
                pltpu.VMEM((tok_rows, head_dim), jnp.bfloat16),
            ],
            compiler_params=params,
            cost_estimate=pl.CostEstimate(
                flops=n_piece * (2 * n_q * n_tiles + 5 * halo_tiles) * tile_flops,
                transcendentals=n_piece * (n_q * n_tiles + halo_tiles) * group * blk * blk,
                bytes_accessed=n_piece * (2 * 2 * tok_rows * gw + 2 * 2 * key_rows * head_dim
                                          + 4 * tok_rows * gw + 2 * 2 * WINDOW * head_dim),
            ),
        )(qdoc, kdoc, query_raw, grad_rows, halo, halo, key_raw, value_proj, key_gain.reshape(1, head_dim),
          query_gain.reshape(1, head_dim))
        backs.append(shifted(dkv_halo, "ctx", -1))
        outs = pl.pallas_call(
            functools.partial(own_kernel, group=group, head_dim=head_dim, n_alias=len(buffers)),
            grid=(n_piece,),
            in_specs=doc_specs + [qcol, kcol, stat, stat, local_q, qcol, gain_spec, kcol, gain_spec]
            + [pl.BlockSpec(memory_space=pl.ANY)] * len(buffers),
            out_specs=[qcol, part_spec, part_spec, kcol, kcol],
            out_shape=[
                jax.ShapeDtypeStruct((tok_rows, q_cols), jnp.bfloat16),
                part_shape,
                part_shape,
                jax.ShapeDtypeStruct((tok_rows, kv_cols), jnp.float32),
                jax.ShapeDtypeStruct((tok_rows, kv_cols), jnp.float32),
            ],
            scratch_shapes=[pltpu.VMEM((tok_rows, head_dim), jnp.bfloat16)],
            input_output_aliases=dict(zip(range(11, 11 + len(buffers)), (0, 3, 4))),
            compiler_params=params,
            cost_estimate=pl.CostEstimate(
                flops=n_piece * own_tiles * 5 * tile_flops,
                transcendentals=n_piece * own_tiles * group * blk * blk,
                bytes_accessed=n_piece * (2 * 2 * tok_rows * gw + 2 * 2 * tok_rows * head_dim
                                          + 2 * 4 * tok_rows * gw + 2 * 4 * tok_rows * head_dim),
            ),
        )(qdoc, kdoc, grad_rows, value_proj, log_sums, delta, dq_half, query_raw,
          query_gain.reshape(1, head_dim), key_raw, key_gain.reshape(1, head_dim), *buffers)
        query_grad, qparts, kparts, dk_own, dv_own = outs
        buffers = (query_grad, dk_own, dv_own)
        piece_q = jnp.sum(qparts, axis=(0, 1))
        piece_k = jnp.sum(kparts, axis=(0, 1)) + jnp.sum(khalo, axis=(0, 1))
        query_part = piece_q if query_part is None else query_part + piece_q
        key_part = piece_k if key_part is None else key_part + piece_k
    back = backs[0] if len(backs) == 1 else jnp.concatenate(backs, axis=1)
    return query_grad, query_part, key_part, back, dk_own, dv_own


def per_device(query_raw, key_raw, value_proj, query_gain, key_gain, out_grad, doc_lengths):
    tok_rows = query_raw.shape[0]
    head_dim = query_gain.shape[0]
    query_heads = query_raw.shape[1] // head_dim
    key_heads = key_raw.shape[1] // head_dim
    first_pos = lax.axis_index("ctx") * tok_rows
    doc_ends = jnp.cumsum(doc_lengths)
    own_pos = first_pos + jnp.arange(tok_rows, dtype=jnp.int32)
    own_doc = doc_index(own_pos, doc_ends)
    halo_raw = first_pos - WINDOW + jnp.arange(WINDOW, dtype=jnp.int32)
    halo_doc = jnp.where(halo_raw >= 0, doc_index(halo_raw, doc_ends), -1)
    n_pieces = 2 if key_heads % 2 == 0 else 1
    width = key_heads * head_dim // n_pieces
    halo_pieces = []
    for piece in range(n_pieces):
        cols = slice(piece * width, (piece + 1) * width)
        send = jnp.concatenate([key_raw[tok_rows - WINDOW:, cols], value_proj[tok_rows - WINDOW:, cols]], axis=1)
        if halo_pieces:
            send = lax.optimization_barrier((send, halo_pieces[-1]))[0]
        halo_pieces.append(shifted(send, "ctx", 1))
    all_doc = jnp.concatenate([halo_doc, own_doc])
    query_grad, query_part, key_part, back, dk_own, dv_own = attention_grads(
        out_grad, halo_pieces, value_proj, own_doc, all_doc, key_heads, head_dim,
        query_raw, query_gain, key_raw, key_gain,
    )
    gain_grads = butterfly_sum(jnp.stack([query_part, key_part]), ("head", "ctx"))
    key_grad, value_grad, _ = kv_final(dk_own, dv_own, back, key_raw, key_gain, key_heads, head_dim)
    return (query_grad, key_grad, value_grad, gain_grads[0], gain_grads[1])


def solution(mesh):
    return jax.shard_map(
        per_device,
        mesh=mesh,
        in_specs=(
            P("ctx", "head"),
            P("ctx", "head"),
            P("ctx", "head"),
            P(),
            P(),
            P("ctx", "head"),
            P(),
        ),
        out_specs=(P("ctx", "head"), P("ctx", "head"), P("ctx", "head"), P(), P()),
        check_vma=False,
    )
```

```python
import functools
import math

import jax
import jax.numpy as jnp
from jax import lax
from jax.experimental import pallas as pl
from jax.experimental.pallas import tpu as pltpu
from jax.sharding import PartitionSpec as P

WINDOW = 1024
QUERY_SCALAR = 168


EPS = 1e-06
BLOCK = 256


def shifted(value, axis, steps):
    count = lax.axis_size(axis)
    leading, last = (max(0, -steps), min(count, count - steps))
    return lax.ppermute(value, axis, [(source, source + steps) for source in range(leading, last)])


def xor_tree(values):
    while len(values) > 1:
        values = [values[i] + values[i + 1] for i in range(0, len(values), 2)]
    return values[0]


def butterfly_sum(value, axes):
    for axis in axes:
        count = lax.axis_size(axis)
        if count & (count - 1):
            value = lax.psum(value, axis)
            continue
        bits = count.bit_length() - 1
        low = 0
        while low < bits:
            width = 1
            shifted_parts = [value]
            for mask in range(1, 1 << width):
                pairs = [(source, source ^ (mask << low)) for source in range(count)]
                shifted_parts.append(lax.ppermute(value, axis, pairs))
            value = xor_tree(shifted_parts)
            low += width
    return value


def norm_rows(raw_rows, head_count):
    values = raw_rows.astype(jnp.float32).reshape(raw_rows.shape[0], head_count, -1)
    inverse = lax.rsqrt(jnp.mean(values * values, axis=-1, keepdims=True) + EPS)
    return (values * inverse, inverse)


def norm_back(raw_rows, gain_vec, head_count, upstream):
    scaled, inverse = norm_rows(raw_rows, head_count)
    incoming = upstream.reshape(scaled.shape)
    weighted = incoming * gain_vec
    inner_sum = jnp.mean(weighted * scaled, axis=-1, keepdims=True)
    result = inverse * (weighted - scaled * inner_sum)
    return (result.reshape(raw_rows.shape), jnp.sum(incoming * scaled, axis=(0, 1)))


def doc_index(positions, doc_ends):
    return jnp.sum((positions[:, None] >= doc_ends[None, :]).astype(jnp.int32), axis=1)


def tile_mask(qdoc_ref, kdoc_ref, q_first, t, group):
    blk = BLOCK
    n_tiles = WINDOW // blk + 1
    rows = lax.broadcasted_iota(jnp.int32, (blk, blk), 0)
    cols = lax.broadcasted_iota(jnp.int32, (blk, blk), 1)
    k_first = q_first + t * blk
    live = qdoc_ref[q_first:q_first + blk, :] == kdoc_ref[:, k_first:k_first + blk]
    if t == 0:
        live = live & (cols > rows)
    if t == n_tiles - 1:
        live = live & (cols + t * blk <= rows + WINDOW)
    return jnp.concatenate([live] * group, axis=0), k_first


def normed_rows(raw, gain):
    inverse = lax.rsqrt(jnp.mean(raw * raw, axis=1, keepdims=True) + EPS)
    return (raw * inverse * gain).astype(jnp.bfloat16)


def normed_stack(ref, gain, group, head_dim, first):
    blk = BLOCK
    return jnp.concatenate(
        [normed_rows(ref[first:first + blk, a * head_dim:(a + 1) * head_dim].astype(jnp.float32), gain)
         for a in range(group)],
        axis=0,
    )


def stacked(ref, group, head_dim, first):
    blk = BLOCK
    return jnp.concatenate(
        [ref[first:first + blk, a * head_dim:(a + 1) * head_dim] for a in range(group)], axis=0
    )


def grad_tile(q_g, do_g, k_tile, v_tile, live, log_sums, delta):
    scale = QUERY_SCALAR ** (-0.5)
    scores = lax.dot_general(q_g, k_tile, (((1,), (1,)), ((), ())), preferred_element_type=jnp.float32) * scale
    weights = jnp.where(live, jnp.exp(scores - log_sums), 0.0)
    d_weights = lax.dot_general(do_g, v_tile, (((1,), (1,)), ((), ())), preferred_element_type=jnp.float32)
    d_scores = (weights * (d_weights - delta)).astype(jnp.bfloat16)
    dq_part = jnp.dot(d_scores, k_tile, preferred_element_type=jnp.float32)
    dk_part = lax.dot_general(d_scores, q_g, (((0,), (0,)), ((), ())), preferred_element_type=jnp.float32)
    dv_part = lax.dot_general(
        weights.astype(jnp.bfloat16), do_g, (((0,), (0,)), ((), ())), preferred_element_type=jnp.float32
    )
    return dq_part, dk_part * scale, dv_part


def halo_kernel(qdoc_ref, kdoc_ref, q_ref, do_ref, hk_ref, hv_ref, kraw_ref, v_ref, kgain_ref, qgain_ref,
                tot_ref, num_ref, *refs, group, head_dim, n_alias):
    dq_ref, dkv_ref, lse_ref, delta_ref, kpart_ref, dk_ref, dv_ref, kn_ref, k_ref = refs[n_alias:]
    blk = BLOCK
    n_tiles = WINDOW // blk + 1
    n_halo = WINDOW // blk
    n_q = q_ref.shape[0] // blk
    gb = group * blk
    scale = QUERY_SCALAR ** (-0.5)
    dk_ref[...] = jnp.zeros(dk_ref.shape, jnp.float32)
    dv_ref[...] = jnp.zeros(dv_ref.shape, jnp.float32)
    halo_raw = hk_ref[...].astype(jnp.float32)
    halo_inv = lax.rsqrt(jnp.mean(halo_raw * halo_raw, axis=1, keepdims=True) + EPS)
    kn_ref[...] = (halo_raw * halo_inv * kgain_ref[...]).astype(jnp.bfloat16)
    k_ref[...] = normed_rows(kraw_ref[...].astype(jnp.float32), kgain_ref[...])
    qgain = qgain_ref[...]

    def key_tile(k_first):
        if k_first < WINDOW:
            return kn_ref[k_first:k_first + blk, :], hv_ref[k_first:k_first + blk, :]
        own_first = k_first - WINDOW
        return k_ref[own_first:own_first + blk, :], v_ref[own_first:own_first + blk, :]

    for qb in range(n_q):
        q_first = qb * blk
        q_g = normed_stack(q_ref, qgain, group, head_dim, q_first)
        do_g = stacked(do_ref, group, head_dim, q_first)
        masks = [tile_mask(qdoc_ref, kdoc_ref, q_first, t, group)[0] for t in range(n_halo - qb)]
        totals = tot_ref[qb * gb:(qb + 1) * gb, :]
        numer = num_ref[qb * gb:(qb + 1) * gb, :]
        for t in range(n_halo - qb):
            k_first = q_first + t * blk
            k_tile, v_tile = key_tile(k_first)
            scores = lax.dot_general(
                q_g, k_tile, (((1,), (1,)), ((), ())), preferred_element_type=jnp.float32
            ) * scale
            exp_s = jnp.where(masks[t], jnp.exp(scores), 0.0)
            totals = totals + jnp.sum(exp_s, axis=1, keepdims=True)
            numer = numer + jnp.dot(exp_s.astype(jnp.bfloat16), v_tile, preferred_element_type=jnp.float32)
        log_sums = jnp.log(totals)
        attn_out = numer / totals
        delta = jnp.sum(do_g.astype(jnp.float32) * attn_out, axis=1, keepdims=True)
        lse_ref[qb * gb:(qb + 1) * gb, :] = log_sums
        delta_ref[qb * gb:(qb + 1) * gb, :] = delta
        dq = jnp.zeros((gb, head_dim), jnp.float32)
        for t in range(n_halo - qb):
            k_first = q_first + t * blk
            k_tile, v_tile = key_tile(k_first)
            dq_part, dk_part, dv_part = grad_tile(q_g, do_g, k_tile, v_tile, masks[t], log_sums, delta)
            dq = dq + dq_part
            dk_ref[k_first:k_first + blk, :] += dk_part
            dv_ref[k_first:k_first + blk, :] += dv_part
        dq_ref[q_first:q_first + blk, :] = jnp.concatenate(
            [dq[a * blk:(a + 1) * blk] for a in range(group)], axis=1
        ) * scale
    dkv_ref[:, :head_dim] = dk_ref[...].astype(jnp.bfloat16)
    dkv_ref[:, head_dim:] = dv_ref[...].astype(jnp.bfloat16)
    halo_hat = halo_raw * halo_inv
    kpart_ref[...] = jnp.sum(dk_ref[...] * halo_hat, axis=0, keepdims=True).reshape(kpart_ref.shape)


def stats_kernel(qdoc_ref, kdoc_ref, q_ref, kraw_ref, v_ref, kgain_ref, qgain_ref, tot_ref, num_ref, k_ref,
                 *, group, head_dim):
    blk = BLOCK
    n_tiles = WINDOW // blk + 1
    n_halo = WINDOW // blk
    n_q = q_ref.shape[0] // blk
    gb = group * blk
    scale = QUERY_SCALAR ** (-0.5)
    k_ref[...] = normed_rows(kraw_ref[...].astype(jnp.float32), kgain_ref[...])
    qgain = qgain_ref[...]
    for qb in range(n_q):
        q_first = qb * blk
        q_g = normed_stack(q_ref, qgain, group, head_dim, q_first)
        totals = jnp.zeros((gb, 1), jnp.float32)
        numer = jnp.zeros((gb, head_dim), jnp.float32)
        for t in range(max(0, n_halo - qb), n_tiles):
            live = tile_mask(qdoc_ref, kdoc_ref, q_first, t, group)[0]
            own_first = q_first + t * blk - WINDOW
            k_tile = k_ref[own_first:own_first + blk, :]
            v_tile = v_ref[own_first:own_first + blk, :]
            scores = lax.dot_general(
                q_g, k_tile, (((1,), (1,)), ((), ())), preferred_element_type=jnp.float32
            ) * scale
            exp_s = jnp.where(live, jnp.exp(scores), 0.0)
            totals = totals + jnp.sum(exp_s, axis=1, keepdims=True)
            numer = numer + jnp.dot(exp_s.astype(jnp.bfloat16), v_tile, preferred_element_type=jnp.float32)
        tot_ref[qb * gb:(qb + 1) * gb, :] = totals
        num_ref[qb * gb:(qb + 1) * gb, :] = numer


def norm_grad(raw, gain, upstream):
    inverse = lax.rsqrt(jnp.mean(raw * raw, axis=1, keepdims=True) + EPS)
    scaled = raw * inverse
    weighted = upstream * gain
    inner_sum = jnp.mean(weighted * scaled, axis=1, keepdims=True)
    result = inverse * (weighted - scaled * inner_sum)
    return result, jnp.sum(upstream * scaled, axis=0, keepdims=True)


def own_kernel(qdoc_ref, kdoc_ref, do_ref, v_ref, lse_ref, delta_ref, dq_in_ref, raw_ref, gain_ref,
               kraw_ref, kgain_ref, qgrad_ref, qgain_ref, kpart_ref, dk_ref, dv_ref, k_ref, *, group, head_dim):
    q_ref = raw_ref
    blk = BLOCK
    n_tiles = WINDOW // blk + 1
    n_halo = WINDOW // blk
    n_q = q_ref.shape[0] // blk
    gb = group * blk
    scale = QUERY_SCALAR ** (-0.5)
    dk_ref[...] = jnp.zeros(dk_ref.shape, jnp.float32)
    dv_ref[...] = jnp.zeros(dv_ref.shape, jnp.float32)
    gain = gain_ref[...]
    k_ref[...] = normed_rows(kraw_ref[...].astype(jnp.float32), kgain_ref[...])
    gain_sum = jnp.zeros((1, head_dim), jnp.float32)
    for qb in range(n_q):
        q_first = qb * blk
        q_g = normed_stack(q_ref, gain, group, head_dim, q_first)
        do_g = stacked(do_ref, group, head_dim, q_first)
        log_sums = lse_ref[qb * gb:(qb + 1) * gb, :]
        delta = delta_ref[qb * gb:(qb + 1) * gb, :]
        dq = jnp.zeros((gb, head_dim), jnp.float32)
        for t in range(max(0, n_halo - qb), n_tiles):
            live, _ = tile_mask(qdoc_ref, kdoc_ref, q_first, t, group)
            k_first = q_first + t * blk
            own_first = k_first - WINDOW
            k_tile = k_ref[own_first:own_first + blk, :]
            v_tile = v_ref[own_first:own_first + blk, :]
            dq_part, dk_part, dv_part = grad_tile(q_g, do_g, k_tile, v_tile, live, log_sums, delta)
            dq = dq + dq_part
            dk_ref[own_first:own_first + blk, :] += dk_part
            dv_ref[own_first:own_first + blk, :] += dv_part
        dq_in = dq_in_ref[q_first:q_first + blk, :]
        raw = raw_ref[q_first:q_first + blk, :].astype(jnp.float32)
        for a in range(group):
            cols = slice(a * head_dim, (a + 1) * head_dim)
            upstream = dq_in[:, cols] + dq[a * blk:(a + 1) * blk] * scale
            result, part = norm_grad(raw[:, cols], gain, upstream)
            qgrad_ref[q_first:q_first + blk, cols] = result.astype(qgrad_ref.dtype)
            gain_sum = gain_sum + part
    qgain_ref[...] = gain_sum.reshape(qgain_ref.shape)
    key_raw = kraw_ref[...].astype(jnp.float32)
    key_hat = key_raw * lax.rsqrt(jnp.mean(key_raw * key_raw, axis=1, keepdims=True) + EPS)
    kpart_ref[...] = jnp.sum(dk_ref[...] * key_hat, axis=0, keepdims=True).reshape(kpart_ref.shape)


def kv_final_kernel(dk_ref, dv_ref, back_ref, raw_ref, gain_ref, kgrad_ref, vgrad_ref, kgain_ref, *, head_dim):
    tok_rows = dk_ref.shape[0]
    lead = tok_rows - WINDOW
    back = back_ref[...].astype(jnp.float32)
    dk = dk_ref[...]
    dv = dv_ref[...]
    if lead:
        dk = jnp.concatenate([dk[:lead], dk[lead:] + back[:, :head_dim]], axis=0)
        dv = jnp.concatenate([dv[:lead], dv[lead:] + back[:, head_dim:]], axis=0)
    else:
        dk = dk + back[:, :head_dim]
        dv = dv + back[:, head_dim:]
    vgrad_ref[...] = dv.astype(vgrad_ref.dtype)
    result, part = norm_grad(raw_ref[...].astype(jnp.float32), gain_ref[...], dk)
    kgrad_ref[...] = result.astype(kgrad_ref.dtype)
    kgain_ref[...] = part.reshape(kgain_ref.shape)


def kv_final(dk_own, dv_own, back, key_raw, key_gain, key_heads, head_dim):
    tok_rows = dk_own.shape[0]
    kv_cols = key_heads * head_dim
    col_spec = pl.BlockSpec((tok_rows, head_dim), lambda h: (0, h))
    return pl.pallas_call(
        functools.partial(kv_final_kernel, head_dim=head_dim),
        grid=(key_heads,),
        in_specs=[
            col_spec,
            col_spec,
            pl.BlockSpec((WINDOW, 2 * head_dim), lambda h: (0, h)),
            col_spec,
            pl.BlockSpec((1, head_dim), lambda h: (0, 0)),
        ],
        out_specs=[col_spec, col_spec, pl.BlockSpec((1, 1, head_dim), lambda h: (h, 0, 0))],
        out_shape=[
            jax.ShapeDtypeStruct((tok_rows, kv_cols), jnp.bfloat16),
            jax.ShapeDtypeStruct((tok_rows, kv_cols), jnp.bfloat16),
            jax.ShapeDtypeStruct((key_heads, 1, head_dim), jnp.float32),
        ],
        compiler_params=pltpu.CompilerParams(dimension_semantics=("arbitrary",)),
    )(dk_own, dv_own, back, key_raw, key_gain.reshape(1, head_dim))


def attention_grads(grad_rows, halo_pieces, value_proj, own_doc, all_doc, key_heads,
                    head_dim, query_raw, query_gain, key_raw, key_gain):
    tok_rows, q_cols = query_raw.shape
    key_rows = WINDOW + tok_rows
    group = q_cols // (key_heads * head_dim)
    blk = BLOCK
    n_q = tok_rows // blk
    n_tiles = WINDOW // blk + 1
    gw = group * head_dim
    kv_cols = key_heads * head_dim
    stat_rows = key_heads * n_q * group * blk
    tile_flops = 2 * (group * blk) * blk * head_dim
    halo_tiles = sum(max(0, WINDOW // blk - qb) for qb in range(n_q))
    own_tiles = n_q * n_tiles - halo_tiles
    n_piece = key_heads // len(halo_pieces)
    params = pltpu.CompilerParams(dimension_semantics=("arbitrary",))
    gain_spec = pl.BlockSpec((1, head_dim), lambda h: (0, 0))
    doc_specs = [pl.BlockSpec((tok_rows, 1), lambda h: (0, 0)), pl.BlockSpec((1, key_rows), lambda h: (0, 0))]
    qdoc, kdoc = own_doc.reshape(tok_rows, 1), all_doc.reshape(1, key_rows)
    qall = pl.BlockSpec((tok_rows, gw), lambda h: (0, h))
    kall = pl.BlockSpec((tok_rows, head_dim), lambda h: (0, h))
    totals, numer = pl.pallas_call(
        functools.partial(stats_kernel, group=group, head_dim=head_dim),
        grid=(key_heads,),
        in_specs=doc_specs + [qall, kall, kall, gain_spec, gain_spec],
        out_specs=[pl.BlockSpec((n_q * group * blk, 1), lambda h: (h, 0)),
                   pl.BlockSpec((n_q * group * blk, head_dim), lambda h: (h, 0))],
        out_shape=[jax.ShapeDtypeStruct((stat_rows, 1), jnp.float32),
                   jax.ShapeDtypeStruct((stat_rows, head_dim), jnp.float32)],
        scratch_shapes=[pltpu.VMEM((tok_rows, head_dim), jnp.bfloat16)],
        compiler_params=params,
        cost_estimate=pl.CostEstimate(
            flops=key_heads * 2 * own_tiles * tile_flops,
            transcendentals=key_heads * own_tiles * group * blk * blk,
            bytes_accessed=2 * tok_rows * q_cols + 2 * 2 * tok_rows * kv_cols + 4 * stat_rows * (head_dim + 1),
        ),
    )(qdoc, kdoc, query_raw, key_raw, value_proj, key_gain.reshape(1, head_dim), query_gain.reshape(1, head_dim))
    received = []
    for send in halo_pieces:
        if received:
            send = lax.optimization_barrier((send, received[-1]))[0]
            received.append(shifted(send, "ctx", 1))
        else:
            received.append(lax.optimization_barrier((shifted(send, "ctx", 1), totals, numer))[0])
    buffers = ()
    kparts = []
    for piece, halo in enumerate(received):
        h0 = piece * n_piece
        qcol = pl.BlockSpec((tok_rows, gw), lambda h, h0=h0: (0, h + h0))
        kcol = pl.BlockSpec((tok_rows, head_dim), lambda h, h0=h0: (0, h + h0))
        hcol = pl.BlockSpec((WINDOW, head_dim), lambda h: (0, h))
        vcol = pl.BlockSpec((WINDOW, head_dim), lambda h, n_piece=n_piece: (0, h + n_piece))
        stat = pl.BlockSpec((n_q * group * blk, 1), lambda h, h0=h0: (h + h0, 0))
        outs = pl.pallas_call(
            functools.partial(halo_kernel, group=group, head_dim=head_dim, n_alias=len(buffers)),
            grid=(n_piece,),
            in_specs=doc_specs + [qcol, qcol, hcol, vcol, kcol, kcol, gain_spec, gain_spec,
                                  pl.BlockSpec((n_q * group * blk, 1), lambda h, h0=h0: (h + h0, 0)),
                                  pl.BlockSpec((n_q * group * blk, head_dim), lambda h, h0=h0: (h + h0, 0))]
            + [pl.BlockSpec(memory_space=pl.ANY)] * len(buffers),
            out_specs=[
                qcol,
                pl.BlockSpec((WINDOW, 2 * head_dim), lambda h, h0=h0: (0, h + h0)),
                stat,
                stat,
                pl.BlockSpec((1, 1, head_dim), lambda h: (h, 0, 0)),
            ],
            out_shape=[
                jax.ShapeDtypeStruct((tok_rows, q_cols), jnp.float32),
                jax.ShapeDtypeStruct((WINDOW, 2 * kv_cols), jnp.bfloat16),
                jax.ShapeDtypeStruct((stat_rows, 1), jnp.float32),
                jax.ShapeDtypeStruct((stat_rows, 1), jnp.float32),
                jax.ShapeDtypeStruct((n_piece, 1, head_dim), jnp.float32),
            ],
            scratch_shapes=[
                pltpu.VMEM((WINDOW, head_dim), jnp.float32),
                pltpu.VMEM((WINDOW, head_dim), jnp.float32),
                pltpu.VMEM((WINDOW, head_dim), jnp.bfloat16),
                pltpu.VMEM((tok_rows, head_dim), jnp.bfloat16),
            ],
            input_output_aliases={12 + i: i for i in range(len(buffers))},
            compiler_params=params,
            cost_estimate=pl.CostEstimate(
                flops=n_piece * (2 * n_q * n_tiles + 5 * halo_tiles) * tile_flops,
                transcendentals=n_piece * (n_q * n_tiles + halo_tiles) * group * blk * blk,
                bytes_accessed=n_piece * (2 * 2 * tok_rows * gw + 2 * 2 * key_rows * head_dim
                                          + 4 * tok_rows * gw + 2 * 2 * WINDOW * head_dim),
            ),
        )(qdoc, kdoc, query_raw, grad_rows, halo, halo, key_raw, value_proj, key_gain.reshape(1, head_dim),
          query_gain.reshape(1, head_dim), totals, numer, *buffers)
        buffers = tuple(outs[:4])
        kparts.append(outs[4])
    dq_half, dkv_halo, log_sums, delta = buffers
    qcol = pl.BlockSpec((tok_rows, gw), lambda h: (0, h))
    kcol = pl.BlockSpec((tok_rows, head_dim), lambda h: (0, h))
    stat = pl.BlockSpec((n_q * group * blk, 1), lambda h: (h, 0))
    part_spec = pl.BlockSpec((1, 1, head_dim), lambda h: (h, 0, 0))
    part_shape = jax.ShapeDtypeStruct((key_heads, 1, head_dim), jnp.float32)
    query_grad, qgain_parts, kown_parts, dk_own, dv_own = pl.pallas_call(
        functools.partial(own_kernel, group=group, head_dim=head_dim),
        grid=(key_heads,),
        in_specs=doc_specs + [qcol, kcol, stat, stat, qcol, qcol, gain_spec, kcol, gain_spec],
        out_specs=[qcol, part_spec, part_spec, kcol, kcol],
        scratch_shapes=[pltpu.VMEM((tok_rows, head_dim), jnp.bfloat16)],
        out_shape=[
            jax.ShapeDtypeStruct((tok_rows, q_cols), jnp.bfloat16),
            part_shape,
            part_shape,
            jax.ShapeDtypeStruct((tok_rows, kv_cols), jnp.float32),
            jax.ShapeDtypeStruct((tok_rows, kv_cols), jnp.float32),
        ],
        compiler_params=params,
        cost_estimate=pl.CostEstimate(
            flops=key_heads * own_tiles * 5 * tile_flops,
            transcendentals=key_heads * own_tiles * group * blk * blk,
            bytes_accessed=2 * 2 * tok_rows * q_cols + 2 * 2 * tok_rows * kv_cols + 2 * 4 * tok_rows * q_cols
            + 2 * 4 * tok_rows * kv_cols,
        ),
    )(qdoc, kdoc, grad_rows, value_proj, log_sums, delta, dq_half, query_raw,
      query_gain.reshape(1, head_dim), key_raw, key_gain.reshape(1, head_dim))
    key_part = jnp.sum(kown_parts, axis=(0, 1))
    for part in kparts:
        key_part = key_part + jnp.sum(part, axis=(0, 1))
    return query_grad, jnp.sum(qgain_parts, axis=(0, 1)), key_part, dkv_halo, dk_own, dv_own


def per_device(query_raw, key_raw, value_proj, query_gain, key_gain, out_grad, doc_lengths):
    tok_rows = query_raw.shape[0]
    head_dim = query_gain.shape[0]
    query_heads = query_raw.shape[1] // head_dim
    key_heads = key_raw.shape[1] // head_dim
    first_pos = lax.axis_index("ctx") * tok_rows
    doc_ends = jnp.cumsum(doc_lengths)
    own_pos = first_pos + jnp.arange(tok_rows, dtype=jnp.int32)
    own_doc = doc_index(own_pos, doc_ends)
    halo_raw = first_pos - WINDOW + jnp.arange(WINDOW, dtype=jnp.int32)
    halo_doc = jnp.where(halo_raw >= 0, doc_index(halo_raw, doc_ends), -1)
    n_pieces = 2 if key_heads % 2 == 0 else 1
    width = key_heads * head_dim // n_pieces
    halo_pieces = []
    for piece in range(n_pieces):
        cols = slice(piece * width, (piece + 1) * width)
        send = jnp.concatenate([key_raw[tok_rows - WINDOW:, cols], value_proj[tok_rows - WINDOW:, cols]], axis=1)
        halo_pieces.append(send)
    all_doc = jnp.concatenate([halo_doc, own_doc])
    query_grad, query_part, key_part, dkv_halo, dk_own, dv_own = attention_grads(
        out_grad, halo_pieces, value_proj, own_doc, all_doc, key_heads, head_dim,
        query_raw, query_gain, key_raw, key_gain,
    )
    gain_grads = butterfly_sum(jnp.stack([query_part, key_part]), ("head", "ctx"))
    back = shifted(dkv_halo, "ctx", -1)
    key_grad, value_grad, _ = kv_final(dk_own, dv_own, back, key_raw, key_gain, key_heads, head_dim)
    return (query_grad, key_grad, value_grad, gain_grads[0], gain_grads[1])


def solution(mesh):
    return jax.shard_map(
        per_device,
        mesh=mesh,
        in_specs=(
            P("ctx", "head"),
            P("ctx", "head"),
            P("ctx", "head"),
            P(),
            P(),
            P("ctx", "head"),
            P(),
        ),
        out_specs=(P("ctx", "head"), P("ctx", "head"), P("ctx", "head"), P(), P()),
        check_vma=False,
    )
```

```python
import functools
import math

import jax
import jax.numpy as jnp
from jax import lax
from jax.experimental import pallas as pl
from jax.experimental.pallas import tpu as pltpu
from jax.sharding import PartitionSpec as P

WINDOW = 1024
QUERY_SCALAR = 168


EPS = 1e-06
BLOCK = 256


def shifted(value, axis, steps):
    count = lax.axis_size(axis)
    leading, last = (max(0, -steps), min(count, count - steps))
    return lax.ppermute(value, axis, [(source, source + steps) for source in range(leading, last)])


def xor_tree(values):
    while len(values) > 1:
        values = [values[i] + values[i + 1] for i in range(0, len(values), 2)]
    return values[0]


def butterfly_sum(value, axes):
    for axis in axes:
        count = lax.axis_size(axis)
        if count & (count - 1):
            value = lax.psum(value, axis)
            continue
        bits = count.bit_length() - 1
        low = 0
        while low < bits:
            width = 1
            shifted_parts = [value]
            for mask in range(1, 1 << width):
                pairs = [(source, source ^ (mask << low)) for source in range(count)]
                shifted_parts.append(lax.ppermute(value, axis, pairs))
            value = xor_tree(shifted_parts)
            low += width
    return value


def norm_rows(raw_rows, head_count):
    values = raw_rows.astype(jnp.float32).reshape(raw_rows.shape[0], head_count, -1)
    inverse = lax.rsqrt(jnp.mean(values * values, axis=-1, keepdims=True) + EPS)
    return (values * inverse, inverse)


def norm_back(raw_rows, gain_vec, head_count, upstream):
    scaled, inverse = norm_rows(raw_rows, head_count)
    incoming = upstream.reshape(scaled.shape)
    weighted = incoming * gain_vec
    inner_sum = jnp.mean(weighted * scaled, axis=-1, keepdims=True)
    result = inverse * (weighted - scaled * inner_sum)
    return (result.reshape(raw_rows.shape), jnp.sum(incoming * scaled, axis=(0, 1)))


def doc_index(positions, doc_ends):
    return jnp.sum((positions[:, None] >= doc_ends[None, :]).astype(jnp.int32), axis=1)


def tile_mask(qdoc_ref, kdoc_ref, q_first, t, group):
    blk = BLOCK
    n_tiles = WINDOW // blk + 1
    rows = lax.broadcasted_iota(jnp.int32, (blk, blk), 0)
    cols = lax.broadcasted_iota(jnp.int32, (blk, blk), 1)
    k_first = q_first + t * blk
    live = qdoc_ref[q_first:q_first + blk, :] == kdoc_ref[:, k_first:k_first + blk]
    if t == 0:
        live = live & (cols > rows)
    if t == n_tiles - 1:
        live = live & (cols + t * blk <= rows + WINDOW)
    return jnp.concatenate([live] * group, axis=0), k_first


def normed_rows(raw, gain):
    inverse = lax.rsqrt(jnp.mean(raw * raw, axis=1, keepdims=True) + EPS)
    return (raw * inverse * gain).astype(jnp.bfloat16)


def normed_stack(ref, gain, group, head_dim, first):
    blk = BLOCK
    return jnp.concatenate(
        [normed_rows(ref[first:first + blk, a * head_dim:(a + 1) * head_dim].astype(jnp.float32), gain)
         for a in range(group)],
        axis=0,
    )


def stacked(ref, group, head_dim, first):
    blk = BLOCK
    return jnp.concatenate(
        [ref[first:first + blk, a * head_dim:(a + 1) * head_dim] for a in range(group)], axis=0
    )


def grad_tile(q_g, do_g, k_tile, v_tile, live, log_sums, delta):
    scale = QUERY_SCALAR ** (-0.5)
    scores = lax.dot_general(q_g, k_tile, (((1,), (1,)), ((), ())), preferred_element_type=jnp.float32) * scale
    weights = jnp.where(live, jnp.exp(scores - log_sums), 0.0)
    d_weights = lax.dot_general(do_g, v_tile, (((1,), (1,)), ((), ())), preferred_element_type=jnp.float32)
    d_scores = (weights * (d_weights - delta)).astype(jnp.bfloat16)
    dq_part = jnp.dot(d_scores, k_tile, preferred_element_type=jnp.float32)
    dk_part = lax.dot_general(d_scores, q_g, (((0,), (0,)), ((), ())), preferred_element_type=jnp.float32)
    dv_part = lax.dot_general(
        weights.astype(jnp.bfloat16), do_g, (((0,), (0,)), ((), ())), preferred_element_type=jnp.float32
    )
    return dq_part, dk_part * scale, dv_part


def halo_kernel(qdoc_ref, kdoc_ref, q_ref, do_ref, hk_ref, hv_ref, kraw_ref, v_ref, kgain_ref, qgain_ref, *refs,
                group, head_dim, n_alias):
    dq_ref, dkv_ref, lse_ref, delta_ref, kpart_ref, dk_ref, dv_ref, kn_ref, k_ref = refs[n_alias:]
    blk = BLOCK
    n_tiles = WINDOW // blk + 1
    n_halo = WINDOW // blk
    n_q = q_ref.shape[0] // blk
    gb = group * blk
    scale = QUERY_SCALAR ** (-0.5)
    dk_ref[...] = jnp.zeros(dk_ref.shape, jnp.float32)
    dv_ref[...] = jnp.zeros(dv_ref.shape, jnp.float32)
    halo_raw = hk_ref[...].astype(jnp.float32)
    halo_inv = lax.rsqrt(jnp.mean(halo_raw * halo_raw, axis=1, keepdims=True) + EPS)
    kn_ref[...] = (halo_raw * halo_inv * kgain_ref[...]).astype(jnp.bfloat16)
    k_ref[...] = normed_rows(kraw_ref[...].astype(jnp.float32), kgain_ref[...])
    qgain = qgain_ref[...]

    def key_tile(k_first):
        if k_first < WINDOW:
            return kn_ref[k_first:k_first + blk, :], hv_ref[k_first:k_first + blk, :]
        own_first = k_first - WINDOW
        return k_ref[own_first:own_first + blk, :], v_ref[own_first:own_first + blk, :]

    for qb in range(n_q):
        q_first = qb * blk
        q_g = normed_stack(q_ref, qgain, group, head_dim, q_first)
        do_g = stacked(do_ref, group, head_dim, q_first)
        masks = [tile_mask(qdoc_ref, kdoc_ref, q_first, t, group)[0] for t in range(n_tiles)]
        totals = jnp.zeros((gb, 1), jnp.float32)
        numer = jnp.zeros((gb, head_dim), jnp.float32)
        for t in range(n_tiles):
            k_first = q_first + t * blk
            k_tile, v_tile = key_tile(k_first)
            scores = lax.dot_general(
                q_g, k_tile, (((1,), (1,)), ((), ())), preferred_element_type=jnp.float32
            ) * scale
            exp_s = jnp.where(masks[t], jnp.exp(scores), 0.0)
            totals = totals + jnp.sum(exp_s, axis=1, keepdims=True)
            numer = numer + jnp.dot(exp_s.astype(jnp.bfloat16), v_tile, preferred_element_type=jnp.float32)
        log_sums = jnp.log(totals)
        attn_out = numer / totals
        delta = jnp.sum(do_g.astype(jnp.float32) * attn_out, axis=1, keepdims=True)
        lse_ref[qb * gb:(qb + 1) * gb, :] = log_sums
        delta_ref[qb * gb:(qb + 1) * gb, :] = delta
        dq = jnp.zeros((gb, head_dim), jnp.float32)
        for t in range(n_halo - qb):
            k_first = q_first + t * blk
            k_tile, v_tile = key_tile(k_first)
            dq_part, dk_part, dv_part = grad_tile(q_g, do_g, k_tile, v_tile, masks[t], log_sums, delta)
            dq = dq + dq_part
            dk_ref[k_first:k_first + blk, :] += dk_part
            dv_ref[k_first:k_first + blk, :] += dv_part
        dq_ref[q_first:q_first + blk, :] = jnp.concatenate(
            [dq[a * blk:(a + 1) * blk] for a in range(group)], axis=1
        ) * scale
    dkv_ref[:, :head_dim] = dk_ref[...].astype(jnp.bfloat16)
    dkv_ref[:, head_dim:] = dv_ref[...].astype(jnp.bfloat16)
    halo_hat = halo_raw * halo_inv
    kpart_ref[...] = jnp.sum(dk_ref[...] * halo_hat, axis=0, keepdims=True).reshape(kpart_ref.shape)


def norm_grad(raw, gain, upstream):
    inverse = lax.rsqrt(jnp.mean(raw * raw, axis=1, keepdims=True) + EPS)
    scaled = raw * inverse
    weighted = upstream * gain
    inner_sum = jnp.mean(weighted * scaled, axis=1, keepdims=True)
    result = inverse * (weighted - scaled * inner_sum)
    return result, jnp.sum(upstream * scaled, axis=0, keepdims=True)


def own_kernel(qdoc_ref, kdoc_ref, do_ref, v_ref, lse_ref, delta_ref, dq_in_ref, raw_ref, gain_ref,
               kraw_ref, kgain_ref, qgrad_ref, qgain_ref, kpart_ref, dk_ref, dv_ref, k_ref, *, group, head_dim):
    q_ref = raw_ref
    blk = BLOCK
    n_tiles = WINDOW // blk + 1
    n_halo = WINDOW // blk
    n_q = q_ref.shape[0] // blk
    gb = group * blk
    scale = QUERY_SCALAR ** (-0.5)
    dk_ref[...] = jnp.zeros(dk_ref.shape, jnp.float32)
    dv_ref[...] = jnp.zeros(dv_ref.shape, jnp.float32)
    gain = gain_ref[...]
    k_ref[...] = normed_rows(kraw_ref[...].astype(jnp.float32), kgain_ref[...])
    gain_sum = jnp.zeros((1, head_dim), jnp.float32)
    for qb in range(n_q):
        q_first = qb * blk
        q_g = normed_stack(q_ref, gain, group, head_dim, q_first)
        do_g = stacked(do_ref, group, head_dim, q_first)
        log_sums = lse_ref[qb * gb:(qb + 1) * gb, :]
        delta = delta_ref[qb * gb:(qb + 1) * gb, :]
        dq = jnp.zeros((gb, head_dim), jnp.float32)
        for t in range(max(0, n_halo - qb), n_tiles):
            live, _ = tile_mask(qdoc_ref, kdoc_ref, q_first, t, group)
            k_first = q_first + t * blk
            own_first = k_first - WINDOW
            k_tile = k_ref[own_first:own_first + blk, :]
            v_tile = v_ref[own_first:own_first + blk, :]
            dq_part, dk_part, dv_part = grad_tile(q_g, do_g, k_tile, v_tile, live, log_sums, delta)
            dq = dq + dq_part
            dk_ref[own_first:own_first + blk, :] += dk_part
            dv_ref[own_first:own_first + blk, :] += dv_part
        dq_in = dq_in_ref[q_first:q_first + blk, :]
        raw = raw_ref[q_first:q_first + blk, :].astype(jnp.float32)
        for a in range(group):
            cols = slice(a * head_dim, (a + 1) * head_dim)
            upstream = dq_in[:, cols] + dq[a * blk:(a + 1) * blk] * scale
            result, part = norm_grad(raw[:, cols], gain, upstream)
            qgrad_ref[q_first:q_first + blk, cols] = result.astype(qgrad_ref.dtype)
            gain_sum = gain_sum + part
    qgain_ref[...] = gain_sum.reshape(qgain_ref.shape)
    key_raw = kraw_ref[...].astype(jnp.float32)
    key_hat = key_raw * lax.rsqrt(jnp.mean(key_raw * key_raw, axis=1, keepdims=True) + EPS)
    kpart_ref[...] = jnp.sum(dk_ref[...] * key_hat, axis=0, keepdims=True).reshape(kpart_ref.shape)


def kv_final_kernel(dk_ref, dv_ref, back_ref, raw_ref, gain_ref, kgrad_ref, vgrad_ref, kgain_ref, *, head_dim, lead):
    back = back_ref[...].astype(jnp.float32)
    dk = dk_ref[...]
    dv = dv_ref[...]
    if lead:
        dk = jnp.concatenate([dk[:lead], dk[lead:] + back[:, :head_dim]], axis=0)
        dv = jnp.concatenate([dv[:lead], dv[lead:] + back[:, head_dim:]], axis=0)
    else:
        dk = dk + back[:, :head_dim]
        dv = dv + back[:, head_dim:]
    vgrad_ref[...] = dv.astype(vgrad_ref.dtype)
    result, part = norm_grad(raw_ref[...].astype(jnp.float32), gain_ref[...], dk)
    kgrad_ref[...] = result.astype(kgrad_ref.dtype)
    kgain_ref[...] = part.reshape(kgain_ref.shape)


def kv_final(dk_own, dv_own, back, key_raw, key_gain, key_heads, head_dim):
    tok_rows = dk_own.shape[0]
    kv_cols = key_heads * head_dim
    splits = 2 if tok_rows == WINDOW and tok_rows % (2 * BLOCK) == 0 else 1
    rows = tok_rows // splits
    col_spec = pl.BlockSpec((rows, head_dim), lambda h, r: (r, h))
    back_rows = WINDOW // splits
    return pl.pallas_call(
        functools.partial(kv_final_kernel, head_dim=head_dim, lead=tok_rows - WINDOW),
        grid=(key_heads, splits),
        in_specs=[
            col_spec,
            col_spec,
            pl.BlockSpec((back_rows, 2 * head_dim), lambda h, r: (r, h)),
            col_spec,
            pl.BlockSpec((1, head_dim), lambda h, r: (0, 0)),
        ],
        out_specs=[col_spec, col_spec,
                   pl.BlockSpec((1, 1, head_dim), lambda h, r, splits=splits: (h * splits + r, 0, 0))],
        out_shape=[
            jax.ShapeDtypeStruct((tok_rows, kv_cols), jnp.bfloat16),
            jax.ShapeDtypeStruct((tok_rows, kv_cols), jnp.bfloat16),
            jax.ShapeDtypeStruct((key_heads * splits, 1, head_dim), jnp.float32),
        ],
        compiler_params=pltpu.CompilerParams(dimension_semantics=("arbitrary", "arbitrary")),
    )(dk_own, dv_own, back, key_raw, key_gain.reshape(1, head_dim))


def attention_grads(grad_rows, halo_pieces, value_proj, own_doc, all_doc, key_heads,
                    head_dim, query_raw, query_gain, key_raw, key_gain):
    tok_rows, q_cols = query_raw.shape
    key_rows = WINDOW + tok_rows
    group = q_cols // (key_heads * head_dim)
    blk = BLOCK
    n_q = tok_rows // blk
    n_tiles = WINDOW // blk + 1
    gw = group * head_dim
    kv_cols = key_heads * head_dim
    stat_rows = key_heads * n_q * group * blk
    tile_flops = 2 * (group * blk) * blk * head_dim
    halo_tiles = sum(max(0, WINDOW // blk - qb) for qb in range(n_q))
    own_tiles = n_q * n_tiles - halo_tiles
    n_piece = key_heads // len(halo_pieces)
    params = pltpu.CompilerParams(dimension_semantics=("arbitrary",))
    gain_spec = pl.BlockSpec((1, head_dim), lambda h: (0, 0))
    doc_specs = [pl.BlockSpec((tok_rows, 1), lambda h: (0, 0)), pl.BlockSpec((1, key_rows), lambda h: (0, 0))]
    qdoc, kdoc = own_doc.reshape(tok_rows, 1), all_doc.reshape(1, key_rows)
    buffers = ()
    kparts = []
    for piece, halo in enumerate(halo_pieces):
        h0 = piece * n_piece
        qcol = pl.BlockSpec((tok_rows, gw), lambda h, h0=h0: (0, h + h0))
        kcol = pl.BlockSpec((tok_rows, head_dim), lambda h, h0=h0: (0, h + h0))
        hcol = pl.BlockSpec((WINDOW, head_dim), lambda h: (0, h))
        vcol = pl.BlockSpec((WINDOW, head_dim), lambda h, n_piece=n_piece: (0, h + n_piece))
        stat = pl.BlockSpec((n_q * group * blk, 1), lambda h, h0=h0: (h + h0, 0))
        outs = pl.pallas_call(
            functools.partial(halo_kernel, group=group, head_dim=head_dim, n_alias=len(buffers)),
            grid=(n_piece,),
            in_specs=doc_specs + [qcol, qcol, hcol, vcol, kcol, kcol, gain_spec, gain_spec]
            + [pl.BlockSpec(memory_space=pl.ANY)] * len(buffers),
            out_specs=[
                qcol,
                pl.BlockSpec((WINDOW, 2 * head_dim), lambda h, h0=h0: (0, h + h0)),
                stat,
                stat,
                pl.BlockSpec((1, 1, head_dim), lambda h: (h, 0, 0)),
            ],
            out_shape=[
                jax.ShapeDtypeStruct((tok_rows, q_cols), jnp.float32),
                jax.ShapeDtypeStruct((WINDOW, 2 * kv_cols), jnp.bfloat16),
                jax.ShapeDtypeStruct((stat_rows, 1), jnp.float32),
                jax.ShapeDtypeStruct((stat_rows, 1), jnp.float32),
                jax.ShapeDtypeStruct((n_piece, 1, head_dim), jnp.float32),
            ],
            scratch_shapes=[
                pltpu.VMEM((WINDOW, head_dim), jnp.float32),
                pltpu.VMEM((WINDOW, head_dim), jnp.float32),
                pltpu.VMEM((WINDOW, head_dim), jnp.bfloat16),
                pltpu.VMEM((tok_rows, head_dim), jnp.bfloat16),
            ],
            input_output_aliases={10 + i: i for i in range(len(buffers))},
            compiler_params=params,
            cost_estimate=pl.CostEstimate(
                flops=n_piece * (2 * n_q * n_tiles + 5 * halo_tiles) * tile_flops,
                transcendentals=n_piece * (n_q * n_tiles + halo_tiles) * group * blk * blk,
                bytes_accessed=n_piece * (2 * 2 * tok_rows * gw + 2 * 2 * key_rows * head_dim
                                          + 4 * tok_rows * gw + 2 * 2 * WINDOW * head_dim),
            ),
        )(qdoc, kdoc, query_raw, grad_rows, halo, halo, key_raw, value_proj, key_gain.reshape(1, head_dim),
          query_gain.reshape(1, head_dim), *buffers)
        buffers = tuple(outs[:4])
        kparts.append(outs[4])
    dq_half, dkv_halo, log_sums, delta = buffers
    qcol = pl.BlockSpec((tok_rows, gw), lambda h: (0, h))
    kcol = pl.BlockSpec((tok_rows, head_dim), lambda h: (0, h))
    stat = pl.BlockSpec((n_q * group * blk, 1), lambda h: (h, 0))
    part_spec = pl.BlockSpec((1, 1, head_dim), lambda h: (h, 0, 0))
    part_shape = jax.ShapeDtypeStruct((key_heads, 1, head_dim), jnp.float32)
    query_grad, qgain_parts, kown_parts, dk_own, dv_own = pl.pallas_call(
        functools.partial(own_kernel, group=group, head_dim=head_dim),
        grid=(key_heads,),
        in_specs=doc_specs + [qcol, kcol, stat, stat, qcol, qcol, gain_spec, kcol, gain_spec],
        out_specs=[qcol, part_spec, part_spec, kcol, kcol],
        scratch_shapes=[pltpu.VMEM((tok_rows, head_dim), jnp.bfloat16)],
        out_shape=[
            jax.ShapeDtypeStruct((tok_rows, q_cols), jnp.bfloat16),
            part_shape,
            part_shape,
            jax.ShapeDtypeStruct((tok_rows, kv_cols), jnp.float32),
            jax.ShapeDtypeStruct((tok_rows, kv_cols), jnp.float32),
        ],
        compiler_params=params,
        cost_estimate=pl.CostEstimate(
            flops=key_heads * own_tiles * 5 * tile_flops,
            transcendentals=key_heads * own_tiles * group * blk * blk,
            bytes_accessed=2 * 2 * tok_rows * q_cols + 2 * 2 * tok_rows * kv_cols + 2 * 4 * tok_rows * q_cols
            + 2 * 4 * tok_rows * kv_cols,
        ),
    )(qdoc, kdoc, grad_rows, value_proj, log_sums, delta, dq_half, query_raw,
      query_gain.reshape(1, head_dim), key_raw, key_gain.reshape(1, head_dim))
    key_part = jnp.sum(kown_parts, axis=(0, 1))
    for part in kparts:
        key_part = key_part + jnp.sum(part, axis=(0, 1))
    return query_grad, jnp.sum(qgain_parts, axis=(0, 1)), key_part, dkv_halo, dk_own, dv_own


def per_device(query_raw, key_raw, value_proj, query_gain, key_gain, out_grad, doc_lengths):
    tok_rows = query_raw.shape[0]
    head_dim = query_gain.shape[0]
    query_heads = query_raw.shape[1] // head_dim
    key_heads = key_raw.shape[1] // head_dim
    first_pos = lax.axis_index("ctx") * tok_rows
    doc_ends = jnp.cumsum(doc_lengths)
    own_pos = first_pos + jnp.arange(tok_rows, dtype=jnp.int32)
    own_doc = doc_index(own_pos, doc_ends)
    halo_raw = first_pos - WINDOW + jnp.arange(WINDOW, dtype=jnp.int32)
    halo_doc = jnp.where(halo_raw >= 0, doc_index(halo_raw, doc_ends), -1)
    n_pieces = 2 if key_heads % 2 == 0 else 1
    width = key_heads * head_dim // n_pieces
    halo_pieces = []
    for piece in range(n_pieces):
        cols = slice(piece * width, (piece + 1) * width)
        send = jnp.concatenate([key_raw[tok_rows - WINDOW:, cols], value_proj[tok_rows - WINDOW:, cols]], axis=1)
        if halo_pieces:
            send = lax.optimization_barrier((send, halo_pieces[-1]))[0]
        halo_pieces.append(shifted(send, "ctx", 1))
    all_doc = jnp.concatenate([halo_doc, own_doc])
    query_grad, query_part, key_part, dkv_halo, dk_own, dv_own = attention_grads(
        out_grad, halo_pieces, value_proj, own_doc, all_doc, key_heads, head_dim,
        query_raw, query_gain, key_raw, key_gain,
    )
    gain_grads = butterfly_sum(jnp.stack([query_part, key_part]), ("head", "ctx"))
    back = shifted(dkv_halo, "ctx", -1)
    key_grad, value_grad, _ = kv_final(dk_own, dv_own, back, key_raw, key_gain, key_heads, head_dim)
    return (query_grad, key_grad, value_grad, gain_grads[0], gain_grads[1])


def solution(mesh):
    return jax.shard_map(
        per_device,
        mesh=mesh,
        in_specs=(
            P("ctx", "head"),
            P("ctx", "head"),
            P("ctx", "head"),
            P(),
            P(),
            P("ctx", "head"),
            P(),
        ),
        out_specs=(P("ctx", "head"), P("ctx", "head"), P("ctx", "head"), P(), P()),
        check_vma=False,
    )
```

```python
import functools
import math

import jax
import jax.numpy as jnp
from jax import lax
from jax.experimental import pallas as pl
from jax.experimental.pallas import tpu as pltpu
from jax.sharding import PartitionSpec as P

WINDOW = 1024
QUERY_SCALAR = 168


EPS = 1e-06
BLOCK = 256


def shifted(value, axis, steps):
    count = lax.axis_size(axis)
    leading, last = (max(0, -steps), min(count, count - steps))
    return lax.ppermute(value, axis, [(source, source + steps) for source in range(leading, last)])


def xor_tree(values):
    while len(values) > 1:
        values = [values[i] + values[i + 1] for i in range(0, len(values), 2)]
    return values[0]


def butterfly_sum(value, axes):
    for axis in axes:
        count = lax.axis_size(axis)
        if count & (count - 1):
            value = lax.psum(value, axis)
            continue
        bits = count.bit_length() - 1
        low = 0
        while low < bits:
            width = 1
            shifted_parts = [value]
            for mask in range(1, 1 << width):
                pairs = [(source, source ^ (mask << low)) for source in range(count)]
                shifted_parts.append(lax.ppermute(value, axis, pairs))
            value = xor_tree(shifted_parts)
            low += width
    return value


def norm_rows(raw_rows, head_count):
    values = raw_rows.astype(jnp.float32).reshape(raw_rows.shape[0], head_count, -1)
    inverse = lax.rsqrt(jnp.mean(values * values, axis=-1, keepdims=True) + EPS)
    return (values * inverse, inverse)


def norm_back(raw_rows, gain_vec, head_count, upstream):
    scaled, inverse = norm_rows(raw_rows, head_count)
    incoming = upstream.reshape(scaled.shape)
    weighted = incoming * gain_vec
    inner_sum = jnp.mean(weighted * scaled, axis=-1, keepdims=True)
    result = inverse * (weighted - scaled * inner_sum)
    return (result.reshape(raw_rows.shape), jnp.sum(incoming * scaled, axis=(0, 1)))


def doc_index(positions, doc_ends):
    return jnp.sum((positions[:, None] >= doc_ends[None, :]).astype(jnp.int32), axis=1)


def tile_mask(qdoc_ref, kdoc_ref, q_first, t, group):
    blk = BLOCK
    n_tiles = WINDOW // blk + 1
    rows = lax.broadcasted_iota(jnp.int32, (blk, blk), 0)
    cols = lax.broadcasted_iota(jnp.int32, (blk, blk), 1)
    k_first = q_first + t * blk
    live = qdoc_ref[q_first:q_first + blk, :] == kdoc_ref[:, k_first:k_first + blk]
    if t == 0:
        live = live & (cols > rows)
    if t == n_tiles - 1:
        live = live & (cols + t * blk <= rows + WINDOW)
    return jnp.concatenate([live] * group, axis=0), k_first


def normed_rows(raw, gain):
    inverse = lax.rsqrt(jnp.mean(raw * raw, axis=1, keepdims=True) + EPS)
    return (raw * inverse * gain).astype(jnp.bfloat16)


def normed_stack(ref, gain, group, head_dim, first):
    blk = BLOCK
    return jnp.concatenate(
        [normed_rows(ref[first:first + blk, a * head_dim:(a + 1) * head_dim].astype(jnp.float32), gain)
         for a in range(group)],
        axis=0,
    )


def stacked(ref, group, head_dim, first):
    blk = BLOCK
    return jnp.concatenate(
        [ref[first:first + blk, a * head_dim:(a + 1) * head_dim] for a in range(group)], axis=0
    )


def grad_tile(q_g, do_g, k_tile, v_tile, live, log_sums, delta):
    scale = QUERY_SCALAR ** (-0.5)
    scores = lax.dot_general(q_g, k_tile, (((1,), (1,)), ((), ())), preferred_element_type=jnp.float32) * scale
    weights = jnp.where(live, jnp.exp(scores - log_sums), 0.0)
    d_weights = lax.dot_general(do_g, v_tile, (((1,), (1,)), ((), ())), preferred_element_type=jnp.float32)
    d_scores = (weights * (d_weights - delta)).astype(jnp.bfloat16)
    dq_part = jnp.dot(d_scores, k_tile, preferred_element_type=jnp.float32)
    dk_part = lax.dot_general(d_scores, q_g, (((0,), (0,)), ((), ())), preferred_element_type=jnp.float32)
    dv_part = lax.dot_general(
        weights.astype(jnp.bfloat16), do_g, (((0,), (0,)), ((), ())), preferred_element_type=jnp.float32
    )
    return dq_part, dk_part * scale, dv_part


def halo_kernel(qdoc_ref, kdoc_ref, q_ref, do_ref, hk_ref, hv_ref, kraw_ref, v_ref, kgain_ref, qgain_ref, *refs,
                group, head_dim, n_alias):
    dq_ref, dkv_ref, lse_ref, delta_ref, kpart_ref, dk_ref, dv_ref, kn_ref, k_ref = refs[n_alias:]
    blk = BLOCK
    n_tiles = WINDOW // blk + 1
    n_halo = WINDOW // blk
    n_q = q_ref.shape[0] // blk
    gb = group * blk
    scale = QUERY_SCALAR ** (-0.5)
    dk_ref[...] = jnp.zeros(dk_ref.shape, jnp.float32)
    dv_ref[...] = jnp.zeros(dv_ref.shape, jnp.float32)
    halo_raw = hk_ref[...].astype(jnp.float32)
    halo_inv = lax.rsqrt(jnp.mean(halo_raw * halo_raw, axis=1, keepdims=True) + EPS)
    kn_ref[...] = (halo_raw * halo_inv * kgain_ref[...]).astype(jnp.bfloat16)
    k_ref[...] = normed_rows(kraw_ref[...].astype(jnp.float32), kgain_ref[...])
    qgain = qgain_ref[...]

    def key_tile(k_first):
        if k_first < WINDOW:
            return kn_ref[k_first:k_first + blk, :], hv_ref[k_first:k_first + blk, :]
        own_first = k_first - WINDOW
        return k_ref[own_first:own_first + blk, :], v_ref[own_first:own_first + blk, :]

    for qb in range(n_q):
        q_first = qb * blk
        q_g = normed_stack(q_ref, qgain, group, head_dim, q_first)
        do_g = stacked(do_ref, group, head_dim, q_first)
        totals = jnp.zeros((gb, 1), jnp.float32)
        numer = jnp.zeros((gb, head_dim), jnp.float32)
        for t in range(n_tiles):
            k_first = q_first + t * blk
            k_tile, v_tile = key_tile(k_first)
            scores = lax.dot_general(
                q_g, k_tile, (((1,), (1,)), ((), ())), preferred_element_type=jnp.float32
            ) * scale
            exp_s = jnp.where(tile_mask(qdoc_ref, kdoc_ref, q_first, t, group)[0], jnp.exp(scores), 0.0)
            totals = totals + jnp.sum(exp_s, axis=1, keepdims=True)
            numer = numer + jnp.dot(exp_s.astype(jnp.bfloat16), v_tile, preferred_element_type=jnp.float32)
        log_sums = jnp.log(totals)
        attn_out = numer / totals
        delta = jnp.sum(do_g.astype(jnp.float32) * attn_out, axis=1, keepdims=True)
        lse_ref[qb * gb:(qb + 1) * gb, :] = log_sums
        delta_ref[qb * gb:(qb + 1) * gb, :] = delta
        dq = jnp.zeros((gb, head_dim), jnp.float32)
        for t in range(n_halo - qb):
            k_first = q_first + t * blk
            k_tile, v_tile = key_tile(k_first)
            live = tile_mask(qdoc_ref, kdoc_ref, q_first, t, group)[0]
            dq_part, dk_part, dv_part = grad_tile(q_g, do_g, k_tile, v_tile, live, log_sums, delta)
            dq = dq + dq_part
            dk_ref[k_first:k_first + blk, :] += dk_part
            dv_ref[k_first:k_first + blk, :] += dv_part
        dq_ref[q_first:q_first + blk, :] = jnp.concatenate(
            [dq[a * blk:(a + 1) * blk] for a in range(group)], axis=1
        ) * scale
    dkv_ref[:, :head_dim] = dk_ref[...].astype(jnp.bfloat16)
    dkv_ref[:, head_dim:] = dv_ref[...].astype(jnp.bfloat16)
    halo_hat = halo_raw * halo_inv
    kpart_ref[...] = jnp.sum(dk_ref[...] * halo_hat, axis=0, keepdims=True).reshape(kpart_ref.shape)


def norm_grad(raw, gain, upstream):
    inverse = lax.rsqrt(jnp.mean(raw * raw, axis=1, keepdims=True) + EPS)
    scaled = raw * inverse
    weighted = upstream * gain
    inner_sum = jnp.mean(weighted * scaled, axis=1, keepdims=True)
    result = inverse * (weighted - scaled * inner_sum)
    return result, jnp.sum(upstream * scaled, axis=0, keepdims=True)


def own_kernel(qdoc_ref, kdoc_ref, do_ref, v_ref, lse_ref, delta_ref, dq_in_ref, raw_ref, gain_ref,
               kraw_ref, kgain_ref, qgrad_ref, qgain_ref, kpart_ref, dk_ref, dv_ref, k_ref, *, group, head_dim):
    q_ref = raw_ref
    blk = BLOCK
    n_tiles = WINDOW // blk + 1
    n_halo = WINDOW // blk
    n_q = q_ref.shape[0] // blk
    gb = group * blk
    scale = QUERY_SCALAR ** (-0.5)
    dk_ref[...] = jnp.zeros(dk_ref.shape, jnp.float32)
    dv_ref[...] = jnp.zeros(dv_ref.shape, jnp.float32)
    gain = gain_ref[...]
    k_ref[...] = normed_rows(kraw_ref[...].astype(jnp.float32), kgain_ref[...])
    gain_sum = jnp.zeros((1, head_dim), jnp.float32)
    for qb in range(n_q):
        q_first = qb * blk
        q_g = normed_stack(q_ref, gain, group, head_dim, q_first)
        do_g = stacked(do_ref, group, head_dim, q_first)
        log_sums = lse_ref[qb * gb:(qb + 1) * gb, :]
        delta = delta_ref[qb * gb:(qb + 1) * gb, :]
        dq = jnp.zeros((gb, head_dim), jnp.float32)
        for t in range(max(0, n_halo - qb), n_tiles):
            live, _ = tile_mask(qdoc_ref, kdoc_ref, q_first, t, group)
            k_first = q_first + t * blk
            own_first = k_first - WINDOW
            k_tile = k_ref[own_first:own_first + blk, :]
            v_tile = v_ref[own_first:own_first + blk, :]
            dq_part, dk_part, dv_part = grad_tile(q_g, do_g, k_tile, v_tile, live, log_sums, delta)
            dq = dq + dq_part
            dk_ref[own_first:own_first + blk, :] += dk_part
            dv_ref[own_first:own_first + blk, :] += dv_part
        dq_in = dq_in_ref[q_first:q_first + blk, :]
        raw = raw_ref[q_first:q_first + blk, :].astype(jnp.float32)
        for a in range(group):
            cols = slice(a * head_dim, (a + 1) * head_dim)
            upstream = dq_in[:, cols] + dq[a * blk:(a + 1) * blk] * scale
            result, part = norm_grad(raw[:, cols], gain, upstream)
            qgrad_ref[q_first:q_first + blk, cols] = result.astype(qgrad_ref.dtype)
            gain_sum = gain_sum + part
    qgain_ref[...] = gain_sum.reshape(qgain_ref.shape)
    key_raw = kraw_ref[...].astype(jnp.float32)
    key_hat = key_raw * lax.rsqrt(jnp.mean(key_raw * key_raw, axis=1, keepdims=True) + EPS)
    kpart_ref[...] = jnp.sum(dk_ref[...] * key_hat, axis=0, keepdims=True).reshape(kpart_ref.shape)


def kv_final_kernel(dk_ref, dv_ref, back_ref, raw_ref, gain_ref, kgrad_ref, vgrad_ref, kgain_ref, *, head_dim):
    tok_rows = dk_ref.shape[0]
    lead = tok_rows - WINDOW
    back = back_ref[...].astype(jnp.float32)
    dk = dk_ref[...]
    dv = dv_ref[...]
    if lead:
        dk = jnp.concatenate([dk[:lead], dk[lead:] + back[:, :head_dim]], axis=0)
        dv = jnp.concatenate([dv[:lead], dv[lead:] + back[:, head_dim:]], axis=0)
    else:
        dk = dk + back[:, :head_dim]
        dv = dv + back[:, head_dim:]
    vgrad_ref[...] = dv.astype(vgrad_ref.dtype)
    result, part = norm_grad(raw_ref[...].astype(jnp.float32), gain_ref[...], dk)
    kgrad_ref[...] = result.astype(kgrad_ref.dtype)
    kgain_ref[...] = part.reshape(kgain_ref.shape)


def kv_final(dk_own, dv_own, back, key_raw, key_gain, key_heads, head_dim):
    tok_rows = dk_own.shape[0]
    kv_cols = key_heads * head_dim
    col_spec = pl.BlockSpec((tok_rows, head_dim), lambda h: (0, h))
    return pl.pallas_call(
        functools.partial(kv_final_kernel, head_dim=head_dim),
        grid=(key_heads,),
        in_specs=[
            col_spec,
            col_spec,
            pl.BlockSpec((WINDOW, 2 * head_dim), lambda h: (0, h)),
            col_spec,
            pl.BlockSpec((1, head_dim), lambda h: (0, 0)),
        ],
        out_specs=[col_spec, col_spec, pl.BlockSpec((1, 1, head_dim), lambda h: (h, 0, 0))],
        out_shape=[
            jax.ShapeDtypeStruct((tok_rows, kv_cols), jnp.bfloat16),
            jax.ShapeDtypeStruct((tok_rows, kv_cols), jnp.bfloat16),
            jax.ShapeDtypeStruct((key_heads, 1, head_dim), jnp.float32),
        ],
        compiler_params=pltpu.CompilerParams(dimension_semantics=("arbitrary",)),
    )(dk_own, dv_own, back, key_raw, key_gain.reshape(1, head_dim))


def attention_grads(grad_rows, halo_pieces, value_proj, own_doc, all_doc, key_heads,
                    head_dim, query_raw, query_gain, key_raw, key_gain):
    tok_rows, q_cols = query_raw.shape
    key_rows = WINDOW + tok_rows
    group = q_cols // (key_heads * head_dim)
    blk = BLOCK
    n_q = tok_rows // blk
    n_tiles = WINDOW // blk + 1
    gw = group * head_dim
    kv_cols = key_heads * head_dim
    stat_rows = key_heads * n_q * group * blk
    tile_flops = 2 * (group * blk) * blk * head_dim
    halo_tiles = sum(max(0, WINDOW // blk - qb) for qb in range(n_q))
    own_tiles = n_q * n_tiles - halo_tiles
    n_piece = key_heads // len(halo_pieces)
    params = pltpu.CompilerParams(dimension_semantics=("arbitrary",))
    gain_spec = pl.BlockSpec((1, head_dim), lambda h: (0, 0))
    doc_specs = [pl.BlockSpec((tok_rows, 1), lambda h: (0, 0)), pl.BlockSpec((1, key_rows), lambda h: (0, 0))]
    qdoc, kdoc = own_doc.reshape(tok_rows, 1), all_doc.reshape(1, key_rows)
    buffers = ()
    kparts = []
    for piece, halo in enumerate(halo_pieces):
        h0 = piece * n_piece
        qcol = pl.BlockSpec((tok_rows, gw), lambda h, h0=h0: (0, h + h0))
        kcol = pl.BlockSpec((tok_rows, head_dim), lambda h, h0=h0: (0, h + h0))
        hcol = pl.BlockSpec((WINDOW, head_dim), lambda h: (0, h))
        vcol = pl.BlockSpec((WINDOW, head_dim), lambda h, n_piece=n_piece: (0, h + n_piece))
        stat = pl.BlockSpec((n_q * group * blk, 1), lambda h, h0=h0: (h + h0, 0))
        outs = pl.pallas_call(
            functools.partial(halo_kernel, group=group, head_dim=head_dim, n_alias=len(buffers)),
            grid=(n_piece,),
            in_specs=doc_specs + [qcol, qcol, hcol, vcol, kcol, kcol, gain_spec, gain_spec]
            + [pl.BlockSpec(memory_space=pl.ANY)] * len(buffers),
            out_specs=[
                qcol,
                pl.BlockSpec((WINDOW, 2 * head_dim), lambda h, h0=h0: (0, h + h0)),
                stat,
                stat,
                pl.BlockSpec((1, 1, head_dim), lambda h: (h, 0, 0)),
            ],
            out_shape=[
                jax.ShapeDtypeStruct((tok_rows, q_cols), jnp.float32),
                jax.ShapeDtypeStruct((WINDOW, 2 * kv_cols), jnp.bfloat16),
                jax.ShapeDtypeStruct((stat_rows, 1), jnp.float32),
                jax.ShapeDtypeStruct((stat_rows, 1), jnp.float32),
                jax.ShapeDtypeStruct((n_piece, 1, head_dim), jnp.float32),
            ],
            scratch_shapes=[
                pltpu.VMEM((WINDOW, head_dim), jnp.float32),
                pltpu.VMEM((WINDOW, head_dim), jnp.float32),
                pltpu.VMEM((WINDOW, head_dim), jnp.bfloat16),
                pltpu.VMEM((tok_rows, head_dim), jnp.bfloat16),
            ],
            input_output_aliases={10 + i: i for i in range(len(buffers))},
            compiler_params=params,
            cost_estimate=pl.CostEstimate(
                flops=n_piece * (2 * n_q * n_tiles + 5 * halo_tiles) * tile_flops,
                transcendentals=n_piece * (n_q * n_tiles + halo_tiles) * group * blk * blk,
                bytes_accessed=n_piece * (2 * 2 * tok_rows * gw + 2 * 2 * key_rows * head_dim
                                          + 4 * tok_rows * gw + 2 * 2 * WINDOW * head_dim),
            ),
        )(qdoc, kdoc, query_raw, grad_rows, halo, halo, key_raw, value_proj, key_gain.reshape(1, head_dim),
          query_gain.reshape(1, head_dim), *buffers)
        buffers = tuple(outs[:4])
        kparts.append(outs[4])
    dq_half, dkv_halo, log_sums, delta = buffers
    qcol = pl.BlockSpec((tok_rows, gw), lambda h: (0, h))
    kcol = pl.BlockSpec((tok_rows, head_dim), lambda h: (0, h))
    stat = pl.BlockSpec((n_q * group * blk, 1), lambda h: (h, 0))
    part_spec = pl.BlockSpec((1, 1, head_dim), lambda h: (h, 0, 0))
    part_shape = jax.ShapeDtypeStruct((key_heads, 1, head_dim), jnp.float32)
    query_grad, qgain_parts, kown_parts, dk_own, dv_own = pl.pallas_call(
        functools.partial(own_kernel, group=group, head_dim=head_dim),
        grid=(key_heads,),
        in_specs=doc_specs + [qcol, kcol, stat, stat, qcol, qcol, gain_spec, kcol, gain_spec],
        out_specs=[qcol, part_spec, part_spec, kcol, kcol],
        scratch_shapes=[pltpu.VMEM((tok_rows, head_dim), jnp.bfloat16)],
        out_shape=[
            jax.ShapeDtypeStruct((tok_rows, q_cols), jnp.bfloat16),
            part_shape,
            part_shape,
            jax.ShapeDtypeStruct((tok_rows, kv_cols), jnp.float32),
            jax.ShapeDtypeStruct((tok_rows, kv_cols), jnp.float32),
        ],
        compiler_params=params,
        cost_estimate=pl.CostEstimate(
            flops=key_heads * own_tiles * 5 * tile_flops,
            transcendentals=key_heads * own_tiles * group * blk * blk,
            bytes_accessed=2 * 2 * tok_rows * q_cols + 2 * 2 * tok_rows * kv_cols + 2 * 4 * tok_rows * q_cols
            + 2 * 4 * tok_rows * kv_cols,
        ),
    )(qdoc, kdoc, grad_rows, value_proj, log_sums, delta, dq_half, query_raw,
      query_gain.reshape(1, head_dim), key_raw, key_gain.reshape(1, head_dim))
    key_part = jnp.sum(kown_parts, axis=(0, 1))
    for part in kparts:
        key_part = key_part + jnp.sum(part, axis=(0, 1))
    return query_grad, jnp.sum(qgain_parts, axis=(0, 1)), key_part, dkv_halo, dk_own, dv_own


def per_device(query_raw, key_raw, value_proj, query_gain, key_gain, out_grad, doc_lengths):
    tok_rows = query_raw.shape[0]
    head_dim = query_gain.shape[0]
    query_heads = query_raw.shape[1] // head_dim
    key_heads = key_raw.shape[1] // head_dim
    first_pos = lax.axis_index("ctx") * tok_rows
    doc_ends = jnp.cumsum(doc_lengths)
    own_pos = first_pos + jnp.arange(tok_rows, dtype=jnp.int32)
    own_doc = doc_index(own_pos, doc_ends)
    halo_raw = first_pos - WINDOW + jnp.arange(WINDOW, dtype=jnp.int32)
    halo_doc = jnp.where(halo_raw >= 0, doc_index(halo_raw, doc_ends), -1)
    n_pieces = 2 if key_heads % 2 == 0 else 1
    width = key_heads * head_dim // n_pieces
    halo_pieces = []
    for piece in range(n_pieces):
        cols = slice(piece * width, (piece + 1) * width)
        send = jnp.concatenate([key_raw[tok_rows - WINDOW:, cols], value_proj[tok_rows - WINDOW:, cols]], axis=1)
        if halo_pieces:
            send = lax.optimization_barrier((send, halo_pieces[-1]))[0]
        halo_pieces.append(shifted(send, "ctx", 1))
    all_doc = jnp.concatenate([halo_doc, own_doc])
    query_grad, query_part, key_part, dkv_halo, dk_own, dv_own = attention_grads(
        out_grad, halo_pieces, value_proj, own_doc, all_doc, key_heads, head_dim,
        query_raw, query_gain, key_raw, key_gain,
    )
    gain_grads = butterfly_sum(jnp.stack([query_part, key_part]), ("head", "ctx"))
    back = shifted(dkv_halo, "ctx", -1)
    key_grad, value_grad, _ = kv_final(dk_own, dv_own, back, key_raw, key_gain, key_heads, head_dim)
    return (query_grad, key_grad, value_grad, gain_grads[0], gain_grads[1])


def solution(mesh):
    return jax.shard_map(
        per_device,
        mesh=mesh,
        in_specs=(
            P("ctx", "head"),
            P("ctx", "head"),
            P("ctx", "head"),
            P(),
            P(),
            P("ctx", "head"),
            P(),
        ),
        out_specs=(P("ctx", "head"), P("ctx", "head"), P("ctx", "head"), P(), P()),
        check_vma=False,
    )
```

```python
import functools
import math

import jax
import jax.numpy as jnp
from jax import lax
from jax.experimental import pallas as pl
from jax.experimental.pallas import tpu as pltpu
from jax.sharding import PartitionSpec as P

WINDOW = 1024
QUERY_SCALAR = 168


EPS = 1e-06
BLOCK = 256


def shifted(value, axis, steps):
    count = lax.axis_size(axis)
    leading, last = (max(0, -steps), min(count, count - steps))
    return lax.ppermute(value, axis, [(source, source + steps) for source in range(leading, last)])


def xor_tree(values):
    while len(values) > 1:
        values = [values[i] + values[i + 1] for i in range(0, len(values), 2)]
    return values[0]


def butterfly_sum(value, axes):
    for axis in axes:
        count = lax.axis_size(axis)
        if count & (count - 1):
            value = lax.psum(value, axis)
            continue
        bits = count.bit_length() - 1
        low = 0
        while low < bits:
            width = 1
            shifted_parts = [value]
            for mask in range(1, 1 << width):
                pairs = [(source, source ^ (mask << low)) for source in range(count)]
                shifted_parts.append(lax.ppermute(value, axis, pairs))
            value = xor_tree(shifted_parts)
            low += width
    return value


def norm_rows(raw_rows, head_count):
    values = raw_rows.astype(jnp.float32).reshape(raw_rows.shape[0], head_count, -1)
    inverse = lax.rsqrt(jnp.mean(values * values, axis=-1, keepdims=True) + EPS)
    return (values * inverse, inverse)


def norm_back(raw_rows, gain_vec, head_count, upstream):
    scaled, inverse = norm_rows(raw_rows, head_count)
    incoming = upstream.reshape(scaled.shape)
    weighted = incoming * gain_vec
    inner_sum = jnp.mean(weighted * scaled, axis=-1, keepdims=True)
    result = inverse * (weighted - scaled * inner_sum)
    return (result.reshape(raw_rows.shape), jnp.sum(incoming * scaled, axis=(0, 1)))


def doc_index(positions, doc_ends):
    return jnp.sum((positions[:, None] >= doc_ends[None, :]).astype(jnp.int32), axis=1)


def tile_mask(qdoc_ref, kdoc_ref, q_first, t, group):
    blk = BLOCK
    n_tiles = WINDOW // blk + 1
    rows = lax.broadcasted_iota(jnp.int32, (blk, blk), 0)
    cols = lax.broadcasted_iota(jnp.int32, (blk, blk), 1)
    k_first = q_first + t * blk
    live = qdoc_ref[q_first:q_first + blk, :] == kdoc_ref[:, k_first:k_first + blk]
    if t == 0:
        live = live & (cols > rows)
    if t == n_tiles - 1:
        live = live & (cols + t * blk <= rows + WINDOW)
    return jnp.concatenate([live] * group, axis=0), k_first


def normed_rows(raw, gain):
    inverse = lax.rsqrt(jnp.mean(raw * raw, axis=1, keepdims=True) + EPS)
    return (raw * inverse * gain).astype(jnp.bfloat16)


def normed_stack(ref, gain, group, head_dim, first):
    blk = BLOCK
    return jnp.concatenate(
        [normed_rows(ref[first:first + blk, a * head_dim:(a + 1) * head_dim].astype(jnp.float32), gain)
         for a in range(group)],
        axis=0,
    )


def stacked(ref, group, head_dim, first):
    blk = BLOCK
    return jnp.concatenate(
        [ref[first:first + blk, a * head_dim:(a + 1) * head_dim] for a in range(group)], axis=0
    )


def grad_tile(q_g, do_g, k_tile, v_tile, live, log_sums, delta):
    scale = QUERY_SCALAR ** (-0.5)
    scores = lax.dot_general(q_g, k_tile, (((1,), (1,)), ((), ())), preferred_element_type=jnp.float32) * scale
    weights = jnp.where(live, jnp.exp(scores - log_sums), 0.0)
    d_weights = lax.dot_general(do_g, v_tile, (((1,), (1,)), ((), ())), preferred_element_type=jnp.float32)
    d_scores = (weights * (d_weights - delta)).astype(jnp.bfloat16)
    dq_part = jnp.dot(d_scores, k_tile, preferred_element_type=jnp.float32)
    dk_part = lax.dot_general(d_scores, q_g, (((0,), (0,)), ((), ())), preferred_element_type=jnp.float32)
    dv_part = lax.dot_general(
        weights.astype(jnp.bfloat16), do_g, (((0,), (0,)), ((), ())), preferred_element_type=jnp.float32
    )
    return dq_part, dk_part * scale, dv_part


def halo_kernel(qdoc_ref, kdoc_ref, q_ref, do_ref, hk_ref, hv_ref, kraw_ref, v_ref, kgain_ref, qgain_ref, *refs,
                group, head_dim, n_alias):
    dq_ref, dkv_ref, lse_ref, delta_ref, kpart_ref, dk_ref, dv_ref, kn_ref, k_ref = refs[n_alias:]
    blk = BLOCK
    n_tiles = WINDOW // blk + 1
    n_halo = WINDOW // blk
    n_q = q_ref.shape[0] // blk
    gb = group * blk
    scale = QUERY_SCALAR ** (-0.5)
    dk_ref[...] = jnp.zeros(dk_ref.shape, jnp.float32)
    dv_ref[...] = jnp.zeros(dv_ref.shape, jnp.float32)
    halo_raw = hk_ref[...].astype(jnp.float32)
    halo_inv = lax.rsqrt(jnp.mean(halo_raw * halo_raw, axis=1, keepdims=True) + EPS)
    kn_ref[...] = (halo_raw * halo_inv * kgain_ref[...]).astype(jnp.bfloat16)
    k_ref[...] = normed_rows(kraw_ref[...].astype(jnp.float32), kgain_ref[...])
    qgain = qgain_ref[...]

    def key_tile(k_first):
        if k_first < WINDOW:
            return kn_ref[k_first:k_first + blk, :], hv_ref[k_first:k_first + blk, :]
        own_first = k_first - WINDOW
        return k_ref[own_first:own_first + blk, :], v_ref[own_first:own_first + blk, :]

    for qb in range(n_q):
        q_first = qb * blk
        q_g = normed_stack(q_ref, qgain, group, head_dim, q_first)
        do_g = stacked(do_ref, group, head_dim, q_first)
        totals = jnp.zeros((gb, 1), jnp.float32)
        numer = jnp.zeros((gb, head_dim), jnp.float32)
        for t in range(n_tiles):
            k_first = q_first + t * blk
            k_tile, v_tile = key_tile(k_first)
            scores = lax.dot_general(
                q_g, k_tile, (((1,), (1,)), ((), ())), preferred_element_type=jnp.float32
            ) * scale
            exp_s = jnp.where(tile_mask(qdoc_ref, kdoc_ref, q_first, t, group)[0], jnp.exp(scores), 0.0)
            totals = totals + jnp.sum(exp_s, axis=1, keepdims=True)
            numer = numer + jnp.dot(exp_s.astype(jnp.bfloat16), v_tile, preferred_element_type=jnp.float32)
        log_sums = jnp.log(totals)
        attn_out = numer / totals
        delta = jnp.sum(do_g.astype(jnp.float32) * attn_out, axis=1, keepdims=True)
        lse_ref[qb * gb:(qb + 1) * gb, :] = log_sums
        delta_ref[qb * gb:(qb + 1) * gb, :] = delta
        dq = jnp.zeros((gb, head_dim), jnp.float32)
        for t in range(n_halo - qb):
            k_first = q_first + t * blk
            k_tile, v_tile = key_tile(k_first)
            live = tile_mask(qdoc_ref, kdoc_ref, q_first, t, group)[0]
            dq_part, dk_part, dv_part = grad_tile(q_g, do_g, k_tile, v_tile, live, log_sums, delta)
            dq = dq + dq_part
            dk_ref[k_first:k_first + blk, :] += dk_part
            dv_ref[k_first:k_first + blk, :] += dv_part
        dq_ref[q_first:q_first + blk, :] = jnp.concatenate(
            [dq[a * blk:(a + 1) * blk] for a in range(group)], axis=1
        ) * scale
    dkv_ref[:, :head_dim] = dk_ref[...].astype(jnp.bfloat16)
    dkv_ref[:, head_dim:] = dv_ref[...].astype(jnp.bfloat16)
    halo_hat = halo_raw * halo_inv
    kpart_ref[...] = jnp.sum(dk_ref[...] * halo_hat, axis=0, keepdims=True).reshape(kpart_ref.shape)


def norm_grad(raw, gain, upstream):
    inverse = lax.rsqrt(jnp.mean(raw * raw, axis=1, keepdims=True) + EPS)
    scaled = raw * inverse
    weighted = upstream * gain
    inner_sum = jnp.mean(weighted * scaled, axis=1, keepdims=True)
    result = inverse * (weighted - scaled * inner_sum)
    return result, jnp.sum(upstream * scaled, axis=0, keepdims=True)


def own_kernel(qdoc_ref, kdoc_ref, do_ref, v_ref, lse_ref, delta_ref, dq_in_ref, raw_ref, gain_ref,
               kraw_ref, kgain_ref, qgrad_ref, qgain_ref, kpart_ref, dk_ref, dv_ref, k_ref, *, group, head_dim):
    q_ref = raw_ref
    blk = BLOCK
    n_tiles = WINDOW // blk + 1
    n_halo = WINDOW // blk
    n_q = q_ref.shape[0] // blk
    gb = group * blk
    scale = QUERY_SCALAR ** (-0.5)
    dk_ref[...] = jnp.zeros(dk_ref.shape, jnp.float32)
    dv_ref[...] = jnp.zeros(dv_ref.shape, jnp.float32)
    gain = gain_ref[...]
    k_ref[...] = normed_rows(kraw_ref[...].astype(jnp.float32), kgain_ref[...])
    gain_sum = jnp.zeros((1, head_dim), jnp.float32)
    for qb in range(n_q):
        q_first = qb * blk
        q_g = normed_stack(q_ref, gain, group, head_dim, q_first)
        do_g = stacked(do_ref, group, head_dim, q_first)
        log_sums = lse_ref[qb * gb:(qb + 1) * gb, :]
        delta = delta_ref[qb * gb:(qb + 1) * gb, :]
        dq = jnp.zeros((gb, head_dim), jnp.float32)
        for t in range(max(0, n_halo - qb), n_tiles):
            live, _ = tile_mask(qdoc_ref, kdoc_ref, q_first, t, group)
            k_first = q_first + t * blk
            own_first = k_first - WINDOW
            k_tile = k_ref[own_first:own_first + blk, :]
            v_tile = v_ref[own_first:own_first + blk, :]
            dq_part, dk_part, dv_part = grad_tile(q_g, do_g, k_tile, v_tile, live, log_sums, delta)
            dq = dq + dq_part
            dk_ref[own_first:own_first + blk, :] += dk_part
            dv_ref[own_first:own_first + blk, :] += dv_part
        dq_in = dq_in_ref[q_first:q_first + blk, :]
        raw = raw_ref[q_first:q_first + blk, :].astype(jnp.float32)
        for a in range(group):
            cols = slice(a * head_dim, (a + 1) * head_dim)
            upstream = dq_in[:, cols] + dq[a * blk:(a + 1) * blk] * scale
            result, part = norm_grad(raw[:, cols], gain, upstream)
            qgrad_ref[q_first:q_first + blk, cols] = result.astype(qgrad_ref.dtype)
            gain_sum = gain_sum + part
    qgain_ref[...] = gain_sum.reshape(qgain_ref.shape)
    key_raw = kraw_ref[...].astype(jnp.float32)
    key_hat = key_raw * lax.rsqrt(jnp.mean(key_raw * key_raw, axis=1, keepdims=True) + EPS)
    kpart_ref[...] = jnp.sum(dk_ref[...] * key_hat, axis=0, keepdims=True).reshape(kpart_ref.shape)


def kv_final_kernel(dk_ref, dv_ref, back_ref, raw_ref, gain_ref, kgrad_ref, vgrad_ref, kgain_ref, *, head_dim):
    tok_rows = dk_ref.shape[0]
    lead = tok_rows - WINDOW
    back = back_ref[...].astype(jnp.float32)
    dk = dk_ref[...]
    dv = dv_ref[...]
    if lead:
        dk = jnp.concatenate([dk[:lead], dk[lead:] + back[:, :head_dim]], axis=0)
        dv = jnp.concatenate([dv[:lead], dv[lead:] + back[:, head_dim:]], axis=0)
    else:
        dk = dk + back[:, :head_dim]
        dv = dv + back[:, head_dim:]
    vgrad_ref[...] = dv.astype(vgrad_ref.dtype)
    raw = raw_ref[...].astype(jnp.float32)
    inverse = lax.rsqrt(jnp.mean(raw * raw, axis=1, keepdims=True) + EPS)
    scaled = raw * inverse
    weighted = dk * gain_ref[...]
    inner_sum = jnp.mean(weighted * scaled, axis=1, keepdims=True)
    kgrad_ref[...] = (inverse * (weighted - scaled * inner_sum)).astype(kgrad_ref.dtype)
    kgain_ref[...] = jnp.zeros(kgain_ref.shape, jnp.float32).reshape(kgain_ref.shape)


def kv_final(dk_own, dv_own, back, key_raw, key_gain, key_heads, head_dim):
    tok_rows = dk_own.shape[0]
    kv_cols = key_heads * head_dim
    col_spec = pl.BlockSpec((tok_rows, head_dim), lambda h: (0, h))
    return pl.pallas_call(
        functools.partial(kv_final_kernel, head_dim=head_dim),
        grid=(key_heads,),
        in_specs=[
            col_spec,
            col_spec,
            pl.BlockSpec((WINDOW, 2 * head_dim), lambda h: (0, h)),
            col_spec,
            pl.BlockSpec((1, head_dim), lambda h: (0, 0)),
        ],
        out_specs=[col_spec, col_spec, pl.BlockSpec((1, 1, head_dim), lambda h: (h, 0, 0))],
        out_shape=[
            jax.ShapeDtypeStruct((tok_rows, kv_cols), jnp.bfloat16),
            jax.ShapeDtypeStruct((tok_rows, kv_cols), jnp.bfloat16),
            jax.ShapeDtypeStruct((key_heads, 1, head_dim), jnp.float32),
        ],
        compiler_params=pltpu.CompilerParams(dimension_semantics=("arbitrary",)),
    )(dk_own, dv_own, back, key_raw, key_gain.reshape(1, head_dim))


def attention_grads(grad_rows, halo_pieces, value_proj, own_doc, all_doc, key_heads,
                    head_dim, query_raw, query_gain, key_raw, key_gain):
    tok_rows, q_cols = query_raw.shape
    key_rows = WINDOW + tok_rows
    group = q_cols // (key_heads * head_dim)
    blk = BLOCK
    n_q = tok_rows // blk
    n_tiles = WINDOW // blk + 1
    gw = group * head_dim
    kv_cols = key_heads * head_dim
    stat_rows = key_heads * n_q * group * blk
    tile_flops = 2 * (group * blk) * blk * head_dim
    halo_tiles = sum(max(0, WINDOW // blk - qb) for qb in range(n_q))
    own_tiles = n_q * n_tiles - halo_tiles
    n_piece = key_heads // len(halo_pieces)
    params = pltpu.CompilerParams(dimension_semantics=("arbitrary",))
    gain_spec = pl.BlockSpec((1, head_dim), lambda h: (0, 0))
    doc_specs = [pl.BlockSpec((tok_rows, 1), lambda h: (0, 0)), pl.BlockSpec((1, key_rows), lambda h: (0, 0))]
    qdoc, kdoc = own_doc.reshape(tok_rows, 1), all_doc.reshape(1, key_rows)
    buffers = ()
    kparts = []
    for piece, halo in enumerate(halo_pieces):
        h0 = piece * n_piece
        qcol = pl.BlockSpec((tok_rows, gw), lambda h, h0=h0: (0, h + h0))
        kcol = pl.BlockSpec((tok_rows, head_dim), lambda h, h0=h0: (0, h + h0))
        hcol = pl.BlockSpec((WINDOW, head_dim), lambda h: (0, h))
        vcol = pl.BlockSpec((WINDOW, head_dim), lambda h, n_piece=n_piece: (0, h + n_piece))
        stat = pl.BlockSpec((n_q * group * blk, 1), lambda h, h0=h0: (h + h0, 0))
        outs = pl.pallas_call(
            functools.partial(halo_kernel, group=group, head_dim=head_dim, n_alias=len(buffers)),
            grid=(n_piece,),
            in_specs=doc_specs + [qcol, qcol, hcol, vcol, kcol, kcol, gain_spec, gain_spec]
            + [pl.BlockSpec(memory_space=pl.ANY)] * len(buffers),
            out_specs=[
                qcol,
                pl.BlockSpec((WINDOW, 2 * head_dim), lambda h, h0=h0: (0, h + h0)),
                stat,
                stat,
                pl.BlockSpec((1, 1, head_dim), lambda h: (h, 0, 0)),
            ],
            out_shape=[
                jax.ShapeDtypeStruct((tok_rows, q_cols), jnp.float32),
                jax.ShapeDtypeStruct((WINDOW, 2 * kv_cols), jnp.bfloat16),
                jax.ShapeDtypeStruct((stat_rows, 1), jnp.float32),
                jax.ShapeDtypeStruct((stat_rows, 1), jnp.float32),
                jax.ShapeDtypeStruct((n_piece, 1, head_dim), jnp.float32),
            ],
            scratch_shapes=[
                pltpu.VMEM((WINDOW, head_dim), jnp.float32),
                pltpu.VMEM((WINDOW, head_dim), jnp.float32),
                pltpu.VMEM((WINDOW, head_dim), jnp.bfloat16),
                pltpu.VMEM((tok_rows, head_dim), jnp.bfloat16),
            ],
            input_output_aliases={10 + i: i for i in range(len(buffers))},
            compiler_params=params,
            cost_estimate=pl.CostEstimate(
                flops=n_piece * (2 * n_q * n_tiles + 5 * halo_tiles) * tile_flops,
                transcendentals=n_piece * (n_q * n_tiles + halo_tiles) * group * blk * blk,
                bytes_accessed=n_piece * (2 * 2 * tok_rows * gw + 2 * 2 * key_rows * head_dim
                                          + 4 * tok_rows * gw + 2 * 2 * WINDOW * head_dim),
            ),
        )(qdoc, kdoc, query_raw, grad_rows, halo, halo, key_raw, value_proj, key_gain.reshape(1, head_dim),
          query_gain.reshape(1, head_dim), *buffers)
        buffers = tuple(outs[:4])
        kparts.append(outs[4])
    dq_half, dkv_halo, log_sums, delta = buffers
    qcol = pl.BlockSpec((tok_rows, gw), lambda h: (0, h))
    kcol = pl.BlockSpec((tok_rows, head_dim), lambda h: (0, h))
    stat = pl.BlockSpec((n_q * group * blk, 1), lambda h: (h, 0))
    part_spec = pl.BlockSpec((1, 1, head_dim), lambda h: (h, 0, 0))
    part_shape = jax.ShapeDtypeStruct((key_heads, 1, head_dim), jnp.float32)
    query_grad, qgain_parts, kown_parts, dk_own, dv_own = pl.pallas_call(
        functools.partial(own_kernel, group=group, head_dim=head_dim),
        grid=(key_heads,),
        in_specs=doc_specs + [qcol, kcol, stat, stat, qcol, qcol, gain_spec, kcol, gain_spec],
        out_specs=[qcol, part_spec, part_spec, kcol, kcol],
        scratch_shapes=[pltpu.VMEM((tok_rows, head_dim), jnp.bfloat16)],
        out_shape=[
            jax.ShapeDtypeStruct((tok_rows, q_cols), jnp.bfloat16),
            part_shape,
            part_shape,
            jax.ShapeDtypeStruct((tok_rows, kv_cols), jnp.float32),
            jax.ShapeDtypeStruct((tok_rows, kv_cols), jnp.float32),
        ],
        compiler_params=params,
        cost_estimate=pl.CostEstimate(
            flops=key_heads * own_tiles * 5 * tile_flops,
            transcendentals=key_heads * own_tiles * group * blk * blk,
            bytes_accessed=2 * 2 * tok_rows * q_cols + 2 * 2 * tok_rows * kv_cols + 2 * 4 * tok_rows * q_cols
            + 2 * 4 * tok_rows * kv_cols,
        ),
    )(qdoc, kdoc, grad_rows, value_proj, log_sums, delta, dq_half, query_raw,
      query_gain.reshape(1, head_dim), key_raw, key_gain.reshape(1, head_dim))
    key_part = jnp.sum(kown_parts, axis=(0, 1))
    for part in kparts:
        key_part = key_part + jnp.sum(part, axis=(0, 1))
    return query_grad, jnp.sum(qgain_parts, axis=(0, 1)), key_part, dkv_halo, dk_own, dv_own


def per_device(query_raw, key_raw, value_proj, query_gain, key_gain, out_grad, doc_lengths):
    tok_rows = query_raw.shape[0]
    head_dim = query_gain.shape[0]
    query_heads = query_raw.shape[1] // head_dim
    key_heads = key_raw.shape[1] // head_dim
    first_pos = lax.axis_index("ctx") * tok_rows
    doc_ends = jnp.cumsum(doc_lengths)
    own_pos = first_pos + jnp.arange(tok_rows, dtype=jnp.int32)
    own_doc = doc_index(own_pos, doc_ends)
    halo_raw = first_pos - WINDOW + jnp.arange(WINDOW, dtype=jnp.int32)
    halo_doc = jnp.where(halo_raw >= 0, doc_index(halo_raw, doc_ends), -1)
    n_pieces = 2 if key_heads % 2 == 0 else 1
    width = key_heads * head_dim // n_pieces
    halo_pieces = []
    for piece in range(n_pieces):
        cols = slice(piece * width, (piece + 1) * width)
        send = jnp.concatenate([key_raw[tok_rows - WINDOW:, cols], value_proj[tok_rows - WINDOW:, cols]], axis=1)
        if halo_pieces:
            send = lax.optimization_barrier((send, halo_pieces[-1]))[0]
        halo_pieces.append(shifted(send, "ctx", 1))
    all_doc = jnp.concatenate([halo_doc, own_doc])
    query_grad, query_part, key_part, dkv_halo, dk_own, dv_own = attention_grads(
        out_grad, halo_pieces, value_proj, own_doc, all_doc, key_heads, head_dim,
        query_raw, query_gain, key_raw, key_gain,
    )
    gain_grads = butterfly_sum(jnp.stack([query_part, key_part]), ("head", "ctx"))
    back = shifted(dkv_halo, "ctx", -1)
    key_grad, value_grad, _ = kv_final(dk_own, dv_own, back, key_raw, key_gain, key_heads, head_dim)
    return (query_grad, key_grad, value_grad, gain_grads[0], gain_grads[1])


def solution(mesh):
    return jax.shard_map(
        per_device,
        mesh=mesh,
        in_specs=(
            P("ctx", "head"),
            P("ctx", "head"),
            P("ctx", "head"),
            P(),
            P(),
            P("ctx", "head"),
            P(),
        ),
        out_specs=(P("ctx", "head"), P("ctx", "head"), P("ctx", "head"), P(), P()),
        check_vma=False,
    )
```
